32 devices in a mesh: gz: 8 (over y, x, core), sa: 4 (over z).
Axes of the slice: x: 2, y: 2, z: 4, core: 2. Of those that a mesh axis runs over, the one named last changes fastest.
Arguments:
- volume: bfloat16 [4, 4, 32, 16, 512], P('sa', None, 'gz'), may hold values from -6 to 6
- kernel_one: bfloat16 [32, 4, 3, 3, 3], replicated, may hold values from -0.625 to 0.625
- kernel_two: bfloat16 [64, 32, 3, 3, 3], replicated, may hold values from -0.21875 to 0.21875
- cotangent: bfloat16 [4, 64, 8, 4, 128], P('sa', None, 'gz'), may hold values from -6 to 6
Outputs:
- level_two: bfloat16 [4, 64, 8, 4, 128], P('sa', None, 'gz')
- grad_level_one: bfloat16 [4, 32, 16, 8, 256], P('sa', None, 'gz')
- grad_kernel_one: float32 [32, 4, 3, 3, 3], replicated
- grad_kernel_two: float32 [64, 32, 3, 3, 3], replicated
The draws below stay inside these ranges and needn't reach their ends.
All inputs are finite; a program needn't handle non-finite values.
Results may differ from the reference program's by a relative error of at most 0.0057.
Values may be sent and summed in bfloat16 or wider, within the bound.
No kernel may reach another device: no remote copies, remote signals or barrier semaphores. Data moves between devices by JAX's collectives and lax.ppermute only.
A program may use at most 128 MiB of HBM per device.

```python
import math
import jax
import jax.numpy as jnp
from jax import lax

C0 = 4
C1 = 32
C2 = 64
NY = 16
NX = 512
SAMPLES = 4
NZ = 32


def block_levels(rng, extent, cuts, least, largest):
    def one(position, blocks):
        draws = jax.random.uniform(jax.random.fold_in(jax.random.fold_in(rng, 6), position), (blocks,), jnp.float32, least / len(cuts), largest / len(cuts))
        return jnp.repeat(jnp.exp(draws), extent[position] // blocks).reshape((-1,) + (1,) * (len(extent) - position - 1))

    loudness = one(*cuts[0])
    for cut in cuts[1:]:
        loudness = loudness * one(*cut)
    return loudness


def normal_values(key, shape, deviation, reach, split=(), kind=jnp.bfloat16):
    drawn = jax.random.normal(key, shape, jnp.float32) * deviation
    if len(split) > 0:
        drawn = block_levels(key, shape, split, -0.22, 0.18) * drawn
    return jnp.clip(drawn, min=-reach, max=reach).astype(kind)


def setup_inputs(seed: int = 0) -> dict:
    arg_keys = jax.random.split(jax.random.key(seed), 5)
    return {
        "volume": normal_values(arg_keys[0], (SAMPLES, C0, NZ, NY, NX), 1.0, 6.0, ((0, 4), (2, 8))),
        "kernel_one": normal_values(arg_keys[1], (C1, C0, 3, 3, 3), (C0 * 27) ** -0.5, 0.625),
        "kernel_two": normal_values(arg_keys[2], (C2, C1, 3, 3, 3), (C1 * 27) ** -0.5, 0.21875),
        "cotangent": normal_values(arg_keys[3], (SAMPLES, C2, NZ // 4, NY // 4, NX // 4), 1.0, 6.0, ((0, 4), (2, 8))),
    }


def forward_conv(data, kernel):
    return lax.conv_general_dilated(data, kernel, (2, 2, 2), ((1, 1), (1, 1), (1, 1)), dimension_numbers=('NCDHW', 'OIDHW', 'NCDHW'), preferred_element_type=jnp.float32)

def silu_slope(value):
    sig = jax.nn.sigmoid(value)
    return sig * (1.0 + value * (1.0 - sig))

def weight_taps(grad, padded):
    depth, rows, cols = (grad.shape[2], grad.shape[3], grad.shape[4])
    cropped = padded[:, :, :2 * depth + 1, :2 * rows + 1, :2 * cols + 1]
    return lax.conv_general_dilated(cropped, grad, (1, 1, 1), ((0, 0), (0, 0), (0, 0)), rhs_dilation=(2, 2, 2), dimension_numbers=('CNDHW', 'IODHW', 'CNDHW'), preferred_element_type=jnp.float32)

def input_taps(grad, kernel):
    depth_k = kernel.shape[2]
    flipped = jnp.flip(kernel, (2, 3, 4))
    return lax.conv_general_dilated(grad, flipped, (1, 1, 1), ((depth_k - 1, depth_k - 1), (2, 2), (2, 2)), lhs_dilation=(2, 2, 2), dimension_numbers=('NCDHW', 'IODHW', 'NCDHW'), preferred_element_type=jnp.float32)

def reference(volume, kernel_one, kernel_two, cotangent):
    pad_all = ((0, 0), (0, 0), (1, 1), (1, 1), (1, 1))

    def one_sample(pair):
        sample = pair[0][None]
        cot = pair[1][None]
        pre_one = forward_conv(sample, kernel_one)
        act_one = jax.nn.silu(pre_one).astype(jnp.bfloat16)
        pre_two = forward_conv(act_one, kernel_two)
        level_two = jax.nn.silu(pre_two).astype(jnp.bfloat16)
        back_two = (cot.astype(jnp.float32) * silu_slope(pre_two)).astype(jnp.bfloat16)
        act_padded = jnp.pad(act_one, pad_all)
        sum_two = weight_taps(back_two, act_padded)
        full = input_taps(back_two, kernel_two)
        grad_one = full[:, :, 1:1 + act_one.shape[2], 1:1 + act_one.shape[3], 1:1 + act_one.shape[4]]
        back_one = (grad_one * silu_slope(pre_one)).astype(jnp.bfloat16)
        sum_one = weight_taps(back_one, jnp.pad(sample, pad_all))
        return (level_two[0], grad_one.astype(jnp.bfloat16)[0], sum_one, sum_two)
    level_two, grad_level_one, sums_one, sums_two = lax.map(one_sample, (volume, cotangent))
    cells_one = SAMPLES * (NZ // 2) * (NY // 2) * (NX // 2)
    cells_two = SAMPLES * (NZ // 4) * (NY // 4) * (NX // 4)
    grad_kernel_one = lax.optimization_barrier(jnp.sum(sums_one, 0)) / math.sqrt(float(cells_one))
    grad_kernel_two = lax.optimization_barrier(jnp.sum(sums_two, 0)) / math.sqrt(float(cells_two))
    return (level_two, grad_level_one, grad_kernel_one, grad_kernel_two)
```

```python
import math

import jax
import jax.numpy as jnp
from jax import lax
from jax.experimental import pallas as pl
from jax.experimental.pallas import tpu as pltpu
from jax.sharding import PartitionSpec as P

F32 = jnp.float32
BF16 = jnp.bfloat16


def shifted(block, axis, distance):
    devices = range(lax.axis_size(axis))
    route = [(i - distance, i) for i in devices if i - distance in devices]
    return lax.ppermute(block, axis, route)


def _sigmoid(v):
    return 1.0 / (1.0 + jnp.exp(-v))


def _shift_right(x):
    lane = lax.broadcasted_iota(jnp.int32, x.shape, x.ndim - 1)
    return jnp.where(lane == 0, 0.0, pltpu.roll(x, 1, x.ndim - 1))


def _shift_left(x):
    n = x.shape[-1]
    lane = lax.broadcasted_iota(jnp.int32, x.shape, x.ndim - 1)
    return jnp.where(lane == n - 1, 0.0, pltpu.roll(x, n - 1, x.ndim - 1))


def _nt(a, b):
    return lax.dot_general(a, b, (((1,), (1,)), ((), ())), preferred_element_type=F32)


def _kernel(vz_ref, k1_ref, k2_ref, k2t_ref, cot_ref,
            lvl_ref, g1_ref, s1_ref, s2_ref,
            tp, p1, t2, pre1, p2, bt, gs, gacc, b1, g1s):
    nzi, ny, rows0, lanes = vz_ref.shape
    n_act = p1.shape[0]
    ny1 = ny // 2
    ny2 = ny1 // 2
    c2 = t2.shape[2]
    c1 = c2 // 2

    tp[:, 0] = jnp.zeros((nzi, 2 * rows0, lanes), BF16)
    for zi in range(nzi):
        x = vz_ref[zi].astype(F32)
        tp[zi, 1:] = jnp.concatenate([x, _shift_right(x)], axis=1).astype(BF16)

    for a in range(n_act):
        for d in range(3):
            for y1 in range(ny1):
                p1[a, d * 3 * 2 * rows0:(d + 1) * 3 * 2 * rows0, y1 * lanes:(y1 + 1) * lanes] = (
                    tp[2 * a + d, 2 * y1:2 * y1 + 3].reshape(3 * 2 * rows0, lanes))

    k1 = k1_ref[...]
    t2[:, 0] = jnp.zeros((n_act, c2, lanes), BF16)
    for a in range(n_act):
        pre = jnp.dot(k1, p1[a], preferred_element_type=F32)
        if a in (1, 2):
            pre1[a - 1] = pre
        act = pre * _sigmoid(pre)
        for y1 in range(ny1):
            blk = act[:, y1 * lanes:(y1 + 1) * lanes]
            t2[a, y1 + 1] = jnp.concatenate([blk, _shift_right(blk)], axis=0).astype(BF16)

    for tt in range(2):
        for d in range(3):
            for y2 in range(ny2):
                p2[tt, d * 3 * c2:(d + 1) * 3 * c2, y2 * lanes:(y2 + 1) * lanes] = (
                    t2[2 * tt + d, 2 * y2:2 * y2 + 3].reshape(3 * c2, lanes))

    k2 = k2_ref[...]
    for tt in range(2):
        pre = jnp.dot(k2, p2[tt], preferred_element_type=F32)
        sig = _sigmoid(pre)
        if tt == 0:
            lvl_ref[...] = (pre * sig).astype(BF16)
        slope = sig * (1.0 + pre * (1.0 - sig))
        bt[tt] = (cot_ref[tt].astype(F32) * slope).astype(BF16)

    s2_ref[...] = _nt(bt[0], p2[0])

    gacc[...] = jnp.zeros(gacc.shape, F32)
    k2t = k2t_ref[...]
    for tt in range(2):
        if tt == 0:
            gs[...] = jnp.dot(k2t, bt[0], preferred_element_type=F32)
            taps_d = (1, 2)
        else:
            gs[0:3 * c2] = jnp.dot(k2t[0:3 * c2], bt[1], preferred_element_type=F32)
            taps_d = (0,)
        for d in taps_d:
            a = 2 * tt + d
            for h in range(3):
                for y2 in range(ny2):
                    y1 = 2 * y2 + h - 1
                    if y1 < 0:
                        continue
                    r0 = (d * 3 + h) * c2
                    blk = gs[r0:r0 + c2, y2 * lanes:(y2 + 1) * lanes]
                    gacc[a - 1, :, y1 * lanes:(y1 + 1) * lanes] += blk[:c1] + _shift_left(blk[c1:])

    half = c1 // 2
    for a_ in range(2):
        g = gacc[a_]
        pre = pre1[a_]
        sig = _sigmoid(pre)
        slope = sig * (1.0 + pre * (1.0 - sig))
        b1[a_] = (g * slope).astype(BF16)
        gb = g.astype(BF16)
        for y1 in range(ny1):
            blk = gb[:, y1 * lanes:(y1 + 1) * lanes]
            r0 = (a_ * ny1 + y1) * half
            g1s[r0:r0 + half] = jnp.concatenate([blk[:half], blk[half:]], axis=1)
    s1_ref[...] = _nt(b1[0], p1[1]) + _nt(b1[1], p1[2])

    n2 = 2 * lanes
    row = lax.broadcasted_iota(jnp.int32, (n2, n2), 0)
    col = lax.broadcasted_iota(jnp.int32, (n2, n2), 1)
    inter = jnp.where(col == 2 * (row % lanes) + row // lanes, 1.0, 0.0).astype(BF16)
    g1_ref[...] = jnp.dot(g1s[...], inter, preferred_element_type=F32).astype(BF16)


def _level_one_weights(k1):
    kt = jnp.transpose(k1, (0, 2, 3, 1, 4))
    w0, w1, w2 = kt[..., 0], kt[..., 1], kt[..., 2]
    z = jnp.zeros_like(w0)
    p0 = jnp.stack([jnp.stack([w1, w2, z, z], -1), jnp.stack([z, z, z, w0], -1)], 3)
    p1 = jnp.stack([jnp.stack([z, w0, w1, w2], -1), jnp.stack([z, z, z, z], -1)], 3)
    e = jnp.stack([p0, p1], 0)
    return e.reshape(2 * k1.shape[0], -1)


def _level_two_weights(k2):
    kt = jnp.transpose(k2, (0, 2, 3, 4, 1))
    w0, w1, w2 = kt[:, :, :, 0], kt[:, :, :, 1], kt[:, :, :, 2]
    z = jnp.zeros_like(w0)
    e = jnp.stack([jnp.stack([w1, w2], 3), jnp.stack([z, w0], 3)], 3)
    return e.reshape(k2.shape[0], -1)


def per_device(volume, kernel_one, kernel_two, cotangent):
    _, c0, nz, ny, nx = volume.shape
    c1 = kernel_one.shape[0]
    c2 = kernel_two.shape[0]
    assert nz == 4 and cotangent.shape[2] == 1
    q = nx // 4
    below = shifted(volume[:, :, 1:], "gz", 1)
    above = shifted(volume, "gz", -1)
    cot_above = shifted(cotangent, "gz", -1)
    ext = jnp.concatenate([below, volume, above], 2)[0]
    nzi = ext.shape[1]
    vz = ext.reshape(c0, nzi, ny, q, 4).transpose(1, 2, 0, 4, 3).reshape(nzi, ny, 4 * c0, q)
    n2 = cotangent.shape[3] * cotangent.shape[4]
    cots = jnp.concatenate([cotangent, cot_above], 2)[0].transpose(1, 0, 2, 3).reshape(2, c2, n2)

    k1m = _level_one_weights(kernel_one)
    k2m = _level_two_weights(kernel_two)
    k2t = k2m.T

    ny1, ny2 = ny // 2, ny // 4
    n_act = 5
    vm = pltpu.VMEM
    lvl, g1, s1, s2 = pl.pallas_call(
        _kernel,
        out_shape=(
            jax.ShapeDtypeStruct((c2, n2), BF16),
            jax.ShapeDtypeStruct((2 * ny1 * c1, 2 * q), BF16),
            jax.ShapeDtypeStruct(k1m.shape, F32),
            jax.ShapeDtypeStruct(k2m.shape, F32),
        ),
        scratch_shapes=[
            vm((nzi, ny + 1, 8 * c0, q), BF16),
            vm((n_act, k1m.shape[1], ny1 * q), BF16),
            vm((n_act, ny1 + 1, 4 * c1, q), BF16),
            vm((2, 2 * c1, ny1 * q), F32),
            vm((2, k2m.shape[1], n2), BF16),
            vm((2, c2, n2), BF16),
            vm((k2m.shape[1], n2), F32),
            vm((2, 2 * c1, ny1 * q), F32),
            vm((2, 2 * c1, ny1 * q), BF16),
            vm((2 * ny1 * c1, 2 * q), BF16),
        ],
        cost_estimate=pl.CostEstimate(flops=60_000_000, transcendentals=200_000, bytes_accessed=3_000_000),
    )(vz, k1m, k2m, k2t, cots)

    level_two = lvl.reshape(1, c2, 1, ny2, n2 // ny2)
    grad_one = g1.reshape(2, ny1, c1, 2 * q).transpose(2, 0, 1, 3)[None]

    s2r = s2.reshape(c2, 3, 3, 2, 2, c1)
    gk2 = jnp.stack([s2r[:, :, :, 1, 1], s2r[:, :, :, 0, 0], s2r[:, :, :, 0, 1]], -1)
    gk2 = gk2.transpose(0, 3, 1, 2, 4)
    s1r = s1.reshape(2, c1, 3, 3, 2, c0, 4)
    gk1 = jnp.stack([
        s1r[0, :, :, :, 1, :, 3] + s1r[1, :, :, :, 0, :, 1],
        s1r[0, :, :, :, 0, :, 0] + s1r[1, :, :, :, 0, :, 2],
        s1r[0, :, :, :, 0, :, 1] + s1r[1, :, :, :, 0, :, 3],
    ], -1).transpose(0, 3, 1, 2, 4)

    n1 = gk1.size
    total = lax.psum(jnp.concatenate([gk1.reshape(-1), gk2.reshape(-1)]), ("gz", "sa"))
    samples = volume.shape[0] * lax.axis_size("sa")
    cells_one = samples * (nz // 2) * lax.axis_size("gz") * ny1 * (nx // 2)
    cells_two = samples * cotangent.shape[2] * lax.axis_size("gz") * cotangent.shape[3] * cotangent.shape[4]
    grad_kernel_one = total[:n1].reshape(gk1.shape) / math.sqrt(float(cells_one))
    grad_kernel_two = total[n1:].reshape(gk2.shape) / math.sqrt(float(cells_two))
    return (level_two, grad_one, grad_kernel_one, grad_kernel_two)


def solution(mesh):
    placed = (P("sa", None, "gz", None, None), P(), P(), P("sa", None, "gz", None, None))
    return jax.shard_map(
        per_device,
        mesh=mesh,
        in_specs=placed,
        out_specs=(P("sa", None, "gz", None, None), P("sa", None, "gz", None, None), P(), P()),
        check_vma=False,
    )
```

```python
import math

import jax
import jax.numpy as jnp
from jax import lax
from jax.experimental import pallas as pl
from jax.experimental.pallas import tpu as pltpu
from jax.sharding import PartitionSpec as P

F32 = jnp.float32
BF16 = jnp.bfloat16


def shifted(block, axis, distance):
    devices = range(lax.axis_size(axis))
    route = [(i - distance, i) for i in devices if i - distance in devices]
    return lax.ppermute(block, axis, route)


def _all_sum(x, axes):
    for axis in axes:
        n = lax.axis_size(axis)
        assert n & (n - 1) == 0
        k = 1
        while k < n:
            x = x + lax.ppermute(x, axis, [(i, i ^ k) for i in range(n)])
            k *= 2
    return x


def _sigmoid(v):
    return 1.0 / (1.0 + jnp.exp(-v))


def _shift_right(x):
    lane = lax.broadcasted_iota(jnp.int32, x.shape, x.ndim - 1)
    return jnp.where(lane == 0, 0.0, pltpu.roll(x, 1, x.ndim - 1))


def _shift_left(x):
    n = x.shape[-1]
    lane = lax.broadcasted_iota(jnp.int32, x.shape, x.ndim - 1)
    return jnp.where(lane == n - 1, 0.0, pltpu.roll(x, n - 1, x.ndim - 1))


def _nt(a, b):
    return lax.dot_general(a, b, (((1,), (1,)), ((), ())), preferred_element_type=F32)


def _kernel(vz_ref, k1_ref, k2_ref, k2t_ref, cot_ref,
            lvl_ref, g1_ref, s1_ref, s2_ref,
            tp, p1, t2, pre1, p2, bt, gs, gacc, b1, g1s):
    nzi, ny, rows0, lanes = vz_ref.shape
    n_act = p1.shape[0]
    ny1 = ny // 2
    ny2 = ny1 // 2
    c2 = t2.shape[2]
    c1 = c2 // 2

    tp[:, 0] = jnp.zeros((nzi, 2 * rows0, lanes), BF16)
    for zi in range(nzi):
        x = vz_ref[zi].astype(F32)
        tp[zi, 1:] = jnp.concatenate([x, _shift_right(x)], axis=1).astype(BF16)

    for a in range(n_act):
        for d in range(3):
            for y1 in range(ny1):
                p1[a, d * 3 * 2 * rows0:(d + 1) * 3 * 2 * rows0, y1 * lanes:(y1 + 1) * lanes] = (
                    tp[2 * a + d, 2 * y1:2 * y1 + 3].reshape(3 * 2 * rows0, lanes))

    k1 = k1_ref[...]
    t2[:, 0] = jnp.zeros((n_act, c2, lanes), BF16)
    for a in range(n_act):
        pre = jnp.dot(k1, p1[a], preferred_element_type=F32)
        if a in (1, 2):
            pre1[a - 1] = pre
        act = pre * _sigmoid(pre)
        for y1 in range(ny1):
            blk = act[:, y1 * lanes:(y1 + 1) * lanes]
            t2[a, y1 + 1] = jnp.concatenate([blk, _shift_right(blk)], axis=0).astype(BF16)

    for tt in range(2):
        for d in range(3):
            for y2 in range(ny2):
                p2[tt, d * 3 * c2:(d + 1) * 3 * c2, y2 * lanes:(y2 + 1) * lanes] = (
                    t2[2 * tt + d, 2 * y2:2 * y2 + 3].reshape(3 * c2, lanes))

    k2 = k2_ref[...]
    for tt in range(2):
        pre = jnp.dot(k2, p2[tt], preferred_element_type=F32)
        sig = _sigmoid(pre)
        if tt == 0:
            lvl_ref[...] = (pre * sig).astype(BF16)
        slope = sig * (1.0 + pre * (1.0 - sig))
        bt[tt] = (cot_ref[tt].astype(F32) * slope).astype(BF16)

    dup = _nt(p2[0], jnp.concatenate([bt[0], bt[0]], axis=0))
    c2n = dup.shape[1] // 2
    qi = c1 // 4
    lane2 = lax.broadcasted_iota(jnp.int32, (qi, 2 * c2n), 1)
    for dh in range(9):
        for w, off in enumerate((3 * c1 // 2, 0, c1 // 2)):
            r0 = dh * c2 + off
            s2_ref[(dh * 3 + w) * qi:(dh * 3 + w + 1) * qi] = jnp.where(
                lane2 < c2n, dup[r0:r0 + qi], dup[r0 + qi:r0 + 2 * qi])

    gacc[...] = jnp.zeros(gacc.shape, F32)
    k2t = k2t_ref[...]
    for tt in range(2):
        if tt == 0:
            gs[...] = jnp.dot(k2t, bt[0], preferred_element_type=F32)
            taps_d = (1, 2)
        else:
            gs[0:3 * c2] = jnp.dot(k2t[0:3 * c2], bt[1], preferred_element_type=F32)
            taps_d = (0,)
        for d in taps_d:
            a = 2 * tt + d
            for h in range(3):
                for y2 in range(ny2):
                    y1 = 2 * y2 + h - 1
                    if y1 < 0:
                        continue
                    r0 = (d * 3 + h) * c2
                    blk = gs[r0:r0 + c2, y2 * lanes:(y2 + 1) * lanes]
                    gacc[a - 1, :, y1 * lanes:(y1 + 1) * lanes] += blk[:c1] + _shift_left(blk[c1:])

    half = c1 // 2
    for a_ in range(2):
        g = gacc[a_]
        pre = pre1[a_]
        sig = _sigmoid(pre)
        slope = sig * (1.0 + pre * (1.0 - sig))
        b1[a_] = (g * slope).astype(BF16)
        gb = g.astype(BF16)
        for y1 in range(ny1):
            blk = gb[:, y1 * lanes:(y1 + 1) * lanes]
            r0 = (a_ * ny1 + y1) * half
            g1s[r0:r0 + half] = jnp.concatenate([blk[:half], blk[half:]], axis=1)
    s1_ref[...] = _nt(p1[1], b1[0]) + _nt(p1[2], b1[1])

    n2 = 2 * lanes
    row = lax.broadcasted_iota(jnp.int32, (n2, n2), 0)
    col = lax.broadcasted_iota(jnp.int32, (n2, n2), 1)
    inter = jnp.where(col == 2 * (row % lanes) + row // lanes, 1.0, 0.0).astype(BF16)
    g1_ref[...] = jnp.dot(g1s[...], inter, preferred_element_type=F32).astype(BF16)


def _level_one_weights(k1):
    kt = jnp.transpose(k1, (0, 2, 3, 1, 4))
    w0, w1, w2 = kt[..., 0], kt[..., 1], kt[..., 2]
    z = jnp.zeros_like(w0)
    p0 = jnp.stack([jnp.stack([w1, w2, z, z], -1), jnp.stack([z, z, z, w0], -1)], 3)
    p1 = jnp.stack([jnp.stack([z, w0, w1, w2], -1), jnp.stack([z, z, z, z], -1)], 3)
    e = jnp.stack([p0, p1], 0)
    return e.reshape(2 * k1.shape[0], -1)


def _level_two_weights(k2):
    kt = jnp.transpose(k2, (0, 2, 3, 4, 1))
    w0, w1, w2 = kt[:, :, :, 0], kt[:, :, :, 1], kt[:, :, :, 2]
    z = jnp.zeros_like(w0)
    e = jnp.stack([jnp.stack([w1, w2], 3), jnp.stack([z, w0], 3)], 3)
    return e.reshape(k2.shape[0], -1)


def per_device(volume, kernel_one, kernel_two, cotangent):
    _, c0, nz, ny, nx = volume.shape
    c1 = kernel_one.shape[0]
    c2 = kernel_two.shape[0]
    assert nz == 4 and cotangent.shape[2] == 1
    q = nx // 4
    below = shifted(volume[:, :, 1:], "gz", 1)
    above = shifted(volume, "gz", -1)
    cot_above = shifted(cotangent, "gz", -1)
    ext = jnp.concatenate([below, volume, above], 2)[0]
    nzi = ext.shape[1]
    vz = ext.reshape(c0, nzi, ny, q, 4).transpose(1, 2, 0, 4, 3).reshape(nzi, ny, 4 * c0, q)
    n2 = cotangent.shape[3] * cotangent.shape[4]
    cots = jnp.concatenate([cotangent, cot_above], 2)[0].transpose(1, 0, 2, 3).reshape(2, c2, n2)

    k1m = _level_one_weights(kernel_one)
    k2m = _level_two_weights(kernel_two)
    k2t = k2m.T

    ny1, ny2 = ny // 2, ny // 4
    n_act = 5
    vm = pltpu.VMEM
    lvl, g1, s1, s2 = pl.pallas_call(
        _kernel,
        out_shape=(
            jax.ShapeDtypeStruct((c2, n2), BF16),
            jax.ShapeDtypeStruct((2 * ny1 * c1, 2 * q), BF16),
            jax.ShapeDtypeStruct((k1m.shape[1], k1m.shape[0]), F32),
            jax.ShapeDtypeStruct((27 * c1 // 2, 2 * c2), F32),
        ),
        scratch_shapes=[
            vm((nzi, ny + 1, 8 * c0, q), BF16),
            vm((n_act, k1m.shape[1], ny1 * q), BF16),
            vm((n_act, ny1 + 1, 4 * c1, q), BF16),
            vm((2, 2 * c1, ny1 * q), F32),
            vm((2, k2m.shape[1], n2), BF16),
            vm((2, c2, n2), BF16),
            vm((k2m.shape[1], n2), F32),
            vm((2, 2 * c1, ny1 * q), F32),
            vm((2, 2 * c1, ny1 * q), BF16),
            vm((2 * ny1 * c1, 2 * q), BF16),
        ],
        cost_estimate=pl.CostEstimate(flops=60_000_000, transcendentals=200_000, bytes_accessed=3_000_000),
    )(vz, k1m, k2m, k2t, cots)

    level_two = lvl.reshape(1, c2, 1, ny2, n2 // ny2)
    grad_one = g1.reshape(2, ny1, c1, 2 * q).transpose(2, 0, 1, 3)[None]

    s1r = s1.reshape(3, 3, 2, c0, 4, 2, c1)
    gk1 = jnp.stack([
        s1r[:, :, 1, :, 3, 0] + s1r[:, :, 0, :, 1, 1],
        s1r[:, :, 0, :, 0, 0] + s1r[:, :, 0, :, 2, 1],
        s1r[:, :, 0, :, 1, 0] + s1r[:, :, 0, :, 3, 1],
    ], 2)
    rows1 = gk1.size // s2.shape[1]
    total = _all_sum(jnp.concatenate([gk1.reshape(rows1, s2.shape[1]), s2], 0), ("gz", "sa"))
    samples = volume.shape[0] * lax.axis_size("sa")
    cells_one = samples * (nz // 2) * lax.axis_size("gz") * ny1 * (nx // 2)
    cells_two = samples * cotangent.shape[2] * lax.axis_size("gz") * cotangent.shape[3] * cotangent.shape[4]
    t1 = total[:rows1] / math.sqrt(float(cells_one))
    t2 = total[rows1:] / math.sqrt(float(cells_two))
    grad_kernel_one = t1.reshape(3, 3, 3, c0, c1).transpose(4, 3, 0, 1, 2)
    t2 = t2.reshape(27, c1 // 2, 2, c2).transpose(0, 2, 1, 3).reshape(3, 3, 3, c1, c2)
    grad_kernel_two = t2.transpose(4, 3, 0, 1, 2)
    return (level_two, grad_one, grad_kernel_one, grad_kernel_two)


def solution(mesh):
    placed = (P("sa", None, "gz", None, None), P(), P(), P("sa", None, "gz", None, None))
    return jax.shard_map(
        per_device,
        mesh=mesh,
        in_specs=placed,
        out_specs=(P("sa", None, "gz", None, None), P("sa", None, "gz", None, None), P(), P()),
        check_vma=False,
    )
```

```python
import math

import jax
import jax.numpy as jnp
from jax import lax
from jax.experimental import pallas as pl
from jax.experimental.pallas import tpu as pltpu
from jax.sharding import PartitionSpec as P

F32 = jnp.float32
BF16 = jnp.bfloat16


def shifted(block, axis, distance):
    devices = range(lax.axis_size(axis))
    route = [(i - distance, i) for i in devices if i - distance in devices]
    return lax.ppermute(block, axis, route)


def _all_sum(x, axes):
    for axis in axes:
        n = lax.axis_size(axis)
        assert n & (n - 1) == 0
        k = 1
        while k < n:
            x = x + lax.ppermute(x, axis, [(i, i ^ k) for i in range(n)])
            k *= 2
    return x


def _sigmoid(v):
    return 1.0 / (1.0 + jnp.exp(-v))


def _shift_right(x):
    lane = lax.broadcasted_iota(jnp.int32, x.shape, x.ndim - 1)
    return jnp.where(lane == 0, 0.0, pltpu.roll(x, 1, x.ndim - 1))


def _shift_left(x):
    n = x.shape[-1]
    lane = lax.broadcasted_iota(jnp.int32, x.shape, x.ndim - 1)
    return jnp.where(lane == n - 1, 0.0, pltpu.roll(x, n - 1, x.ndim - 1))


def _nt(a, b):
    return lax.dot_general(a, b, (((1,), (1,)), ((), ())), preferred_element_type=F32)


def _kernel(vb_ref, vo_ref, va_ref, k1_ref, k2_ref, k2t_ref, cot_ref,
            lvl_ref, g1_ref, s1_ref, s2_ref,
            tp, p1, t2, pre1, p2, bt, gs, gacc, b1, g1s):
    c0, ny, nx = vo_ref.shape[1], vo_ref.shape[3], vo_ref.shape[4]
    lanes = nx // 4
    nzi = tp.shape[0]
    n_act = p1.shape[0]
    ny1 = ny // 2
    ny2 = ny1 // 2
    c2 = t2.shape[2]
    c1 = c2 // 2
    rows0 = 4 * c0

    xs = lax.broadcasted_iota(jnp.int32, (nx, nx), 0)
    cs = lax.broadcasted_iota(jnp.int32, (nx, nx), 1)
    sel_x = jnp.where(xs == 4 * (cs % lanes) + cs // lanes, 1.0, 0.0).astype(BF16)
    nq = 2 * rows0 * ny
    orow = lax.broadcasted_iota(jnp.int32, (nq, nq), 0)
    icol = lax.broadcasted_iota(jnp.int32, (nq, nq), 1)
    y_, s_ = orow // (2 * rows0), (orow // rows0) % 2
    i_, r_ = (orow // 4) % c0, orow % 4
    perm = jnp.where(icol == ((s_ * 4 + r_) * c0 + i_) * ny + y_, 1.0, 0.0).astype(BF16)

    tp[:, 0] = jnp.zeros((nzi, 2 * rows0, lanes), BF16)
    pieces = [(vb_ref, z) for z in range(vb_ref.shape[2])] + [(vo_ref, z) for z in range(vo_ref.shape[2])] + [
        (va_ref, z) for z in range(va_ref.shape[2])]
    for zi, (ref, z) in enumerate(pieces):
        zmat = ref[0, :, z].reshape(c0 * ny, nx)
        ymat = jnp.dot(zmat, sel_x, preferred_element_type=F32)
        blocks = [ymat[:, r * lanes:(r + 1) * lanes] for r in range(4)]
        q = jnp.concatenate(blocks + [_shift_right(b) for b in blocks], axis=0).astype(BF16)
        t = jnp.dot(perm, q, preferred_element_type=F32).astype(BF16)
        tp[zi, 1:] = t.reshape(ny, 2 * rows0, lanes)

    for a in range(n_act):
        for d in range(3):
            for y1 in range(ny1):
                p1[a, d * 3 * 2 * rows0:(d + 1) * 3 * 2 * rows0, y1 * lanes:(y1 + 1) * lanes] = (
                    tp[2 * a + d, 2 * y1:2 * y1 + 3].reshape(3 * 2 * rows0, lanes))

    k1 = k1_ref[...]
    t2[:, 0] = jnp.zeros((n_act, c2, lanes), BF16)
    for a in range(n_act):
        pre = jnp.dot(k1, p1[a], preferred_element_type=F32)
        if a in (1, 2):
            pre1[a - 1] = pre
        act = pre * _sigmoid(pre)
        for y1 in range(ny1):
            blk = act[:, y1 * lanes:(y1 + 1) * lanes]
            t2[a, y1 + 1] = jnp.concatenate([blk, _shift_right(blk)], axis=0).astype(BF16)

    for tt in range(2):
        for d in range(3):
            for y2 in range(ny2):
                p2[tt, d * 3 * c2:(d + 1) * 3 * c2, y2 * lanes:(y2 + 1) * lanes] = (
                    t2[2 * tt + d, 2 * y2:2 * y2 + 3].reshape(3 * c2, lanes))

    k2 = k2_ref[...]
    for tt in range(2):
        pre = jnp.dot(k2, p2[tt], preferred_element_type=F32)
        sig = _sigmoid(pre)
        if tt == 0:
            lvl_ref[...] = (pre * sig).astype(BF16)
        slope = sig * (1.0 + pre * (1.0 - sig))
        bt[tt] = (cot_ref[tt].astype(F32) * slope).astype(BF16)

    dup = _nt(p2[0], jnp.concatenate([bt[0], bt[0]], axis=0))
    c2n = dup.shape[1] // 2
    qi = c1 // 4
    lane2 = lax.broadcasted_iota(jnp.int32, (qi, 2 * c2n), 1)
    for dh in range(9):
        for w, off in enumerate((3 * c1 // 2, 0, c1 // 2)):
            r0 = dh * c2 + off
            s2_ref[(dh * 3 + w) * qi:(dh * 3 + w + 1) * qi] = jnp.where(
                lane2 < c2n, dup[r0:r0 + qi], dup[r0 + qi:r0 + 2 * qi])

    gacc[...] = jnp.zeros(gacc.shape, F32)
    k2t = k2t_ref[...]
    for tt in range(2):
        if tt == 0:
            gs[...] = jnp.dot(k2t, bt[0], preferred_element_type=F32)
            taps_d = (1, 2)
        else:
            gs[0:3 * c2] = jnp.dot(k2t[0:3 * c2], bt[1], preferred_element_type=F32)
            taps_d = (0,)
        for d in taps_d:
            a = 2 * tt + d
            for h in range(3):
                for y2 in range(ny2):
                    y1 = 2 * y2 + h - 1
                    if y1 < 0:
                        continue
                    r0 = (d * 3 + h) * c2
                    blk = gs[r0:r0 + c2, y2 * lanes:(y2 + 1) * lanes]
                    gacc[a - 1, :, y1 * lanes:(y1 + 1) * lanes] += blk[:c1] + _shift_left(blk[c1:])

    half = c1 // 2
    for a_ in range(2):
        g = gacc[a_]
        pre = pre1[a_]
        sig = _sigmoid(pre)
        slope = sig * (1.0 + pre * (1.0 - sig))
        b1[a_] = (g * slope).astype(BF16)
        gb = g.astype(BF16)
        for y1 in range(ny1):
            blk = gb[:, y1 * lanes:(y1 + 1) * lanes]
            r0 = (a_ * ny1 + y1) * half
            g1s[r0:r0 + half] = jnp.concatenate([blk[:half], blk[half:]], axis=1)
    s1_ref[...] = _nt(p1[1], b1[0]) + _nt(p1[2], b1[1])

    n2 = 2 * lanes
    row = lax.broadcasted_iota(jnp.int32, (n2, n2), 0)
    col = lax.broadcasted_iota(jnp.int32, (n2, n2), 1)
    inter = jnp.where(col == 2 * (row % lanes) + row // lanes, 1.0, 0.0).astype(BF16)
    g1_ref[...] = jnp.dot(g1s[...], inter, preferred_element_type=F32).astype(BF16)


def _level_one_weights(k1):
    kt = jnp.transpose(k1, (0, 2, 3, 1, 4))
    w0, w1, w2 = kt[..., 0], kt[..., 1], kt[..., 2]
    z = jnp.zeros_like(w0)
    p0 = jnp.stack([jnp.stack([w1, w2, z, z], -1), jnp.stack([z, z, z, w0], -1)], 3)
    p1 = jnp.stack([jnp.stack([z, w0, w1, w2], -1), jnp.stack([z, z, z, z], -1)], 3)
    e = jnp.stack([p0, p1], 0)
    return e.reshape(2 * k1.shape[0], -1)


def _level_two_weights(k2):
    kt = jnp.transpose(k2, (0, 2, 3, 4, 1))
    w0, w1, w2 = kt[:, :, :, 0], kt[:, :, :, 1], kt[:, :, :, 2]
    z = jnp.zeros_like(w0)
    e = jnp.stack([jnp.stack([w1, w2], 3), jnp.stack([z, w0], 3)], 3)
    return e.reshape(k2.shape[0], -1)


def per_device(volume, kernel_one, kernel_two, cotangent):
    _, c0, nz, ny, nx = volume.shape
    c1 = kernel_one.shape[0]
    c2 = kernel_two.shape[0]
    assert nz == 4 and cotangent.shape[2] == 1
    q = nx // 4
    below = shifted(volume[:, :, 1:], "gz", 1)
    above = shifted(volume, "gz", -1)
    cot_above = shifted(cotangent, "gz", -1)
    nzi = below.shape[2] + nz + above.shape[2]
    n2 = cotangent.shape[3] * cotangent.shape[4]
    cots = jnp.concatenate([cotangent, cot_above], 2)[0].transpose(1, 0, 2, 3).reshape(2, c2, n2)

    k1m = _level_one_weights(kernel_one)
    k2m = _level_two_weights(kernel_two)
    k2t = k2m.T

    ny1, ny2 = ny // 2, ny // 4
    n_act = 5
    vm = pltpu.VMEM
    lvl, g1, s1, s2 = pl.pallas_call(
        _kernel,
        out_shape=(
            jax.ShapeDtypeStruct((c2, n2), BF16),
            jax.ShapeDtypeStruct((2 * ny1 * c1, 2 * q), BF16),
            jax.ShapeDtypeStruct((k1m.shape[1], k1m.shape[0]), F32),
            jax.ShapeDtypeStruct((27 * c1 // 2, 2 * c2), F32),
        ),
        scratch_shapes=[
            vm((nzi, ny + 1, 8 * c0, q), BF16),
            vm((n_act, k1m.shape[1], ny1 * q), BF16),
            vm((n_act, ny1 + 1, 4 * c1, q), BF16),
            vm((2, 2 * c1, ny1 * q), F32),
            vm((2, k2m.shape[1], n2), BF16),
            vm((2, c2, n2), BF16),
            vm((k2m.shape[1], n2), F32),
            vm((2, 2 * c1, ny1 * q), F32),
            vm((2, 2 * c1, ny1 * q), BF16),
            vm((2 * ny1 * c1, 2 * q), BF16),
        ],
        cost_estimate=pl.CostEstimate(flops=60_000_000, transcendentals=200_000, bytes_accessed=3_000_000),
    )(below, volume, above, k1m, k2m, k2t, cots)

    level_two = lvl.reshape(1, c2, 1, ny2, n2 // ny2)
    grad_one = g1.reshape(2, ny1, c1, 2 * q).transpose(2, 0, 1, 3)[None]

    s1r = s1.reshape(3, 3, 2, c0, 4, 2, c1)
    gk1 = jnp.stack([
        s1r[:, :, 1, :, 3, 0] + s1r[:, :, 0, :, 1, 1],
        s1r[:, :, 0, :, 0, 0] + s1r[:, :, 0, :, 2, 1],
        s1r[:, :, 0, :, 1, 0] + s1r[:, :, 0, :, 3, 1],
    ], 2)
    rows1 = gk1.size // s2.shape[1]
    total = _all_sum(jnp.concatenate([gk1.reshape(rows1, s2.shape[1]), s2], 0), ("gz", "sa"))
    samples = volume.shape[0] * lax.axis_size("sa")
    cells_one = samples * (nz // 2) * lax.axis_size("gz") * ny1 * (nx // 2)
    cells_two = samples * cotangent.shape[2] * lax.axis_size("gz") * cotangent.shape[3] * cotangent.shape[4]
    t1 = total[:rows1] / math.sqrt(float(cells_one))
    t2 = total[rows1:] / math.sqrt(float(cells_two))
    grad_kernel_one = t1.reshape(3, 3, 3, c0, c1).transpose(4, 3, 0, 1, 2)
    t2 = t2.reshape(27, c1 // 2, 2, c2).transpose(0, 2, 1, 3).reshape(3, 3, 3, c1, c2)
    grad_kernel_two = t2.transpose(4, 3, 0, 1, 2)
    return (level_two, grad_one, grad_kernel_one, grad_kernel_two)


def solution(mesh):
    placed = (P("sa", None, "gz", None, None), P(), P(), P("sa", None, "gz", None, None))
    return jax.shard_map(
        per_device,
        mesh=mesh,
        in_specs=placed,
        out_specs=(P("sa", None, "gz", None, None), P("sa", None, "gz", None, None), P(), P()),
        check_vma=False,
    )
```

```python
import math

import jax
import jax.numpy as jnp
from jax import lax
from jax.experimental import pallas as pl
from jax.experimental.pallas import tpu as pltpu
from jax.sharding import PartitionSpec as P

F32 = jnp.float32
BF16 = jnp.bfloat16


def shifted(block, axis, distance):
    devices = range(lax.axis_size(axis))
    route = [(i - distance, i) for i in devices if i - distance in devices]
    return lax.ppermute(block, axis, route)


def _all_sum(x, axes):
    steps = []
    for axis in axes:
        n = lax.axis_size(axis)
        assert n & (n - 1) == 0
        k = 1
        while k < n:
            steps.append((axis, n, k))
            k *= 2
    m = len(steps)
    size = -(-x.shape[0] // (8 * m)) * 8
    chunks = [x[c * size:(c + 1) * size] for c in range(m) if c * size < x.shape[0]]
    for j in range(m):
        for c in range(len(chunks)):
            axis, n, k = steps[(c + j) % m]
            chunks[c] = chunks[c] + lax.ppermute(chunks[c], axis, [(i, i ^ k) for i in range(n)])
    return jnp.concatenate(chunks, 0)


def _sigmoid(v):
    return 1.0 / (1.0 + jnp.exp(-v))


def _shift_right(x):
    lane = lax.broadcasted_iota(jnp.int32, x.shape, x.ndim - 1)
    return jnp.where(lane == 0, 0.0, pltpu.roll(x, 1, x.ndim - 1))


def _shift_left(x):
    n = x.shape[-1]
    lane = lax.broadcasted_iota(jnp.int32, x.shape, x.ndim - 1)
    return jnp.where(lane == n - 1, 0.0, pltpu.roll(x, n - 1, x.ndim - 1))


def _nt(a, b):
    return lax.dot_general(a, b, (((1,), (1,)), ((), ())), preferred_element_type=F32)


def _kernel(vb_ref, vo_ref, va_ref, k1_ref, k2_ref, k2t_ref, cot_ref,
            lvl_ref, g1_ref, s1_ref, s2_ref,
            tp, p1, t2, pre1, p2, bt, gs, gacc, b1, g1s):
    c0, ny, nx = vo_ref.shape[1], vo_ref.shape[3], vo_ref.shape[4]
    lanes = nx // 4
    nzi = tp.shape[0]
    n_act = p1.shape[0]
    ny1 = ny // 2
    ny2 = ny1 // 2
    c2 = t2.shape[2]
    c1 = c2 // 2
    rows0 = 4 * c0

    xs = lax.broadcasted_iota(jnp.int32, (nx, nx), 0)
    cs = lax.broadcasted_iota(jnp.int32, (nx, nx), 1)
    sel_x = jnp.where(xs == 4 * (cs % lanes) + cs // lanes, 1.0, 0.0).astype(BF16)
    nq = 2 * rows0 * ny
    orow = lax.broadcasted_iota(jnp.int32, (nq, nq), 0)
    icol = lax.broadcasted_iota(jnp.int32, (nq, nq), 1)
    y_, s_ = orow // (2 * rows0), (orow // rows0) % 2
    i_, r_ = (orow // 4) % c0, orow % 4
    perm = jnp.where(icol == ((s_ * 4 + r_) * c0 + i_) * ny + y_, 1.0, 0.0).astype(BF16)

    tp[:, 0] = jnp.zeros((nzi, 2 * rows0, lanes), BF16)
    pieces = [(vb_ref, z) for z in range(vb_ref.shape[2])] + [(vo_ref, z) for z in range(vo_ref.shape[2])] + [
        (va_ref, z) for z in range(va_ref.shape[2])]
    for zi, (ref, z) in enumerate(pieces):
        zmat = ref[0, :, z].reshape(c0 * ny, nx)
        ymat = jnp.dot(zmat, sel_x, preferred_element_type=F32)
        blocks = [ymat[:, r * lanes:(r + 1) * lanes] for r in range(4)]
        q = jnp.concatenate(blocks + [_shift_right(b) for b in blocks], axis=0).astype(BF16)
        t = jnp.dot(perm, q, preferred_element_type=F32).astype(BF16)
        tp[zi, 1:] = t.reshape(ny, 2 * rows0, lanes)

    for a in range(n_act):
        for d in range(3):
            for y1 in range(ny1):
                p1[a, d * 3 * 2 * rows0:(d + 1) * 3 * 2 * rows0, y1 * lanes:(y1 + 1) * lanes] = (
                    tp[2 * a + d, 2 * y1:2 * y1 + 3].reshape(3 * 2 * rows0, lanes))

    k1 = k1_ref[...]
    t2[:, 0] = jnp.zeros((n_act, c2, lanes), BF16)
    for a in range(n_act):
        pre = jnp.dot(k1, p1[a], preferred_element_type=F32)
        if a in (1, 2):
            pre1[a - 1] = pre
        act = pre * _sigmoid(pre)
        for y1 in range(ny1):
            blk = act[:, y1 * lanes:(y1 + 1) * lanes]
            t2[a, y1 + 1] = jnp.concatenate([blk, _shift_right(blk)], axis=0).astype(BF16)

    for tt in range(2):
        for d in range(3):
            for y2 in range(ny2):
                p2[tt, d * 3 * c2:(d + 1) * 3 * c2, y2 * lanes:(y2 + 1) * lanes] = (
                    t2[2 * tt + d, 2 * y2:2 * y2 + 3].reshape(3 * c2, lanes))

    k2 = k2_ref[...]
    for tt in range(2):
        pre = jnp.dot(k2, p2[tt], preferred_element_type=F32)
        sig = _sigmoid(pre)
        if tt == 0:
            lvl_ref[...] = (pre * sig).astype(BF16)
        slope = sig * (1.0 + pre * (1.0 - sig))
        bt[tt] = (cot_ref[tt].astype(F32) * slope).astype(BF16)

    dup = _nt(p2[0], jnp.concatenate([bt[0], bt[0]], axis=0))
    c2n = dup.shape[1] // 2
    qi = c1 // 4
    lane2 = lax.broadcasted_iota(jnp.int32, (qi, 2 * c2n), 1)
    for dh in range(9):
        for w, off in enumerate((3 * c1 // 2, 0, c1 // 2)):
            r0 = dh * c2 + off
            s2_ref[(dh * 3 + w) * qi:(dh * 3 + w + 1) * qi] = jnp.where(
                lane2 < c2n, dup[r0:r0 + qi], dup[r0 + qi:r0 + 2 * qi])

    gacc[...] = jnp.zeros(gacc.shape, F32)
    k2t = k2t_ref[...]
    for tt in range(2):
        if tt == 0:
            gs[...] = jnp.dot(k2t, bt[0], preferred_element_type=F32)
            taps_d = (1, 2)
        else:
            gs[0:3 * c2] = jnp.dot(k2t[0:3 * c2], bt[1], preferred_element_type=F32)
            taps_d = (0,)
        for d in taps_d:
            a = 2 * tt + d
            for h in range(3):
                for y2 in range(ny2):
                    y1 = 2 * y2 + h - 1
                    if y1 < 0:
                        continue
                    r0 = (d * 3 + h) * c2
                    blk = gs[r0:r0 + c2, y2 * lanes:(y2 + 1) * lanes]
                    gacc[a - 1, :, y1 * lanes:(y1 + 1) * lanes] += blk[:c1] + _shift_left(blk[c1:])

    half = c1 // 2
    for a_ in range(2):
        g = gacc[a_]
        pre = pre1[a_]
        sig = _sigmoid(pre)
        slope = sig * (1.0 + pre * (1.0 - sig))
        b1[a_] = (g * slope).astype(BF16)
        gb = g.astype(BF16)
        for y1 in range(ny1):
            blk = gb[:, y1 * lanes:(y1 + 1) * lanes]
            r0 = (a_ * ny1 + y1) * half
            g1s[r0:r0 + half] = jnp.concatenate([blk[:half], blk[half:]], axis=1)
    s1_ref[...] = _nt(p1[1], b1[0]) + _nt(p1[2], b1[1])

    n2 = 2 * lanes
    row = lax.broadcasted_iota(jnp.int32, (n2, n2), 0)
    col = lax.broadcasted_iota(jnp.int32, (n2, n2), 1)
    inter = jnp.where(col == 2 * (row % lanes) + row // lanes, 1.0, 0.0).astype(BF16)
    g1_ref[...] = jnp.dot(g1s[...], inter, preferred_element_type=F32).astype(BF16)


def _level_one_weights(k1):
    kt = jnp.transpose(k1, (0, 2, 3, 1, 4))
    w0, w1, w2 = kt[..., 0], kt[..., 1], kt[..., 2]
    z = jnp.zeros_like(w0)
    p0 = jnp.stack([jnp.stack([w1, w2, z, z], -1), jnp.stack([z, z, z, w0], -1)], 3)
    p1 = jnp.stack([jnp.stack([z, w0, w1, w2], -1), jnp.stack([z, z, z, z], -1)], 3)
    e = jnp.stack([p0, p1], 0)
    return e.reshape(2 * k1.shape[0], -1)


def _level_two_weights(k2):
    kt = jnp.transpose(k2, (0, 2, 3, 4, 1))
    w0, w1, w2 = kt[:, :, :, 0], kt[:, :, :, 1], kt[:, :, :, 2]
    z = jnp.zeros_like(w0)
    e = jnp.stack([jnp.stack([w1, w2], 3), jnp.stack([z, w0], 3)], 3)
    return e.reshape(k2.shape[0], -1)


def per_device(volume, kernel_one, kernel_two, cotangent):
    _, c0, nz, ny, nx = volume.shape
    c1 = kernel_one.shape[0]
    c2 = kernel_two.shape[0]
    assert nz == 4 and cotangent.shape[2] == 1
    q = nx // 4
    below = shifted(volume[:, :, 1:], "gz", 1)
    above = shifted(volume, "gz", -1)
    cot_above = shifted(cotangent, "gz", -1)
    nzi = below.shape[2] + nz + above.shape[2]
    n2 = cotangent.shape[3] * cotangent.shape[4]
    cots = jnp.concatenate([cotangent, cot_above], 2)[0].transpose(1, 0, 2, 3).reshape(2, c2, n2)

    k1m = _level_one_weights(kernel_one)
    k2m = _level_two_weights(kernel_two)
    k2t = k2m.T

    ny1, ny2 = ny // 2, ny // 4
    n_act = 5
    vm = pltpu.VMEM
    lvl, g1, s1, s2 = pl.pallas_call(
        _kernel,
        out_shape=(
            jax.ShapeDtypeStruct((c2, n2), BF16),
            jax.ShapeDtypeStruct((2 * ny1 * c1, 2 * q), BF16),
            jax.ShapeDtypeStruct((k1m.shape[1], k1m.shape[0]), F32),
            jax.ShapeDtypeStruct((27 * c1 // 2, 2 * c2), F32),
        ),
        scratch_shapes=[
            vm((nzi, ny + 1, 8 * c0, q), BF16),
            vm((n_act, k1m.shape[1], ny1 * q), BF16),
            vm((n_act, ny1 + 1, 4 * c1, q), BF16),
            vm((2, 2 * c1, ny1 * q), F32),
            vm((2, k2m.shape[1], n2), BF16),
            vm((2, c2, n2), BF16),
            vm((k2m.shape[1], n2), F32),
            vm((2, 2 * c1, ny1 * q), F32),
            vm((2, 2 * c1, ny1 * q), BF16),
            vm((2 * ny1 * c1, 2 * q), BF16),
        ],
        cost_estimate=pl.CostEstimate(flops=60_000_000, transcendentals=200_000, bytes_accessed=3_000_000),
    )(below, volume, above, k1m, k2m, k2t, cots)

    level_two = lvl.reshape(1, c2, 1, ny2, n2 // ny2)
    grad_one = g1.reshape(2, ny1, c1, 2 * q).transpose(2, 0, 1, 3)[None]

    s1r = s1.reshape(3, 3, 2, c0, 4, 2, c1)
    gk1 = jnp.stack([
        s1r[:, :, 1, :, 3, 0] + s1r[:, :, 0, :, 1, 1],
        s1r[:, :, 0, :, 0, 0] + s1r[:, :, 0, :, 2, 1],
        s1r[:, :, 0, :, 1, 0] + s1r[:, :, 0, :, 3, 1],
    ], 2)
    rows1 = gk1.size // s2.shape[1]
    total = _all_sum(jnp.concatenate([gk1.reshape(rows1, s2.shape[1]), s2], 0), ("gz", "sa"))
    samples = volume.shape[0] * lax.axis_size("sa")
    cells_one = samples * (nz // 2) * lax.axis_size("gz") * ny1 * (nx // 2)
    cells_two = samples * cotangent.shape[2] * lax.axis_size("gz") * cotangent.shape[3] * cotangent.shape[4]
    t1 = total[:rows1] / math.sqrt(float(cells_one))
    t2 = total[rows1:] / math.sqrt(float(cells_two))
    grad_kernel_one = t1.reshape(3, 3, 3, c0, c1).transpose(4, 3, 0, 1, 2)
    t2 = t2.reshape(27, c1 // 2, 2, c2).transpose(0, 2, 1, 3).reshape(3, 3, 3, c1, c2)
    grad_kernel_two = t2.transpose(4, 3, 0, 1, 2)
    return (level_two, grad_one, grad_kernel_one, grad_kernel_two)


def solution(mesh):
    placed = (P("sa", None, "gz", None, None), P(), P(), P("sa", None, "gz", None, None))
    return jax.shard_map(
        per_device,
        mesh=mesh,
        in_specs=placed,
        out_specs=(P("sa", None, "gz", None, None), P("sa", None, "gz", None, None), P(), P()),
        check_vma=False,
    )
```

```python
import math

import jax
import jax.numpy as jnp
from jax import lax
from jax.experimental import pallas as pl
from jax.experimental.pallas import tpu as pltpu
from jax.sharding import PartitionSpec as P

F32 = jnp.float32
BF16 = jnp.bfloat16


def shifted(block, axis, distance):
    devices = range(lax.axis_size(axis))
    route = [(i - distance, i) for i in devices if i - distance in devices]
    return lax.ppermute(block, axis, route)


def _all_sum(x, axes):
    steps = []
    for axis in axes:
        n = lax.axis_size(axis)
        assert n & (n - 1) == 0
        k = 1
        while k < n:
            steps.append((axis, n, k))
            k *= 2
    axis0, n0, k0 = steps[0]
    rows = x.shape[0]
    half = -(-rows // 16) * 8
    x = jnp.pad(x, ((0, 2 * half - rows), (0, 0)))
    low = (lax.axis_index(axis0) & k0) == 0
    lo, hi = x[:half], x[half:]
    pair = [(i, i ^ k0) for i in range(n0)]
    part = jnp.where(low, lo, hi) + lax.ppermute(jnp.where(low, hi, lo), axis0, pair)
    for axis, n, k in steps[1:]:
        part = part + lax.ppermute(part, axis, [(i, i ^ k) for i in range(n)])
    other = lax.ppermute(part, axis0, pair)
    return jnp.where(low, jnp.concatenate([part, other], 0), jnp.concatenate([other, part], 0))[:rows]


def _sigmoid(v):
    return 1.0 / (1.0 + jnp.exp(-v))


def _shift_right(x):
    lane = lax.broadcasted_iota(jnp.int32, x.shape, x.ndim - 1)
    return jnp.where(lane == 0, 0.0, pltpu.roll(x, 1, x.ndim - 1))


def _shift_left(x):
    n = x.shape[-1]
    lane = lax.broadcasted_iota(jnp.int32, x.shape, x.ndim - 1)
    return jnp.where(lane == n - 1, 0.0, pltpu.roll(x, n - 1, x.ndim - 1))


def _nt(a, b):
    return lax.dot_general(a, b, (((1,), (1,)), ((), ())), preferred_element_type=F32)


def _kernel(vb_ref, vo_ref, va_ref, k1_ref, k2_ref, k2t_ref, cot_ref,
            lvl_ref, g1_ref, s1_ref, s2_ref,
            tp, p1, t2, pre1, p2, bt, gs, gacc, b1, g1s):
    c0, ny, nx = vo_ref.shape[1], vo_ref.shape[3], vo_ref.shape[4]
    lanes = nx // 4
    nzi = tp.shape[0]
    n_act = p1.shape[0]
    ny1 = ny // 2
    ny2 = ny1 // 2
    c2 = t2.shape[2]
    c1 = c2 // 2
    rows0 = 4 * c0

    xs = lax.broadcasted_iota(jnp.int32, (nx, nx), 0)
    cs = lax.broadcasted_iota(jnp.int32, (nx, nx), 1)
    sel_x = jnp.where(xs == 4 * (cs % lanes) + cs // lanes, 1.0, 0.0).astype(BF16)
    nq = 2 * rows0 * ny
    orow = lax.broadcasted_iota(jnp.int32, (nq, nq), 0)
    icol = lax.broadcasted_iota(jnp.int32, (nq, nq), 1)
    y_, s_ = orow // (2 * rows0), (orow // rows0) % 2
    i_, r_ = (orow // 4) % c0, orow % 4
    perm = jnp.where(icol == ((s_ * 4 + r_) * c0 + i_) * ny + y_, 1.0, 0.0).astype(BF16)

    tp[:, 0] = jnp.zeros((nzi, 2 * rows0, lanes), BF16)
    pieces = [(vb_ref, z) for z in range(vb_ref.shape[2])] + [(vo_ref, z) for z in range(vo_ref.shape[2])] + [
        (va_ref, z) for z in range(va_ref.shape[2])]
    for zi, (ref, z) in enumerate(pieces):
        zmat = ref[0, :, z].reshape(c0 * ny, nx)
        ymat = jnp.dot(zmat, sel_x, preferred_element_type=F32)
        blocks = [ymat[:, r * lanes:(r + 1) * lanes] for r in range(4)]
        q = jnp.concatenate(blocks + [_shift_right(b) for b in blocks], axis=0).astype(BF16)
        t = jnp.dot(perm, q, preferred_element_type=F32).astype(BF16)
        tp[zi, 1:] = t.reshape(ny, 2 * rows0, lanes)

    for a in range(n_act):
        for d in range(3):
            for y1 in range(ny1):
                p1[a, d * 3 * 2 * rows0:(d + 1) * 3 * 2 * rows0, y1 * lanes:(y1 + 1) * lanes] = (
                    tp[2 * a + d, 2 * y1:2 * y1 + 3].reshape(3 * 2 * rows0, lanes))

    k1 = k1_ref[...]
    t2[:, 0] = jnp.zeros((n_act, c2, lanes), BF16)
    for a in range(n_act):
        pre = jnp.dot(k1, p1[a], preferred_element_type=F32)
        if a in (1, 2):
            pre1[a - 1] = pre
        act = pre * _sigmoid(pre)
        for y1 in range(ny1):
            blk = act[:, y1 * lanes:(y1 + 1) * lanes]
            t2[a, y1 + 1] = jnp.concatenate([blk, _shift_right(blk)], axis=0).astype(BF16)

    for tt in range(2):
        for d in range(3):
            for y2 in range(ny2):
                p2[tt, d * 3 * c2:(d + 1) * 3 * c2, y2 * lanes:(y2 + 1) * lanes] = (
                    t2[2 * tt + d, 2 * y2:2 * y2 + 3].reshape(3 * c2, lanes))

    k2 = k2_ref[...]
    for tt in range(2):
        pre = jnp.dot(k2, p2[tt], preferred_element_type=F32)
        sig = _sigmoid(pre)
        if tt == 0:
            lvl_ref[...] = (pre * sig).astype(BF16)
        slope = sig * (1.0 + pre * (1.0 - sig))
        bt[tt] = (cot_ref[tt].astype(F32) * slope).astype(BF16)

    dup = _nt(p2[0], jnp.concatenate([bt[0], bt[0]], axis=0))
    c2n = dup.shape[1] // 2
    qi = c1 // 4
    lane2 = lax.broadcasted_iota(jnp.int32, (qi, 2 * c2n), 1)
    for dh in range(9):
        for w, off in enumerate((3 * c1 // 2, 0, c1 // 2)):
            r0 = dh * c2 + off
            s2_ref[(dh * 3 + w) * qi:(dh * 3 + w + 1) * qi] = jnp.where(
                lane2 < c2n, dup[r0:r0 + qi], dup[r0 + qi:r0 + 2 * qi])

    gacc[...] = jnp.zeros(gacc.shape, F32)
    k2t = k2t_ref[...]
    for tt in range(2):
        if tt == 0:
            gs[...] = jnp.dot(k2t, bt[0], preferred_element_type=F32)
            taps_d = (1, 2)
        else:
            gs[0:3 * c2] = jnp.dot(k2t[0:3 * c2], bt[1], preferred_element_type=F32)
            taps_d = (0,)
        for d in taps_d:
            a = 2 * tt + d
            for h in range(3):
                for y2 in range(ny2):
                    y1 = 2 * y2 + h - 1
                    if y1 < 0:
                        continue
                    r0 = (d * 3 + h) * c2
                    blk = gs[r0:r0 + c2, y2 * lanes:(y2 + 1) * lanes]
                    gacc[a - 1, :, y1 * lanes:(y1 + 1) * lanes] += blk[:c1] + _shift_left(blk[c1:])

    half = c1 // 2
    for a_ in range(2):
        g = gacc[a_]
        pre = pre1[a_]
        sig = _sigmoid(pre)
        slope = sig * (1.0 + pre * (1.0 - sig))
        b1[a_] = (g * slope).astype(BF16)
        gb = g.astype(BF16)
        for y1 in range(ny1):
            blk = gb[:, y1 * lanes:(y1 + 1) * lanes]
            r0 = (a_ * ny1 + y1) * half
            g1s[r0:r0 + half] = jnp.concatenate([blk[:half], blk[half:]], axis=1)
    s1_ref[...] = _nt(p1[1], b1[0]) + _nt(p1[2], b1[1])

    n2 = 2 * lanes
    row = lax.broadcasted_iota(jnp.int32, (n2, n2), 0)
    col = lax.broadcasted_iota(jnp.int32, (n2, n2), 1)
    inter = jnp.where(col == 2 * (row % lanes) + row // lanes, 1.0, 0.0).astype(BF16)
    g1_ref[...] = jnp.dot(g1s[...], inter, preferred_element_type=F32).astype(BF16)


def _level_one_weights(k1):
    kt = jnp.transpose(k1, (0, 2, 3, 1, 4))
    w0, w1, w2 = kt[..., 0], kt[..., 1], kt[..., 2]
    z = jnp.zeros_like(w0)
    p0 = jnp.stack([jnp.stack([w1, w2, z, z], -1), jnp.stack([z, z, z, w0], -1)], 3)
    p1 = jnp.stack([jnp.stack([z, w0, w1, w2], -1), jnp.stack([z, z, z, z], -1)], 3)
    e = jnp.stack([p0, p1], 0)
    return e.reshape(2 * k1.shape[0], -1)


def _level_two_weights(k2):
    kt = jnp.transpose(k2, (0, 2, 3, 4, 1))
    w0, w1, w2 = kt[:, :, :, 0], kt[:, :, :, 1], kt[:, :, :, 2]
    z = jnp.zeros_like(w0)
    e = jnp.stack([jnp.stack([w1, w2], 3), jnp.stack([z, w0], 3)], 3)
    return e.reshape(k2.shape[0], -1)


def per_device(volume, kernel_one, kernel_two, cotangent):
    _, c0, nz, ny, nx = volume.shape
    c1 = kernel_one.shape[0]
    c2 = kernel_two.shape[0]
    assert nz == 4 and cotangent.shape[2] == 1
    q = nx // 4
    below = shifted(volume[:, :, 1:], "gz", 1)
    above = shifted(volume, "gz", -1)
    cot_above = shifted(cotangent, "gz", -1)
    nzi = below.shape[2] + nz + above.shape[2]
    n2 = cotangent.shape[3] * cotangent.shape[4]
    cots = jnp.concatenate([cotangent, cot_above], 2)[0].transpose(1, 0, 2, 3).reshape(2, c2, n2)

    k1m = _level_one_weights(kernel_one)
    k2m = _level_two_weights(kernel_two)
    k2t = k2m.T

    ny1, ny2 = ny // 2, ny // 4
    n_act = 5
    vm = pltpu.VMEM
    lvl, g1, s1, s2 = pl.pallas_call(
        _kernel,
        out_shape=(
            jax.ShapeDtypeStruct((c2, n2), BF16),
            jax.ShapeDtypeStruct((2 * ny1 * c1, 2 * q), BF16),
            jax.ShapeDtypeStruct((k1m.shape[1], k1m.shape[0]), F32),
            jax.ShapeDtypeStruct((27 * c1 // 2, 2 * c2), F32),
        ),
        scratch_shapes=[
            vm((nzi, ny + 1, 8 * c0, q), BF16),
            vm((n_act, k1m.shape[1], ny1 * q), BF16),
            vm((n_act, ny1 + 1, 4 * c1, q), BF16),
            vm((2, 2 * c1, ny1 * q), F32),
            vm((2, k2m.shape[1], n2), BF16),
            vm((2, c2, n2), BF16),
            vm((k2m.shape[1], n2), F32),
            vm((2, 2 * c1, ny1 * q), F32),
            vm((2, 2 * c1, ny1 * q), BF16),
            vm((2 * ny1 * c1, 2 * q), BF16),
        ],
        cost_estimate=pl.CostEstimate(flops=60_000_000, transcendentals=200_000, bytes_accessed=3_000_000),
    )(below, volume, above, k1m, k2m, k2t, cots)

    level_two = lvl.reshape(1, c2, 1, ny2, n2 // ny2)
    grad_one = g1.reshape(2, ny1, c1, 2 * q).transpose(2, 0, 1, 3)[None]

    s1r = s1.reshape(3, 3, 2, c0, 4, 2, c1)
    gk1 = jnp.stack([
        s1r[:, :, 1, :, 3, 0] + s1r[:, :, 0, :, 1, 1],
        s1r[:, :, 0, :, 0, 0] + s1r[:, :, 0, :, 2, 1],
        s1r[:, :, 0, :, 1, 0] + s1r[:, :, 0, :, 3, 1],
    ], 2)
    rows1 = gk1.size // s2.shape[1]
    total = _all_sum(jnp.concatenate([gk1.reshape(rows1, s2.shape[1]), s2], 0), ("gz", "sa"))
    samples = volume.shape[0] * lax.axis_size("sa")
    cells_one = samples * (nz // 2) * lax.axis_size("gz") * ny1 * (nx // 2)
    cells_two = samples * cotangent.shape[2] * lax.axis_size("gz") * cotangent.shape[3] * cotangent.shape[4]
    t1 = total[:rows1] / math.sqrt(float(cells_one))
    t2 = total[rows1:] / math.sqrt(float(cells_two))
    grad_kernel_one = t1.reshape(3, 3, 3, c0, c1).transpose(4, 3, 0, 1, 2)
    t2 = t2.reshape(27, c1 // 2, 2, c2).transpose(0, 2, 1, 3).reshape(3, 3, 3, c1, c2)
    grad_kernel_two = t2.transpose(4, 3, 0, 1, 2)
    return (level_two, grad_one, grad_kernel_one, grad_kernel_two)


def solution(mesh):
    placed = (P("sa", None, "gz", None, None), P(), P(), P("sa", None, "gz", None, None))
    return jax.shard_map(
        per_device,
        mesh=mesh,
        in_specs=placed,
        out_specs=(P("sa", None, "gz", None, None), P("sa", None, "gz", None, None), P(), P()),
        check_vma=False,
    )
```

```python
import math

import jax
import jax.numpy as jnp
from jax import lax
from jax.experimental import pallas as pl
from jax.experimental.pallas import tpu as pltpu
from jax.sharding import PartitionSpec as P

F32 = jnp.float32
BF16 = jnp.bfloat16


def shifted(block, axis, distance):
    devices = range(lax.axis_size(axis))
    route = [(i - distance, i) for i in devices if i - distance in devices]
    return lax.ppermute(block, axis, route)


def _all_sum(x, axes):
    steps = []
    for axis in axes:
        n = lax.axis_size(axis)
        assert n & (n - 1) == 0
        k = 1
        while k < n:
            steps.append((axis, n, k))
            k *= 2
    axis0, n0, k0 = steps[0]
    rows = x.shape[0]
    half = -(-rows // 16) * 8
    x = jnp.pad(x, ((0, 2 * half - rows), (0, 0)))
    low = (lax.axis_index(axis0) & k0) == 0
    lo, hi = x[:half], x[half:]
    pair = [(i, i ^ k0) for i in range(n0)]
    part = jnp.where(low, lo, hi) + lax.ppermute(jnp.where(low, hi, lo), axis0, pair)
    for axis, n, k in steps[1:]:
        part = part + lax.ppermute(part, axis, [(i, i ^ k) for i in range(n)])
    other = lax.ppermute(part, axis0, pair)
    return jnp.where(low, jnp.concatenate([part, other], 0), jnp.concatenate([other, part], 0))[:rows]


def _sigmoid(v):
    return 1.0 / (1.0 + jnp.exp(-v))


def _shift_right(x):
    lane = lax.broadcasted_iota(jnp.int32, x.shape, x.ndim - 1)
    return jnp.where(lane == 0, 0.0, pltpu.roll(x, 1, x.ndim - 1))


def _shift_left(x):
    n = x.shape[-1]
    lane = lax.broadcasted_iota(jnp.int32, x.shape, x.ndim - 1)
    return jnp.where(lane == n - 1, 0.0, pltpu.roll(x, n - 1, x.ndim - 1))


def _nt(a, b):
    return lax.dot_general(a, b, (((1,), (1,)), ((), ())), preferred_element_type=F32)


def _relayout_volume(pieces, tp, c0, ny, nx):
    lanes = nx // 4
    rows0 = 4 * c0
    xs = lax.broadcasted_iota(jnp.int32, (nx, nx), 0)
    cs = lax.broadcasted_iota(jnp.int32, (nx, nx), 1)
    sel_x = jnp.where(xs == 4 * (cs % lanes) + cs // lanes, 1.0, 0.0).astype(BF16)
    nq = 2 * rows0 * ny
    orow = lax.broadcasted_iota(jnp.int32, (nq, nq), 0)
    icol = lax.broadcasted_iota(jnp.int32, (nq, nq), 1)
    y_, s_ = orow // (2 * rows0), (orow // rows0) % 2
    i_, r_ = (orow // 4) % c0, orow % 4
    perm = jnp.where(icol == ((s_ * 4 + r_) * c0 + i_) * ny + y_, 1.0, 0.0).astype(BF16)
    tp[:, 0] = jnp.zeros((tp.shape[0], 2 * rows0, lanes), BF16)
    for zi, (ref, z) in enumerate(pieces):
        zmat = ref[0, :, z].reshape(c0 * ny, nx)
        ymat = jnp.dot(zmat, sel_x, preferred_element_type=F32)
        blocks = [ymat[:, r * lanes:(r + 1) * lanes] for r in range(4)]
        q = jnp.concatenate(blocks + [_shift_right(b) for b in blocks], axis=0).astype(BF16)
        t = jnp.dot(perm, q, preferred_element_type=F32).astype(BF16)
        tp[zi, 1:] = t.reshape(ny, 2 * rows0, lanes)


def _add_taps(gacc, slot, gs, row_base, ny2, lanes, c1):
    c2 = 2 * c1
    for h in range(3):
        for y2 in range(ny2):
            y1 = 2 * y2 + h - 1
            if y1 < 0:
                continue
            r0 = row_base + h * c2
            blk = gs[r0:r0 + c2, y2 * lanes:(y2 + 1) * lanes]
            gacc[slot, :, y1 * lanes:(y1 + 1) * lanes] += blk[:c1] + _shift_left(blk[c1:])


def _interleave(g, g1_ref, ny1, lanes):
    half = g.shape[0] // 2
    gb = g.astype(BF16)
    rows = [jnp.concatenate([gb[:half, y1 * lanes:(y1 + 1) * lanes], gb[half:, y1 * lanes:(y1 + 1) * lanes]], axis=1)
            for y1 in range(ny1)]
    n2 = 2 * lanes
    row = lax.broadcasted_iota(jnp.int32, (n2, n2), 0)
    col = lax.broadcasted_iota(jnp.int32, (n2, n2), 1)
    inter = jnp.where(col == 2 * (row % lanes) + row // lanes, 1.0, 0.0).astype(BF16)
    g1_ref[...] = jnp.dot(jnp.concatenate(rows, axis=0), inter, preferred_element_type=F32).astype(BF16)


def _slope(pre):
    sig = _sigmoid(pre)
    return sig * (1.0 + pre * (1.0 - sig))


def _kernel_a(vb_ref, vo_ref, k1_ref, k2_ref, k2t_ref, cot_ref,
              lvl_ref, bt_ref, s2_ref, s1_ref, g1_ref, gp_ref, sl_ref, p1o_ref,
              tp, p1, t2, p2, gs, gacc):
    c0, ny, nx = vo_ref.shape[1], vo_ref.shape[3], vo_ref.shape[4]
    lanes = nx // 4
    n_act = p1.shape[0]
    ny1 = ny // 2
    ny2 = ny1 // 2
    c2 = t2.shape[2]
    c1 = c2 // 2
    rows0 = 4 * c0

    pieces = [(vb_ref, z) for z in range(vb_ref.shape[2])] + [(vo_ref, z) for z in range(vo_ref.shape[2])]
    _relayout_volume(pieces, tp, c0, ny, nx)

    for a in range(n_act):
        for d in range(3):
            for y1 in range(ny1):
                p1[a, d * 3 * 2 * rows0:(d + 1) * 3 * 2 * rows0, y1 * lanes:(y1 + 1) * lanes] = (
                    tp[2 * a + d, 2 * y1:2 * y1 + 3].reshape(3 * 2 * rows0, lanes))

    k1 = k1_ref[...]
    t2[:, 0] = jnp.zeros((n_act, c2, lanes), BF16)
    slope1 = None
    for a in range(n_act):
        pre = jnp.dot(k1, p1[a], preferred_element_type=F32)
        if a == 1:
            slope1 = _slope(pre)
        if a == 2:
            sl_ref[...] = _slope(pre)
        act = pre * _sigmoid(pre)
        for y1 in range(ny1):
            blk = act[:, y1 * lanes:(y1 + 1) * lanes]
            t2[a, y1 + 1] = jnp.concatenate([blk, _shift_right(blk)], axis=0).astype(BF16)

    for d in range(3):
        for y2 in range(ny2):
            p2[d * 3 * c2:(d + 1) * 3 * c2, y2 * lanes:(y2 + 1) * lanes] = (
                t2[d, 2 * y2:2 * y2 + 3].reshape(3 * c2, lanes))

    pre = jnp.dot(k2_ref[...], p2[...], preferred_element_type=F32)
    sig = _sigmoid(pre)
    lvl_ref[...] = (pre * sig).astype(BF16)
    bt0 = (cot_ref[...].astype(F32) * (sig * (1.0 + pre * (1.0 - sig)))).astype(BF16)
    bt_ref[...] = bt0

    dup = _nt(p2[...], jnp.concatenate([bt0, bt0], axis=0))
    c2n = dup.shape[1] // 2
    qi = c1 // 4
    lane2 = lax.broadcasted_iota(jnp.int32, (qi, 2 * c2n), 1)
    for dh in range(9):
        for w, off in enumerate((3 * c1 // 2, 0, c1 // 2)):
            r0 = dh * c2 + off
            s2_ref[(dh * 3 + w) * qi:(dh * 3 + w + 1) * qi] = jnp.where(
                lane2 < c2n, dup[r0:r0 + qi], dup[r0 + qi:r0 + 2 * qi])

    gacc[...] = jnp.zeros(gacc.shape, F32)
    gs[...] = jnp.dot(k2t_ref[3 * c2:], bt0, preferred_element_type=F32)
    _add_taps(gacc, 0, gs, 0, ny2, lanes, c1)
    _add_taps(gacc, 1, gs, 3 * c2, ny2, lanes, c1)

    g = gacc[0]
    b1 = (g * slope1).astype(BF16)
    s1_ref[...] = _nt(p1[1], b1)
    _interleave(g, g1_ref, ny1, lanes)
    gp_ref[...] = gacc[1]
    p1o_ref[...] = p1[2]


def _kernel_b(bta_ref, k2t_ref, gp_ref, sl_ref, p1o_ref, s1_ref, g1_ref, gs, gacc):
    c1 = gp_ref.shape[0]
    lanes = bta_ref.shape[1] // 4
    ny2 = 4
    ny1 = gp_ref.shape[1] // lanes
    gacc[0] = gp_ref[...]
    gs[...] = jnp.dot(k2t_ref[:3 * 2 * c1], bta_ref[...], preferred_element_type=F32)
    _add_taps(gacc, 0, gs, 0, ny2, lanes, c1)
    g = gacc[0]
    b1 = (g * sl_ref[...]).astype(BF16)
    s1_ref[...] = _nt(p1o_ref[...], b1)
    _interleave(g, g1_ref, ny1, lanes)


def _level_one_weights(k1):
    kt = jnp.transpose(k1, (0, 2, 3, 1, 4))
    w0, w1, w2 = kt[..., 0], kt[..., 1], kt[..., 2]
    z = jnp.zeros_like(w0)
    p0 = jnp.stack([jnp.stack([w1, w2, z, z], -1), jnp.stack([z, z, z, w0], -1)], 3)
    p1 = jnp.stack([jnp.stack([z, w0, w1, w2], -1), jnp.stack([z, z, z, z], -1)], 3)
    e = jnp.stack([p0, p1], 0)
    return e.reshape(2 * k1.shape[0], -1)


def _level_two_weights(k2):
    kt = jnp.transpose(k2, (0, 2, 3, 4, 1))
    w0, w1, w2 = kt[:, :, :, 0], kt[:, :, :, 1], kt[:, :, :, 2]
    z = jnp.zeros_like(w0)
    e = jnp.stack([jnp.stack([w1, w2], 3), jnp.stack([z, w0], 3)], 3)
    return e.reshape(k2.shape[0], -1)


def per_device(volume, kernel_one, kernel_two, cotangent):
    _, c0, nz, ny, nx = volume.shape
    c1 = kernel_one.shape[0]
    c2 = kernel_two.shape[0]
    assert nz == 4 and cotangent.shape[2] == 1
    q = nx // 4
    below = shifted(volume[:, :, 1:], "gz", 1)
    n2 = cotangent.shape[3] * cotangent.shape[4]
    cot = cotangent[0, :, 0].reshape(c2, n2)

    k1m = _level_one_weights(kernel_one)
    k2m = _level_two_weights(kernel_two)
    k2t = k2m.T

    ny1, ny2 = ny // 2, ny // 4
    nzi = below.shape[2] + nz
    vm = pltpu.VMEM
    kk = k1m.shape[1]
    lvl, bt0, s2, s1a, g1a, gp, sl, p1o = pl.pallas_call(
        _kernel_a,
        out_shape=(
            jax.ShapeDtypeStruct((c2, n2), BF16),
            jax.ShapeDtypeStruct((c2, n2), BF16),
            jax.ShapeDtypeStruct((27 * c1 // 2, 2 * c2), F32),
            jax.ShapeDtypeStruct((kk, 2 * c1), F32),
            jax.ShapeDtypeStruct((ny1 * c1, 2 * q), BF16),
            jax.ShapeDtypeStruct((2 * c1, ny1 * q), F32),
            jax.ShapeDtypeStruct((2 * c1, ny1 * q), F32),
            jax.ShapeDtypeStruct((kk, ny1 * q), BF16),
        ),
        scratch_shapes=[
            vm((nzi, ny + 1, 8 * c0, q), BF16),
            vm((3, kk, ny1 * q), BF16),
            vm((3, ny1 + 1, 4 * c1, q), BF16),
            vm((k2m.shape[1], n2), BF16),
            vm((2 * 3 * 4 * c1, n2), F32),
            vm((2, 2 * c1, ny1 * q), F32),
        ],
        cost_estimate=pl.CostEstimate(flops=40_000_000, transcendentals=150_000, bytes_accessed=3_000_000),
    )(below, volume, k1m, k2m, k2t, cot)

    s1b, g1b = pl.pallas_call(
        _kernel_b,
        out_shape=(
            jax.ShapeDtypeStruct((kk, 2 * c1), F32),
            jax.ShapeDtypeStruct((ny1 * c1, 2 * q), BF16),
        ),
        scratch_shapes=[
            vm((3 * 4 * c1, n2), F32),
            vm((1, 2 * c1, ny1 * q), F32),
        ],
        cost_estimate=pl.CostEstimate(flops=15_000_000, transcendentals=0, bytes_accessed=2_500_000),
    )(shifted(bt0, "gz", -1), k2t, gp, sl, p1o)

    samples = volume.shape[0] * lax.axis_size("sa")
    cells_one = samples * (nz // 2) * lax.axis_size("gz") * ny1 * (nx // 2)
    cells_two = samples * cotangent.shape[2] * lax.axis_size("gz") * cotangent.shape[3] * cotangent.shape[4]

    t2 = _all_sum(s2, ("gz", "sa")) / math.sqrt(float(cells_two))
    t2 = t2.reshape(27, c1 // 2, 2, c2).transpose(0, 2, 1, 3).reshape(3, 3, 3, c1, c2)
    grad_kernel_two = t2.transpose(4, 3, 0, 1, 2)

    s1 = s1a + s1b
    s1r = s1.reshape(3, 3, 2, c0, 4, 2, c1)
    gk1 = jnp.stack([
        s1r[:, :, 1, :, 3, 0] + s1r[:, :, 0, :, 1, 1],
        s1r[:, :, 0, :, 0, 0] + s1r[:, :, 0, :, 2, 1],
        s1r[:, :, 0, :, 1, 0] + s1r[:, :, 0, :, 3, 1],
    ], 2)
    t1 = _all_sum(gk1.reshape(-1, 2 * c2), ("gz", "sa")) / math.sqrt(float(cells_one))
    grad_kernel_one = t1.reshape(3, 3, 3, c0, c1).transpose(4, 3, 0, 1, 2)

    level_two = lvl.reshape(1, c2, 1, ny2, n2 // ny2)
    g1 = jnp.concatenate([g1a, g1b], 0)
    grad_one = g1.reshape(2, ny1, c1, 2 * q).transpose(2, 0, 1, 3)[None]
    return (level_two, grad_one, grad_kernel_one, grad_kernel_two)


def solution(mesh):
    placed = (P("sa", None, "gz", None, None), P(), P(), P("sa", None, "gz", None, None))
    return jax.shard_map(
        per_device,
        mesh=mesh,
        in_specs=placed,
        out_specs=(P("sa", None, "gz", None, None), P("sa", None, "gz", None, None), P(), P()),
        check_vma=False,
    )
```

```python
import math

import jax
import jax.numpy as jnp
from jax import lax
from jax.experimental import pallas as pl
from jax.experimental.pallas import tpu as pltpu
from jax.sharding import PartitionSpec as P

F32 = jnp.float32
BF16 = jnp.bfloat16


def shifted(block, axis, distance):
    devices = range(lax.axis_size(axis))
    route = [(i - distance, i) for i in devices if i - distance in devices]
    return lax.ppermute(block, axis, route)


def _all_sum(x, axes):
    steps = []
    for axis in axes:
        n = lax.axis_size(axis)
        assert n & (n - 1) == 0
        k = 1
        while k < n:
            steps.append((axis, n, k))
            k *= 2
    axis0, n0, k0 = steps[0]
    rows = x.shape[0]
    half = -(-rows // 16) * 8
    x = jnp.pad(x, ((0, 2 * half - rows), (0, 0)))
    low = (lax.axis_index(axis0) & k0) == 0
    lo, hi = x[:half], x[half:]
    pair = [(i, i ^ k0) for i in range(n0)]
    part = jnp.where(low, lo, hi) + lax.ppermute(jnp.where(low, hi, lo), axis0, pair)
    for axis, n, k in steps[1:]:
        part = part + lax.ppermute(part, axis, [(i, i ^ k) for i in range(n)])
    other = lax.ppermute(part, axis0, pair)
    return jnp.where(low, jnp.concatenate([part, other], 0), jnp.concatenate([other, part], 0))[:rows]


def _sigmoid(v):
    return 1.0 / (1.0 + jnp.exp(-v))


def _shift_right(x):
    lane = lax.broadcasted_iota(jnp.int32, x.shape, x.ndim - 1)
    return jnp.where(lane == 0, 0.0, pltpu.roll(x, 1, x.ndim - 1))


def _shift_left(x):
    n = x.shape[-1]
    lane = lax.broadcasted_iota(jnp.int32, x.shape, x.ndim - 1)
    return jnp.where(lane == n - 1, 0.0, pltpu.roll(x, n - 1, x.ndim - 1))


def _nt(a, b):
    return lax.dot_general(a, b, (((1,), (1,)), ((), ())), preferred_element_type=F32)


def _relayout_volume(pieces, tp, c0, ny, nx):
    lanes = nx // 4
    rows0 = 4 * c0
    xs = lax.broadcasted_iota(jnp.int32, (nx, nx), 0)
    cs = lax.broadcasted_iota(jnp.int32, (nx, nx), 1)
    sel_x = jnp.where(xs == 4 * (cs % lanes) + cs // lanes, 1.0, 0.0).astype(BF16)
    nq = 2 * rows0 * ny
    orow = lax.broadcasted_iota(jnp.int32, (nq, nq), 0)
    icol = lax.broadcasted_iota(jnp.int32, (nq, nq), 1)
    y_, s_ = orow // (2 * rows0), (orow // rows0) % 2
    i_, r_ = (orow // 4) % c0, orow % 4
    perm = jnp.where(icol == ((s_ * 4 + r_) * c0 + i_) * ny + y_, 1.0, 0.0).astype(BF16)
    tp[:, 0] = jnp.zeros((tp.shape[0], 2 * rows0, lanes), BF16)
    for zi, (ref, z) in enumerate(pieces):
        zmat = ref[0, :, z].reshape(c0 * ny, nx)
        ymat = jnp.dot(zmat, sel_x, preferred_element_type=F32)
        blocks = [ymat[:, r * lanes:(r + 1) * lanes] for r in range(4)]
        q = jnp.concatenate(blocks + [_shift_right(b) for b in blocks], axis=0).astype(BF16)
        t = jnp.dot(perm, q, preferred_element_type=F32).astype(BF16)
        tp[zi, 1:] = t.reshape(ny, 2 * rows0, lanes)


def _add_taps(gacc, slot, gs, row_base, ny2, lanes, c1):
    c2 = 2 * c1
    for h in range(3):
        for y2 in range(ny2):
            y1 = 2 * y2 + h - 1
            if y1 < 0:
                continue
            r0 = row_base + h * c2
            blk = gs[r0:r0 + c2, y2 * lanes:(y2 + 1) * lanes]
            gacc[slot, :, y1 * lanes:(y1 + 1) * lanes] += blk[:c1] + _shift_left(blk[c1:])


def _interleave(g, g1_ref, ny1, lanes):
    half = g.shape[0] // 2
    gb = g.astype(BF16)
    rows = [jnp.concatenate([gb[:half, y1 * lanes:(y1 + 1) * lanes], gb[half:, y1 * lanes:(y1 + 1) * lanes]], axis=1)
            for y1 in range(ny1)]
    n2 = 2 * lanes
    row = lax.broadcasted_iota(jnp.int32, (n2, n2), 0)
    col = lax.broadcasted_iota(jnp.int32, (n2, n2), 1)
    inter = jnp.where(col == 2 * (row % lanes) + row // lanes, 1.0, 0.0).astype(BF16)
    g1_ref[...] = jnp.dot(jnp.concatenate(rows, axis=0), inter, preferred_element_type=F32).astype(BF16)


def _slope(pre):
    sig = _sigmoid(pre)
    return sig * (1.0 + pre * (1.0 - sig))


def _kernel_a(vb_ref, vo_ref, k1_ref, k2_ref, k2t_ref, cot_ref,
              lvl_ref, bt_ref, s2_ref, s1_ref, g1_ref, gp_ref, sl_ref, p1o_ref,
              tp, p1, t2, p2, gs, gacc):
    c0, ny, nx = vo_ref.shape[1], vo_ref.shape[3], vo_ref.shape[4]
    lanes = nx // 4
    n_act = p1.shape[0]
    ny1 = ny // 2
    ny2 = ny1 // 2
    c2 = t2.shape[2]
    c1 = c2 // 2
    rows0 = 4 * c0

    pieces = [(vb_ref, z) for z in range(vb_ref.shape[2])] + [(vo_ref, z) for z in range(vo_ref.shape[2])]
    _relayout_volume(pieces, tp, c0, ny, nx)

    for a in range(n_act):
        for d in range(3):
            for y1 in range(ny1):
                p1[a, d * 3 * 2 * rows0:(d + 1) * 3 * 2 * rows0, y1 * lanes:(y1 + 1) * lanes] = (
                    tp[2 * a + d, 2 * y1:2 * y1 + 3].reshape(3 * 2 * rows0, lanes))

    k1 = k1_ref[...]
    t2[:, 0] = jnp.zeros((n_act, c2, lanes), BF16)
    slope1 = None
    for a in range(n_act):
        pre = jnp.dot(k1, p1[a], preferred_element_type=F32)
        if a == 1:
            slope1 = _slope(pre)
        if a == 2:
            sl_ref[...] = _slope(pre)
        act = pre * _sigmoid(pre)
        for y1 in range(ny1):
            blk = act[:, y1 * lanes:(y1 + 1) * lanes]
            t2[a, y1 + 1] = jnp.concatenate([blk, _shift_right(blk)], axis=0).astype(BF16)

    for d in range(3):
        for y2 in range(ny2):
            p2[d * 3 * c2:(d + 1) * 3 * c2, y2 * lanes:(y2 + 1) * lanes] = (
                t2[d, 2 * y2:2 * y2 + 3].reshape(3 * c2, lanes))

    pre = jnp.dot(k2_ref[...], p2[...], preferred_element_type=F32)
    sig = _sigmoid(pre)
    lvl_ref[...] = (pre * sig).astype(BF16)
    bt0 = (cot_ref[...].astype(F32) * (sig * (1.0 + pre * (1.0 - sig)))).astype(BF16)
    bt_ref[...] = bt0

    dup = _nt(p2[...], jnp.concatenate([bt0, bt0], axis=0))
    c2n = dup.shape[1] // 2
    qi = c1 // 4
    lane2 = lax.broadcasted_iota(jnp.int32, (qi, 2 * c2n), 1)
    for dh in range(9):
        for w, off in enumerate((3 * c1 // 2, 0, c1 // 2)):
            r0 = dh * c2 + off
            s2_ref[(dh * 3 + w) * qi:(dh * 3 + w + 1) * qi] = jnp.where(
                lane2 < c2n, dup[r0:r0 + qi], dup[r0 + qi:r0 + 2 * qi])

    gacc[...] = jnp.zeros(gacc.shape, F32)
    gs[...] = jnp.dot(k2t_ref[3 * c2:], bt0, preferred_element_type=F32)
    _add_taps(gacc, 0, gs, 0, ny2, lanes, c1)
    _add_taps(gacc, 1, gs, 3 * c2, ny2, lanes, c1)

    g = gacc[0]
    b1 = (g * slope1).astype(BF16)
    s1_ref[...] = _nt(p1[1], b1)
    _interleave(g, g1_ref, ny1, lanes)
    gp_ref[...] = gacc[1]
    p1o_ref[...] = p1[2]


def _kernel_b(bta_ref, k2t_ref, gp_ref, sl_ref, p1o_ref, s1a_ref, s1_ref, g1_ref, gs, gacc):
    c1 = gp_ref.shape[0]
    lanes = bta_ref.shape[1] // 4
    ny2 = 4
    ny1 = gp_ref.shape[1] // lanes
    gacc[0] = gp_ref[...]
    gs[...] = jnp.dot(k2t_ref[:3 * 2 * c1], bta_ref[...], preferred_element_type=F32)
    _add_taps(gacc, 0, gs, 0, ny2, lanes, c1)
    g = gacc[0]
    b1 = (g * sl_ref[...]).astype(BF16)
    s1_ref[...] = s1a_ref[...] + _nt(p1o_ref[...], b1)
    _interleave(g, g1_ref, ny1, lanes)


def _level_one_weights(k1):
    kt = jnp.transpose(k1, (0, 2, 3, 1, 4))
    w0, w1, w2 = kt[..., 0], kt[..., 1], kt[..., 2]
    z = jnp.zeros_like(w0)
    p0 = jnp.stack([jnp.stack([w1, w2, z, z], -1), jnp.stack([z, z, z, w0], -1)], 3)
    p1 = jnp.stack([jnp.stack([z, w0, w1, w2], -1), jnp.stack([z, z, z, z], -1)], 3)
    e = jnp.stack([p0, p1], 0)
    return e.reshape(2 * k1.shape[0], -1)


def _level_two_weights(k2):
    kt = jnp.transpose(k2, (0, 2, 3, 4, 1))
    w0, w1, w2 = kt[:, :, :, 0], kt[:, :, :, 1], kt[:, :, :, 2]
    z = jnp.zeros_like(w0)
    e = jnp.stack([jnp.stack([w1, w2], 3), jnp.stack([z, w0], 3)], 3)
    return e.reshape(k2.shape[0], -1)


def per_device(volume, kernel_one, kernel_two, cotangent):
    _, c0, nz, ny, nx = volume.shape
    c1 = kernel_one.shape[0]
    c2 = kernel_two.shape[0]
    assert nz == 4 and cotangent.shape[2] == 1
    q = nx // 4
    below = shifted(volume[:, :, 1:], "gz", 1)
    n2 = cotangent.shape[3] * cotangent.shape[4]
    cot = cotangent[0, :, 0].reshape(c2, n2)

    k1m = _level_one_weights(kernel_one)
    k2m = _level_two_weights(kernel_two)
    k2t = k2m.T

    ny1, ny2 = ny // 2, ny // 4
    nzi = below.shape[2] + nz
    vm = pltpu.VMEM
    kk = k1m.shape[1]
    lvl, bt0, s2, s1a, g1a, gp, sl, p1o = pl.pallas_call(
        _kernel_a,
        out_shape=(
            jax.ShapeDtypeStruct((c2, n2), BF16),
            jax.ShapeDtypeStruct((c2, n2), BF16),
            jax.ShapeDtypeStruct((27 * c1 // 2, 2 * c2), F32),
            jax.ShapeDtypeStruct((kk, 2 * c1), F32),
            jax.ShapeDtypeStruct((ny1 * c1, 2 * q), BF16),
            jax.ShapeDtypeStruct((2 * c1, ny1 * q), F32),
            jax.ShapeDtypeStruct((2 * c1, ny1 * q), F32),
            jax.ShapeDtypeStruct((kk, ny1 * q), BF16),
        ),
        scratch_shapes=[
            vm((nzi, ny + 1, 8 * c0, q), BF16),
            vm((3, kk, ny1 * q), BF16),
            vm((3, ny1 + 1, 4 * c1, q), BF16),
            vm((k2m.shape[1], n2), BF16),
            vm((2 * 3 * 4 * c1, n2), F32),
            vm((2, 2 * c1, ny1 * q), F32),
        ],
        cost_estimate=pl.CostEstimate(flops=40_000_000, transcendentals=150_000, bytes_accessed=3_000_000),
    )(below, volume, k1m, k2m, k2t, cot)

    s1, g1b = pl.pallas_call(
        _kernel_b,
        out_shape=(
            jax.ShapeDtypeStruct((kk, 2 * c1), F32),
            jax.ShapeDtypeStruct((ny1 * c1, 2 * q), BF16),
        ),
        scratch_shapes=[
            vm((3 * 4 * c1, n2), F32),
            vm((1, 2 * c1, ny1 * q), F32),
        ],
        cost_estimate=pl.CostEstimate(flops=15_000_000, transcendentals=0, bytes_accessed=2_500_000),
    )(shifted(bt0, "gz", -1), k2t, gp, sl, p1o, s1a)

    samples = volume.shape[0] * lax.axis_size("sa")
    cells_one = samples * (nz // 2) * lax.axis_size("gz") * ny1 * (nx // 2)
    cells_two = samples * cotangent.shape[2] * lax.axis_size("gz") * cotangent.shape[3] * cotangent.shape[4]

    s1r = s1.reshape(3, 3, 2, c0, 4, 2, c1)
    gk1 = jnp.stack([
        s1r[:, :, 1, :, 3, 0] + s1r[:, :, 0, :, 1, 1],
        s1r[:, :, 0, :, 0, 0] + s1r[:, :, 0, :, 2, 1],
        s1r[:, :, 0, :, 1, 0] + s1r[:, :, 0, :, 3, 1],
    ], 2)
    rows1 = gk1.size // s2.shape[1]
    total = _all_sum(jnp.concatenate([gk1.reshape(rows1, s2.shape[1]), s2], 0), ("gz", "sa"))
    t1 = total[:rows1] / math.sqrt(float(cells_one))
    t2 = total[rows1:] / math.sqrt(float(cells_two))
    grad_kernel_one = t1.reshape(3, 3, 3, c0, c1).transpose(4, 3, 0, 1, 2)
    t2 = t2.reshape(27, c1 // 2, 2, c2).transpose(0, 2, 1, 3).reshape(3, 3, 3, c1, c2)
    grad_kernel_two = t2.transpose(4, 3, 0, 1, 2)

    level_two = lvl.reshape(1, c2, 1, ny2, n2 // ny2)
    g1 = jnp.concatenate([g1a, g1b], 0)
    grad_one = g1.reshape(2, ny1, c1, 2 * q).transpose(2, 0, 1, 3)[None]
    return (level_two, grad_one, grad_kernel_one, grad_kernel_two)


def solution(mesh):
    placed = (P("sa", None, "gz", None, None), P(), P(), P("sa", None, "gz", None, None))
    return jax.shard_map(
        per_device,
        mesh=mesh,
        in_specs=placed,
        out_specs=(P("sa", None, "gz", None, None), P("sa", None, "gz", None, None), P(), P()),
        check_vma=False,
    )
```

```python
import math

import jax
import jax.numpy as jnp
from jax import lax
from jax.experimental import pallas as pl
from jax.experimental.pallas import tpu as pltpu
from jax.sharding import PartitionSpec as P

F32 = jnp.float32
BF16 = jnp.bfloat16


def shifted(block, axis, distance):
    devices = range(lax.axis_size(axis))
    route = [(i - distance, i) for i in devices if i - distance in devices]
    return lax.ppermute(block, axis, route)


def _all_sum(x, y, axes):
    steps = []
    for axis in axes:
        n = lax.axis_size(axis)
        assert n & (n - 1) == 0
        k = 1
        while k < n:
            steps.append((axis, n, k))
            k *= 2
    axis0, n0, k0 = steps[0]
    rows = x.shape[0]
    half = -(-rows // 16) * 8
    x = jnp.pad(x, ((0, 2 * half - rows), (0, 0)))
    low = (lax.axis_index(axis0) & k0) == 0
    lo, hi = x[:half], x[half:]
    pair = [(i, i ^ k0) for i in range(n0)]
    part = jnp.where(low, lo, hi) + lax.ppermute(jnp.where(low, hi, lo), axis0, pair)
    ry = y.shape[0]
    cur = jnp.concatenate([part, jnp.pad(y, ((0, -ry % 8), (0, 0)))], 0)
    for axis, n, k in steps[1:]:
        cur = cur + lax.ppermute(cur, axis, [(i, i ^ k) for i in range(n)])
    recv = lax.ppermute(cur, axis0, pair)
    part, other = cur[:half], recv[:half]
    xs = jnp.where(low, jnp.concatenate([part, other], 0), jnp.concatenate([other, part], 0))[:rows]
    return xs, cur[half:half + ry] + recv[half:half + ry]


def _sigmoid(v):
    return 1.0 / (1.0 + jnp.exp(-v))


def _shift_right(x):
    lane = lax.broadcasted_iota(jnp.int32, x.shape, x.ndim - 1)
    return jnp.where(lane == 0, 0.0, pltpu.roll(x, 1, x.ndim - 1))


def _shift_left(x):
    n = x.shape[-1]
    lane = lax.broadcasted_iota(jnp.int32, x.shape, x.ndim - 1)
    return jnp.where(lane == n - 1, 0.0, pltpu.roll(x, n - 1, x.ndim - 1))


def _nt(a, b):
    return lax.dot_general(a, b, (((1,), (1,)), ((), ())), preferred_element_type=F32)


def _relayout_volume(pieces, tp, c0, ny, nx):
    lanes = nx // 4
    rows0 = 4 * c0
    xs = lax.broadcasted_iota(jnp.int32, (nx, nx), 0)
    cs = lax.broadcasted_iota(jnp.int32, (nx, nx), 1)
    sel_x = jnp.where(xs == 4 * (cs % lanes) + cs // lanes, 1.0, 0.0).astype(BF16)
    nq = 2 * rows0 * ny
    orow = lax.broadcasted_iota(jnp.int32, (nq, nq), 0)
    icol = lax.broadcasted_iota(jnp.int32, (nq, nq), 1)
    y_, s_ = orow // (2 * rows0), (orow // rows0) % 2
    i_, r_ = (orow // 4) % c0, orow % 4
    perm = jnp.where(icol == ((s_ * 4 + r_) * c0 + i_) * ny + y_, 1.0, 0.0).astype(BF16)
    tp[:, 0] = jnp.zeros((tp.shape[0], 2 * rows0, lanes), BF16)
    for zi, (ref, z) in enumerate(pieces):
        zmat = ref[0, :, z].reshape(c0 * ny, nx)
        ymat = jnp.dot(zmat, sel_x, preferred_element_type=F32)
        blocks = [ymat[:, r * lanes:(r + 1) * lanes] for r in range(4)]
        q = jnp.concatenate(blocks + [_shift_right(b) for b in blocks], axis=0).astype(BF16)
        t = jnp.dot(perm, q, preferred_element_type=F32).astype(BF16)
        tp[zi, 1:] = t.reshape(ny, 2 * rows0, lanes)


def _add_taps(gacc, slot, gs, row_base, ny2, lanes, c1):
    c2 = 2 * c1
    for h in range(3):
        for y2 in range(ny2):
            y1 = 2 * y2 + h - 1
            if y1 < 0:
                continue
            r0 = row_base + h * c2
            blk = gs[r0:r0 + c2, y2 * lanes:(y2 + 1) * lanes]
            gacc[slot, :, y1 * lanes:(y1 + 1) * lanes] += blk[:c1] + _shift_left(blk[c1:])


def _interleave(g, g1_ref, ny1, lanes):
    half = g.shape[0] // 2
    gb = g.astype(BF16)
    rows = [jnp.concatenate([gb[:half, y1 * lanes:(y1 + 1) * lanes], gb[half:, y1 * lanes:(y1 + 1) * lanes]], axis=1)
            for y1 in range(ny1)]
    n2 = 2 * lanes
    row = lax.broadcasted_iota(jnp.int32, (n2, n2), 0)
    col = lax.broadcasted_iota(jnp.int32, (n2, n2), 1)
    inter = jnp.where(col == 2 * (row % lanes) + row // lanes, 1.0, 0.0).astype(BF16)
    g1_ref[...] = jnp.dot(jnp.concatenate(rows, axis=0), inter, preferred_element_type=F32).astype(BF16)


def _slope(pre):
    sig = _sigmoid(pre)
    return sig * (1.0 + pre * (1.0 - sig))


def _kernel_a(vb_ref, vo_ref, k1_ref, k2_ref, k2t_ref, cot_ref,
              lvl_ref, s2_ref, s1_ref, g1_ref, gp_ref, sl_ref, p1o_ref, t2o_ref,
              tp, p1, t2, p2, gs, gacc):
    c0, ny, nx = vo_ref.shape[1], vo_ref.shape[3], vo_ref.shape[4]
    lanes = nx // 4
    n_act = p1.shape[0]
    ny1 = ny // 2
    ny2 = ny1 // 2
    c2 = t2.shape[2]
    c1 = c2 // 2
    rows0 = 4 * c0

    pieces = [(vb_ref, z) for z in range(vb_ref.shape[2])] + [(vo_ref, z) for z in range(vo_ref.shape[2])]
    _relayout_volume(pieces, tp, c0, ny, nx)

    for a in range(n_act):
        for d in range(3):
            for y1 in range(ny1):
                p1[a, d * 3 * 2 * rows0:(d + 1) * 3 * 2 * rows0, y1 * lanes:(y1 + 1) * lanes] = (
                    tp[2 * a + d, 2 * y1:2 * y1 + 3].reshape(3 * 2 * rows0, lanes))

    k1 = k1_ref[...]
    t2[:, 0] = jnp.zeros((n_act, c2, lanes), BF16)
    slope1 = None
    for a in range(n_act):
        pre = jnp.dot(k1, p1[a], preferred_element_type=F32)
        if a == 1:
            slope1 = _slope(pre)
        if a == 2:
            sl_ref[...] = _slope(pre)
        act = pre * _sigmoid(pre)
        for y1 in range(ny1):
            blk = act[:, y1 * lanes:(y1 + 1) * lanes]
            t2[a, y1 + 1] = jnp.concatenate([blk, _shift_right(blk)], axis=0).astype(BF16)

    for d in range(3):
        for y2 in range(ny2):
            p2[d * 3 * c2:(d + 1) * 3 * c2, y2 * lanes:(y2 + 1) * lanes] = (
                t2[d, 2 * y2:2 * y2 + 3].reshape(3 * c2, lanes))

    pre = jnp.dot(k2_ref[...], p2[...], preferred_element_type=F32)
    sig = _sigmoid(pre)
    lvl_ref[...] = (pre * sig).astype(BF16)
    bt0 = (cot_ref[...].astype(F32) * (sig * (1.0 + pre * (1.0 - sig)))).astype(BF16)
    t2o_ref[...] = t2[2]

    dup = _nt(p2[...], jnp.concatenate([bt0, bt0], axis=0))
    c2n = dup.shape[1] // 2
    qi = c1 // 4
    lane2 = lax.broadcasted_iota(jnp.int32, (qi, 2 * c2n), 1)
    for dh in range(9):
        for w, off in enumerate((3 * c1 // 2, 0, c1 // 2)):
            r0 = dh * c2 + off
            s2_ref[(dh * 3 + w) * qi:(dh * 3 + w + 1) * qi] = jnp.where(
                lane2 < c2n, dup[r0:r0 + qi], dup[r0 + qi:r0 + 2 * qi])

    gacc[...] = jnp.zeros(gacc.shape, F32)
    gs[...] = jnp.dot(k2t_ref[3 * c2:], bt0, preferred_element_type=F32)
    _add_taps(gacc, 0, gs, 0, ny2, lanes, c1)
    _add_taps(gacc, 1, gs, 3 * c2, ny2, lanes, c1)

    g = gacc[0]
    b1 = (g * slope1).astype(BF16)
    s1_ref[...] = _nt(p1[1], b1)
    _interleave(g, g1_ref, ny1, lanes)
    gp_ref[...] = gacc[1]
    p1o_ref[...] = p1[2]


def _kernel_b(vo_ref, va_ref, t2i_ref, k1_ref, k2_ref, k2t_ref, cota_ref, gp_ref, sl_ref, p1o_ref, s1a_ref,
              s1_ref, g1_ref, tp, p1, t2, p2, gs, gacc):
    c0, ny, nx = vo_ref.shape[1], vo_ref.shape[3], vo_ref.shape[4]
    lanes = nx // 4
    ny1 = ny // 2
    ny2 = ny1 // 2
    c2 = t2.shape[2]
    c1 = c2 // 2
    rows0 = 4 * c0
    nz = vo_ref.shape[2]
    pieces = [(vo_ref, nz - 1)] + [(va_ref, z) for z in range(va_ref.shape[2])]
    _relayout_volume(pieces, tp, c0, ny, nx)
    for a in range(2):
        for d in range(3):
            for y1 in range(ny1):
                p1[a, d * 3 * 2 * rows0:(d + 1) * 3 * 2 * rows0, y1 * lanes:(y1 + 1) * lanes] = (
                    tp[2 * a + d, 2 * y1:2 * y1 + 3].reshape(3 * 2 * rows0, lanes))
    k1 = k1_ref[...]
    t2[0] = t2i_ref[...]
    t2[1:, 0] = jnp.zeros((2, c2, lanes), BF16)
    for a in range(2):
        pre = jnp.dot(k1, p1[a], preferred_element_type=F32)
        act = pre * _sigmoid(pre)
        for y1 in range(ny1):
            blk = act[:, y1 * lanes:(y1 + 1) * lanes]
            t2[a + 1, y1 + 1] = jnp.concatenate([blk, _shift_right(blk)], axis=0).astype(BF16)
    for d in range(3):
        for y2 in range(ny2):
            p2[d * 3 * c2:(d + 1) * 3 * c2, y2 * lanes:(y2 + 1) * lanes] = (
                t2[d, 2 * y2:2 * y2 + 3].reshape(3 * c2, lanes))
    pre = jnp.dot(k2_ref[...], p2[...], preferred_element_type=F32)
    bt1 = (cota_ref[...].astype(F32) * _slope(pre)).astype(BF16)

    gacc[0] = gp_ref[...]
    gs[...] = jnp.dot(k2t_ref[:3 * c2], bt1, preferred_element_type=F32)
    _add_taps(gacc, 0, gs, 0, ny2, lanes, c1)
    g = gacc[0]
    b1 = (g * sl_ref[...]).astype(BF16)
    s1_ref[...] = s1a_ref[...] + _nt(p1o_ref[...], b1)
    _interleave(g, g1_ref, ny1, lanes)


def _level_one_weights(k1):
    kt = jnp.transpose(k1, (0, 2, 3, 1, 4))
    w0, w1, w2 = kt[..., 0], kt[..., 1], kt[..., 2]
    z = jnp.zeros_like(w0)
    p0 = jnp.stack([jnp.stack([w1, w2, z, z], -1), jnp.stack([z, z, z, w0], -1)], 3)
    p1 = jnp.stack([jnp.stack([z, w0, w1, w2], -1), jnp.stack([z, z, z, z], -1)], 3)
    e = jnp.stack([p0, p1], 0)
    return e.reshape(2 * k1.shape[0], -1)


def _level_two_weights(k2):
    kt = jnp.transpose(k2, (0, 2, 3, 4, 1))
    w0, w1, w2 = kt[:, :, :, 0], kt[:, :, :, 1], kt[:, :, :, 2]
    z = jnp.zeros_like(w0)
    e = jnp.stack([jnp.stack([w1, w2], 3), jnp.stack([z, w0], 3)], 3)
    return e.reshape(k2.shape[0], -1)


def per_device(volume, kernel_one, kernel_two, cotangent):
    _, c0, nz, ny, nx = volume.shape
    c1 = kernel_one.shape[0]
    c2 = kernel_two.shape[0]
    assert nz == 4 and cotangent.shape[2] == 1
    q = nx // 4
    below = shifted(volume[:, :, 1:], "gz", 1)
    above = shifted(volume, "gz", -1)
    n2 = cotangent.shape[3] * cotangent.shape[4]
    cot = cotangent[0, :, 0].reshape(c2, n2)
    cot_above = shifted(cot, "gz", -1)

    k1m = _level_one_weights(kernel_one)
    k2m = _level_two_weights(kernel_two)
    k2t = k2m.T

    ny1, ny2 = ny // 2, ny // 4
    nzi = below.shape[2] + nz
    vm = pltpu.VMEM
    kk = k1m.shape[1]
    lvl, s2, s1a, g1a, gp, sl, p1o, t2o = pl.pallas_call(
        _kernel_a,
        out_shape=(
            jax.ShapeDtypeStruct((c2, n2), BF16),
            jax.ShapeDtypeStruct((27 * c1 // 2, 2 * c2), F32),
            jax.ShapeDtypeStruct((kk, 2 * c1), F32),
            jax.ShapeDtypeStruct((ny1 * c1, 2 * q), BF16),
            jax.ShapeDtypeStruct((2 * c1, ny1 * q), F32),
            jax.ShapeDtypeStruct((2 * c1, ny1 * q), F32),
            jax.ShapeDtypeStruct((kk, ny1 * q), BF16),
            jax.ShapeDtypeStruct((ny1 + 1, 4 * c1, q), BF16),
        ),
        scratch_shapes=[
            vm((nzi, ny + 1, 8 * c0, q), BF16),
            vm((3, kk, ny1 * q), BF16),
            vm((3, ny1 + 1, 4 * c1, q), BF16),
            vm((k2m.shape[1], n2), BF16),
            vm((2 * 3 * 4 * c1, n2), F32),
            vm((2, 2 * c1, ny1 * q), F32),
        ],
        cost_estimate=pl.CostEstimate(flops=40_000_000, transcendentals=150_000, bytes_accessed=3_000_000),
    )(below, volume, k1m, k2m, k2t, cot)

    s1, g1b = pl.pallas_call(
        _kernel_b,
        out_shape=(
            jax.ShapeDtypeStruct((kk, 2 * c1), F32),
            jax.ShapeDtypeStruct((ny1 * c1, 2 * q), BF16),
        ),
        scratch_shapes=[
            vm((1 + above.shape[2], ny + 1, 8 * c0, q), BF16),
            vm((2, kk, ny1 * q), BF16),
            vm((3, ny1 + 1, 4 * c1, q), BF16),
            vm((k2m.shape[1], n2), BF16),
            vm((3 * 4 * c1, n2), F32),
            vm((1, 2 * c1, ny1 * q), F32),
        ],
        cost_estimate=pl.CostEstimate(flops=25_000_000, transcendentals=70_000, bytes_accessed=3_000_000),
    )(volume, above, t2o, k1m, k2m, k2t, cot_above, gp, sl, p1o, s1a)

    samples = volume.shape[0] * lax.axis_size("sa")
    cells_one = samples * (nz // 2) * lax.axis_size("gz") * ny1 * (nx // 2)
    cells_two = samples * cotangent.shape[2] * lax.axis_size("gz") * cotangent.shape[3] * cotangent.shape[4]

    s1r = s1.reshape(3, 3, 2, c0, 4, 2, c1)
    gk1 = jnp.stack([
        s1r[:, :, 1, :, 3, 0] + s1r[:, :, 0, :, 1, 1],
        s1r[:, :, 0, :, 0, 0] + s1r[:, :, 0, :, 2, 1],
        s1r[:, :, 0, :, 1, 0] + s1r[:, :, 0, :, 3, 1],
    ], 2)
    rows1 = gk1.size // s2.shape[1]
    t2, t1 = _all_sum(s2, gk1.reshape(rows1, s2.shape[1]), ("gz", "sa"))
    t1 = t1 / math.sqrt(float(cells_one))
    t2 = t2 / math.sqrt(float(cells_two))
    grad_kernel_one = t1.reshape(3, 3, 3, c0, c1).transpose(4, 3, 0, 1, 2)
    t2 = t2.reshape(27, c1 // 2, 2, c2).transpose(0, 2, 1, 3).reshape(3, 3, 3, c1, c2)
    grad_kernel_two = t2.transpose(4, 3, 0, 1, 2)

    level_two = lvl.reshape(1, c2, 1, ny2, n2 // ny2)
    g1 = jnp.concatenate([g1a, g1b], 0)
    grad_one = g1.reshape(2, ny1, c1, 2 * q).transpose(2, 0, 1, 3)[None]
    return (level_two, grad_one, grad_kernel_one, grad_kernel_two)


def solution(mesh):
    placed = (P("sa", None, "gz", None, None), P(), P(), P("sa", None, "gz", None, None))
    return jax.shard_map(
        per_device,
        mesh=mesh,
        in_specs=placed,
        out_specs=(P("sa", None, "gz", None, None), P("sa", None, "gz", None, None), P(), P()),
        check_vma=False,
    )
```

```python
import math

import jax
import jax.numpy as jnp
from jax import lax
from jax.experimental import pallas as pl
from jax.experimental.pallas import tpu as pltpu
from jax.sharding import PartitionSpec as P

F32 = jnp.float32
BF16 = jnp.bfloat16


def shifted(block, axis, distance):
    devices = range(lax.axis_size(axis))
    route = [(i - distance, i) for i in devices if i - distance in devices]
    return lax.ppermute(block, axis, route)


def _all_sum(x, axes):
    steps = []
    for axis in axes:
        n = lax.axis_size(axis)
        assert n & (n - 1) == 0
        k = 1
        while k < n:
            steps.append((axis, n, k))
            k *= 2
    axis0, n0, k0 = steps[0]
    rows = x.shape[0]
    half = -(-rows // 16) * 8
    x = jnp.pad(x, ((0, 2 * half - rows), (0, 0)))
    low = (lax.axis_index(axis0) & k0) == 0
    lo, hi = x[:half], x[half:]
    pair = [(i, i ^ k0) for i in range(n0)]
    part = jnp.where(low, lo, hi) + lax.ppermute(jnp.where(low, hi, lo), axis0, pair)
    for axis, n, k in steps[1:]:
        part = part + lax.ppermute(part, axis, [(i, i ^ k) for i in range(n)])
    other = lax.ppermute(part, axis0, pair)
    return jnp.where(low, jnp.concatenate([part, other], 0), jnp.concatenate([other, part], 0))[:rows]


def _sigmoid(v):
    return 1.0 / (1.0 + jnp.exp(-v))


def _shift_right(x):
    lane = lax.broadcasted_iota(jnp.int32, x.shape, x.ndim - 1)
    return jnp.where(lane == 0, 0.0, pltpu.roll(x, 1, x.ndim - 1))


def _shift_left(x):
    n = x.shape[-1]
    lane = lax.broadcasted_iota(jnp.int32, x.shape, x.ndim - 1)
    return jnp.where(lane == n - 1, 0.0, pltpu.roll(x, n - 1, x.ndim - 1))


def _nt(a, b):
    return lax.dot_general(a, b, (((1,), (1,)), ((), ())), preferred_element_type=F32)


def _kernel(vb_ref, vo_ref, va_ref, k1_ref, k2_ref, k2t_ref, cot_ref,
            lvl_ref, g1_ref, s1_ref, s2_ref,
            tp, p1, t2, pre1, p2, bt, gs, gacc, b1, g1s):
    c0, ny, nx = vo_ref.shape[1], vo_ref.shape[3], vo_ref.shape[4]
    lanes = nx // 4
    nzi = tp.shape[0]
    n_act = p1.shape[0]
    ny1 = ny // 2
    ny2 = ny1 // 2
    c2 = t2.shape[2]
    c1 = c2 // 2
    rows0 = 4 * c0

    xs = lax.broadcasted_iota(jnp.int32, (nx, nx), 0)
    cs = lax.broadcasted_iota(jnp.int32, (nx, nx), 1)
    sel_x = jnp.where(xs == 4 * (cs % lanes) + cs // lanes, 1.0, 0.0).astype(BF16)
    nq = 2 * rows0 * ny
    orow = lax.broadcasted_iota(jnp.int32, (nq, nq), 0)
    icol = lax.broadcasted_iota(jnp.int32, (nq, nq), 1)
    y_, s_ = orow // (2 * rows0), (orow // rows0) % 2
    i_, r_ = (orow // 4) % c0, orow % 4
    perm = jnp.where(icol == ((s_ * 4 + r_) * c0 + i_) * ny + y_, 1.0, 0.0).astype(BF16)

    tp[:, 0] = jnp.zeros((nzi, 2 * rows0, lanes), BF16)
    zi = 0
    for ref in (vb_ref, vo_ref, va_ref):
        nzp = ref.shape[2]
        whole = jnp.dot(ref[0].reshape(c0 * nzp * ny, nx), sel_x, preferred_element_type=F32)
        for z in range(nzp):
            ymat = jnp.concatenate([whole[(i * nzp + z) * ny:(i * nzp + z + 1) * ny] for i in range(c0)], axis=0)
            blocks = [ymat[:, r * lanes:(r + 1) * lanes] for r in range(4)]
            q = jnp.concatenate(blocks + [_shift_right(b) for b in blocks], axis=0).astype(BF16)
            t = jnp.dot(perm, q, preferred_element_type=F32).astype(BF16)
            tp[zi, 1:] = t.reshape(ny, 2 * rows0, lanes)
            zi += 1

    for a in range(n_act):
        for d in range(3):
            for y1 in range(ny1):
                p1[a, d * 3 * 2 * rows0:(d + 1) * 3 * 2 * rows0, y1 * lanes:(y1 + 1) * lanes] = (
                    tp[2 * a + d, 2 * y1:2 * y1 + 3].reshape(3 * 2 * rows0, lanes))

    k1 = k1_ref[...]
    t2[:, 0] = jnp.zeros((n_act, c2, lanes), BF16)
    for a in range(n_act):
        pre = jnp.dot(k1, p1[a], preferred_element_type=F32)
        if a in (1, 2):
            pre1[a - 1] = pre
        act = pre * _sigmoid(pre)
        for y1 in range(ny1):
            blk = act[:, y1 * lanes:(y1 + 1) * lanes]
            t2[a, y1 + 1] = jnp.concatenate([blk, _shift_right(blk)], axis=0).astype(BF16)

    for tt in range(2):
        for d in range(3):
            for y2 in range(ny2):
                p2[tt, d * 3 * c2:(d + 1) * 3 * c2, y2 * lanes:(y2 + 1) * lanes] = (
                    t2[2 * tt + d, 2 * y2:2 * y2 + 3].reshape(3 * c2, lanes))

    k2 = k2_ref[...]
    for tt in range(2):
        pre = jnp.dot(k2, p2[tt], preferred_element_type=F32)
        sig = _sigmoid(pre)
        if tt == 0:
            lvl_ref[...] = (pre * sig).astype(BF16)
        slope = sig * (1.0 + pre * (1.0 - sig))
        bt[tt] = (cot_ref[tt].astype(F32) * slope).astype(BF16)

    dup = _nt(p2[0], jnp.concatenate([bt[0], bt[0]], axis=0))
    c2n = dup.shape[1] // 2
    qi = c1 // 4
    lane2 = lax.broadcasted_iota(jnp.int32, (qi, 2 * c2n), 1)
    for dh in range(9):
        for w, off in enumerate((3 * c1 // 2, 0, c1 // 2)):
            r0 = dh * c2 + off
            s2_ref[(dh * 3 + w) * qi:(dh * 3 + w + 1) * qi] = jnp.where(
                lane2 < c2n, dup[r0:r0 + qi], dup[r0 + qi:r0 + 2 * qi])

    gacc[...] = jnp.zeros(gacc.shape, F32)
    k2t = k2t_ref[...]
    for tt in range(2):
        if tt == 0:
            gs[...] = jnp.dot(k2t, bt[0], preferred_element_type=F32)
            taps_d = (1, 2)
        else:
            gs[0:3 * c2] = jnp.dot(k2t[0:3 * c2], bt[1], preferred_element_type=F32)
            taps_d = (0,)
        for d in taps_d:
            a = 2 * tt + d
            for h in range(3):
                for y2 in range(ny2):
                    y1 = 2 * y2 + h - 1
                    if y1 < 0:
                        continue
                    r0 = (d * 3 + h) * c2
                    blk = gs[r0:r0 + c2, y2 * lanes:(y2 + 1) * lanes]
                    gacc[a - 1, :, y1 * lanes:(y1 + 1) * lanes] += blk[:c1] + _shift_left(blk[c1:])

    half = c1 // 2
    for a_ in range(2):
        g = gacc[a_]
        pre = pre1[a_]
        sig = _sigmoid(pre)
        slope = sig * (1.0 + pre * (1.0 - sig))
        b1[a_] = (g * slope).astype(BF16)
        gb = g.astype(BF16)
        for y1 in range(ny1):
            blk = gb[:, y1 * lanes:(y1 + 1) * lanes]
            r0 = (a_ * ny1 + y1) * half
            g1s[r0:r0 + half] = jnp.concatenate([blk[:half], blk[half:]], axis=1)
    s1_ref[...] = _nt(p1[1], b1[0]) + _nt(p1[2], b1[1])

    n2 = 2 * lanes
    row = lax.broadcasted_iota(jnp.int32, (n2, n2), 0)
    col = lax.broadcasted_iota(jnp.int32, (n2, n2), 1)
    inter = jnp.where(col == 2 * (row % lanes) + row // lanes, 1.0, 0.0).astype(BF16)
    g1_ref[...] = jnp.dot(g1s[...], inter, preferred_element_type=F32).astype(BF16)


def _level_one_weights(k1):
    kt = jnp.transpose(k1, (0, 2, 3, 1, 4))
    w0, w1, w2 = kt[..., 0], kt[..., 1], kt[..., 2]
    z = jnp.zeros_like(w0)
    p0 = jnp.stack([jnp.stack([w1, w2, z, z], -1), jnp.stack([z, z, z, w0], -1)], 3)
    p1 = jnp.stack([jnp.stack([z, w0, w1, w2], -1), jnp.stack([z, z, z, z], -1)], 3)
    e = jnp.stack([p0, p1], 0)
    return e.reshape(2 * k1.shape[0], -1)


def _level_two_weights(k2):
    kt = jnp.transpose(k2, (0, 2, 3, 4, 1))
    w0, w1, w2 = kt[:, :, :, 0], kt[:, :, :, 1], kt[:, :, :, 2]
    z = jnp.zeros_like(w0)
    e = jnp.stack([jnp.stack([w1, w2], 3), jnp.stack([z, w0], 3)], 3)
    return e.reshape(k2.shape[0], -1)


def per_device(volume, kernel_one, kernel_two, cotangent):
    _, c0, nz, ny, nx = volume.shape
    c1 = kernel_one.shape[0]
    c2 = kernel_two.shape[0]
    assert nz == 4 and cotangent.shape[2] == 1
    q = nx // 4
    below = shifted(volume[:, :, 1:], "gz", 1)
    above = shifted(volume, "gz", -1)
    cot_above = shifted(cotangent, "gz", -1)
    nzi = below.shape[2] + nz + above.shape[2]
    n2 = cotangent.shape[3] * cotangent.shape[4]
    cots = jnp.concatenate([cotangent, cot_above], 2)[0].transpose(1, 0, 2, 3).reshape(2, c2, n2)

    k1m = _level_one_weights(kernel_one)
    k2m = _level_two_weights(kernel_two)
    k2t = k2m.T

    ny1, ny2 = ny // 2, ny // 4
    n_act = 5
    vm = pltpu.VMEM
    lvl, g1, s1, s2 = pl.pallas_call(
        _kernel,
        out_shape=(
            jax.ShapeDtypeStruct((c2, n2), BF16),
            jax.ShapeDtypeStruct((2 * ny1 * c1, 2 * q), BF16),
            jax.ShapeDtypeStruct((k1m.shape[1], k1m.shape[0]), F32),
            jax.ShapeDtypeStruct((27 * c1 // 2, 2 * c2), F32),
        ),
        scratch_shapes=[
            vm((nzi, ny + 1, 8 * c0, q), BF16),
            vm((n_act, k1m.shape[1], ny1 * q), BF16),
            vm((n_act, ny1 + 1, 4 * c1, q), BF16),
            vm((2, 2 * c1, ny1 * q), F32),
            vm((2, k2m.shape[1], n2), BF16),
            vm((2, c2, n2), BF16),
            vm((k2m.shape[1], n2), F32),
            vm((2, 2 * c1, ny1 * q), F32),
            vm((2, 2 * c1, ny1 * q), BF16),
            vm((2 * ny1 * c1, 2 * q), BF16),
        ],
        cost_estimate=pl.CostEstimate(flops=60_000_000, transcendentals=200_000, bytes_accessed=3_000_000),
    )(below, volume, above, k1m, k2m, k2t, cots)

    level_two = lvl.reshape(1, c2, 1, ny2, n2 // ny2)
    grad_one = g1.reshape(2, ny1, c1, 2 * q).transpose(2, 0, 1, 3)[None]

    s1r = s1.reshape(3, 3, 2, c0, 4, 2, c1)
    gk1 = jnp.stack([
        s1r[:, :, 1, :, 3, 0] + s1r[:, :, 0, :, 1, 1],
        s1r[:, :, 0, :, 0, 0] + s1r[:, :, 0, :, 2, 1],
        s1r[:, :, 0, :, 1, 0] + s1r[:, :, 0, :, 3, 1],
    ], 2)
    rows1 = gk1.size // s2.shape[1]
    total = _all_sum(jnp.concatenate([gk1.reshape(rows1, s2.shape[1]), s2], 0), ("gz", "sa"))
    samples = volume.shape[0] * lax.axis_size("sa")
    cells_one = samples * (nz // 2) * lax.axis_size("gz") * ny1 * (nx // 2)
    cells_two = samples * cotangent.shape[2] * lax.axis_size("gz") * cotangent.shape[3] * cotangent.shape[4]
    t1 = total[:rows1] / math.sqrt(float(cells_one))
    t2 = total[rows1:] / math.sqrt(float(cells_two))
    grad_kernel_one = t1.reshape(3, 3, 3, c0, c1).transpose(4, 3, 0, 1, 2)
    t2 = t2.reshape(27, c1 // 2, 2, c2).transpose(0, 2, 1, 3).reshape(3, 3, 3, c1, c2)
    grad_kernel_two = t2.transpose(4, 3, 0, 1, 2)
    return (level_two, grad_one, grad_kernel_one, grad_kernel_two)


def solution(mesh):
    placed = (P("sa", None, "gz", None, None), P(), P(), P("sa", None, "gz", None, None))
    return jax.shard_map(
        per_device,
        mesh=mesh,
        in_specs=placed,
        out_specs=(P("sa", None, "gz", None, None), P("sa", None, "gz", None, None), P(), P()),
        check_vma=False,
    )
```

```python
import math

import jax
import jax.numpy as jnp
from jax import lax
from jax.experimental import pallas as pl
from jax.experimental.pallas import tpu as pltpu
from jax.sharding import PartitionSpec as P

F32 = jnp.float32
BF16 = jnp.bfloat16


def shifted(block, axis, distance):
    devices = range(lax.axis_size(axis))
    route = [(i - distance, i) for i in devices if i - distance in devices]
    return lax.ppermute(block, axis, route)


def _all_sum(x, axes):
    steps = []
    for axis in axes:
        n = lax.axis_size(axis)
        assert n & (n - 1) == 0
        k = 1
        while k < n:
            steps.append((axis, n, k))
            k *= 2
    axis0, n0, k0 = steps[0]
    rows = x.shape[0]
    half = -(-rows // 16) * 8
    x = jnp.pad(x, ((0, 2 * half - rows), (0, 0)))
    low = (lax.axis_index(axis0) & k0) == 0
    lo, hi = x[:half], x[half:]
    pair = [(i, i ^ k0) for i in range(n0)]
    part = jnp.where(low, lo, hi) + lax.ppermute(jnp.where(low, hi, lo), axis0, pair)
    for axis, n, k in steps[1:]:
        part = part + lax.ppermute(part, axis, [(i, i ^ k) for i in range(n)])
    other = lax.ppermute(part, axis0, pair)
    return jnp.where(low, jnp.concatenate([part, other], 0), jnp.concatenate([other, part], 0))[:rows]


def _sigmoid(v):
    return 1.0 / (1.0 + jnp.exp(-v))


def _shift_right(x):
    lane = lax.broadcasted_iota(jnp.int32, x.shape, x.ndim - 1)
    return jnp.where(lane == 0, 0.0, pltpu.roll(x, 1, x.ndim - 1))


def _shift_left(x):
    n = x.shape[-1]
    lane = lax.broadcasted_iota(jnp.int32, x.shape, x.ndim - 1)
    return jnp.where(lane == n - 1, 0.0, pltpu.roll(x, n - 1, x.ndim - 1))


def _nt(a, b):
    return lax.dot_general(a, b, (((1,), (1,)), ((), ())), preferred_element_type=F32)


def _kernel(vb_ref, vo_ref, va_ref, k1_ref, k2_ref, k2t_ref, cot_ref,
            lvl_ref, g1_ref, s1_ref, s2_ref,
            tp, p1, t2, pre1, p2, bt, gs, gacc, b1, g1s):
    c0, ny, nx = vo_ref.shape[1], vo_ref.shape[3], vo_ref.shape[4]
    lanes = nx // 4
    nzi = tp.shape[0]
    n_act = p1.shape[0]
    ny1 = ny // 2
    ny2 = ny1 // 2
    c2 = t2.shape[2]
    c1 = c2 // 2
    rows0 = 4 * c0

    xs = lax.broadcasted_iota(jnp.int32, (nx, nx), 0)
    cs = lax.broadcasted_iota(jnp.int32, (nx, nx), 1)
    sel_x = jnp.where(xs == 4 * (cs % lanes) + cs // lanes, 1.0, 0.0).astype(BF16)
    nq = 2 * rows0 * ny
    orow = lax.broadcasted_iota(jnp.int32, (nq, nq), 0)
    icol = lax.broadcasted_iota(jnp.int32, (nq, nq), 1)
    y_, s_ = orow // (2 * rows0), (orow // rows0) % 2
    i_, r_ = (orow // 4) % c0, orow % 4
    perm = jnp.where(icol == ((s_ * 4 + r_) * c0 + i_) * ny + y_, 1.0, 0.0).astype(BF16)

    tp[:, 0] = jnp.zeros((nzi, 2 * rows0, lanes), BF16)
    zi = 0
    nz_own = vo_ref.shape[2]
    for ref, nzp in ((vb_ref, vb_ref.shape[2]), (vo_ref, nz_own), (va_ref, nz_own)):
        if ref is va_ref:
            zmat = ref[0:c0 * nzp * ny]
        else:
            zmat = ref[0].reshape(c0 * nzp * ny, nx)
        whole = jnp.dot(zmat, sel_x, preferred_element_type=F32)
        for z in range(nzp):
            ymat = jnp.concatenate([whole[(i * nzp + z) * ny:(i * nzp + z + 1) * ny] for i in range(c0)], axis=0)
            blocks = [ymat[:, r * lanes:(r + 1) * lanes] for r in range(4)]
            q = jnp.concatenate(blocks + [_shift_right(b) for b in blocks], axis=0).astype(BF16)
            t = jnp.dot(perm, q, preferred_element_type=F32).astype(BF16)
            tp[zi, 1:] = t.reshape(ny, 2 * rows0, lanes)
            zi += 1

    for a in range(n_act):
        for d in range(3):
            for y1 in range(ny1):
                p1[a, d * 3 * 2 * rows0:(d + 1) * 3 * 2 * rows0, y1 * lanes:(y1 + 1) * lanes] = (
                    tp[2 * a + d, 2 * y1:2 * y1 + 3].reshape(3 * 2 * rows0, lanes))

    k1 = k1_ref[...]
    t2[:, 0] = jnp.zeros((n_act, c2, lanes), BF16)
    for a in range(n_act):
        pre = jnp.dot(k1, p1[a], preferred_element_type=F32)
        if a in (1, 2):
            pre1[a - 1] = pre
        act = pre * _sigmoid(pre)
        for y1 in range(ny1):
            blk = act[:, y1 * lanes:(y1 + 1) * lanes]
            t2[a, y1 + 1] = jnp.concatenate([blk, _shift_right(blk)], axis=0).astype(BF16)

    for tt in range(2):
        for d in range(3):
            for y2 in range(ny2):
                p2[tt, d * 3 * c2:(d + 1) * 3 * c2, y2 * lanes:(y2 + 1) * lanes] = (
                    t2[2 * tt + d, 2 * y2:2 * y2 + 3].reshape(3 * c2, lanes))

    k2 = k2_ref[...]
    for tt in range(2):
        pre = jnp.dot(k2, p2[tt], preferred_element_type=F32)
        sig = _sigmoid(pre)
        if tt == 0:
            lvl_ref[...] = (pre * sig).astype(BF16)
        slope = sig * (1.0 + pre * (1.0 - sig))
        cot_t = cot_ref[...] if tt == 0 else va_ref[va_ref.shape[0] - c1:]
        bt[tt] = (cot_t.astype(F32) * slope).astype(BF16)

    dup = _nt(p2[0], jnp.concatenate([bt[0], bt[0]], axis=0))
    c2n = dup.shape[1] // 2
    qi = c1 // 4
    lane2 = lax.broadcasted_iota(jnp.int32, (qi, 2 * c2n), 1)
    for dh in range(9):
        for w, off in enumerate((3 * c1 // 2, 0, c1 // 2)):
            r0 = dh * c2 + off
            s2_ref[(dh * 3 + w) * qi:(dh * 3 + w + 1) * qi] = jnp.where(
                lane2 < c2n, dup[r0:r0 + qi], dup[r0 + qi:r0 + 2 * qi])

    gacc[...] = jnp.zeros(gacc.shape, F32)
    k2t = k2t_ref[...]
    for tt in range(2):
        if tt == 0:
            gs[...] = jnp.dot(k2t, bt[0], preferred_element_type=F32)
            taps_d = (1, 2)
        else:
            gs[0:3 * c2] = jnp.dot(k2t[0:3 * c2], bt[1], preferred_element_type=F32)
            taps_d = (0,)
        for d in taps_d:
            a = 2 * tt + d
            for h in range(3):
                for y2 in range(ny2):
                    y1 = 2 * y2 + h - 1
                    if y1 < 0:
                        continue
                    r0 = (d * 3 + h) * c2
                    blk = gs[r0:r0 + c2, y2 * lanes:(y2 + 1) * lanes]
                    gacc[a - 1, :, y1 * lanes:(y1 + 1) * lanes] += blk[:c1] + _shift_left(blk[c1:])

    half = c1 // 2
    for a_ in range(2):
        g = gacc[a_]
        pre = pre1[a_]
        sig = _sigmoid(pre)
        slope = sig * (1.0 + pre * (1.0 - sig))
        b1[a_] = (g * slope).astype(BF16)
        gb = g.astype(BF16)
        for y1 in range(ny1):
            blk = gb[:, y1 * lanes:(y1 + 1) * lanes]
            r0 = (a_ * ny1 + y1) * half
            g1s[r0:r0 + half] = jnp.concatenate([blk[:half], blk[half:]], axis=1)
    s1_ref[...] = _nt(p1[1], b1[0]) + _nt(p1[2], b1[1])

    n2 = 2 * lanes
    row = lax.broadcasted_iota(jnp.int32, (n2, n2), 0)
    col = lax.broadcasted_iota(jnp.int32, (n2, n2), 1)
    inter = jnp.where(col == 2 * (row % lanes) + row // lanes, 1.0, 0.0).astype(BF16)
    g1_ref[...] = jnp.dot(g1s[...], inter, preferred_element_type=F32).astype(BF16)


def _level_one_weights(k1):
    kt = jnp.transpose(k1, (0, 2, 3, 1, 4))
    w0, w1, w2 = kt[..., 0], kt[..., 1], kt[..., 2]
    z = jnp.zeros_like(w0)
    p0 = jnp.stack([jnp.stack([w1, w2, z, z], -1), jnp.stack([z, z, z, w0], -1)], 3)
    p1 = jnp.stack([jnp.stack([z, w0, w1, w2], -1), jnp.stack([z, z, z, z], -1)], 3)
    e = jnp.stack([p0, p1], 0)
    return e.reshape(2 * k1.shape[0], -1)


def _level_two_weights(k2):
    kt = jnp.transpose(k2, (0, 2, 3, 4, 1))
    w0, w1, w2 = kt[:, :, :, 0], kt[:, :, :, 1], kt[:, :, :, 2]
    z = jnp.zeros_like(w0)
    e = jnp.stack([jnp.stack([w1, w2], 3), jnp.stack([z, w0], 3)], 3)
    return e.reshape(k2.shape[0], -1)


def per_device(volume, kernel_one, kernel_two, cotangent):
    _, c0, nz, ny, nx = volume.shape
    c1 = kernel_one.shape[0]
    c2 = kernel_two.shape[0]
    assert nz == 4 and cotangent.shape[2] == 1
    q = nx // 4
    below = shifted(volume[:, :, 1:], "gz", 1)
    cot = cotangent[0, :, 0].reshape(cotangent.shape[1], -1)
    above = shifted(jnp.concatenate([volume[0].reshape(-1, nx), cot], 0), "gz", -1)
    nzi = below.shape[2] + 2 * nz
    n2 = cotangent.shape[3] * cotangent.shape[4]

    k1m = _level_one_weights(kernel_one)
    k2m = _level_two_weights(kernel_two)
    k2t = k2m.T

    ny1, ny2 = ny // 2, ny // 4
    n_act = 5
    vm = pltpu.VMEM
    lvl, g1, s1, s2 = pl.pallas_call(
        _kernel,
        out_shape=(
            jax.ShapeDtypeStruct((c2, n2), BF16),
            jax.ShapeDtypeStruct((2 * ny1 * c1, 2 * q), BF16),
            jax.ShapeDtypeStruct((k1m.shape[1], k1m.shape[0]), F32),
            jax.ShapeDtypeStruct((27 * c1 // 2, 2 * c2), F32),
        ),
        scratch_shapes=[
            vm((nzi, ny + 1, 8 * c0, q), BF16),
            vm((n_act, k1m.shape[1], ny1 * q), BF16),
            vm((n_act, ny1 + 1, 4 * c1, q), BF16),
            vm((2, 2 * c1, ny1 * q), F32),
            vm((2, k2m.shape[1], n2), BF16),
            vm((2, c2, n2), BF16),
            vm((k2m.shape[1], n2), F32),
            vm((2, 2 * c1, ny1 * q), F32),
            vm((2, 2 * c1, ny1 * q), BF16),
            vm((2 * ny1 * c1, 2 * q), BF16),
        ],
        cost_estimate=pl.CostEstimate(flops=60_000_000, transcendentals=200_000, bytes_accessed=3_000_000),
    )(below, volume, above, k1m, k2m, k2t, cot)

    level_two = lvl.reshape(1, c2, 1, ny2, n2 // ny2)
    grad_one = g1.reshape(2, ny1, c1, 2 * q).transpose(2, 0, 1, 3)[None]

    s1r = s1.reshape(3, 3, 2, c0, 4, 2, c1)
    gk1 = jnp.stack([
        s1r[:, :, 1, :, 3, 0] + s1r[:, :, 0, :, 1, 1],
        s1r[:, :, 0, :, 0, 0] + s1r[:, :, 0, :, 2, 1],
        s1r[:, :, 0, :, 1, 0] + s1r[:, :, 0, :, 3, 1],
    ], 2)
    rows1 = gk1.size // s2.shape[1]
    total = _all_sum(jnp.concatenate([gk1.reshape(rows1, s2.shape[1]), s2], 0), ("gz", "sa"))
    samples = volume.shape[0] * lax.axis_size("sa")
    cells_one = samples * (nz // 2) * lax.axis_size("gz") * ny1 * (nx // 2)
    cells_two = samples * cotangent.shape[2] * lax.axis_size("gz") * cotangent.shape[3] * cotangent.shape[4]
    t1 = total[:rows1] / math.sqrt(float(cells_one))
    t2 = total[rows1:] / math.sqrt(float(cells_two))
    grad_kernel_one = t1.reshape(3, 3, 3, c0, c1).transpose(4, 3, 0, 1, 2)
    t2 = t2.reshape(27, c1 // 2, 2, c2).transpose(0, 2, 1, 3).reshape(3, 3, 3, c1, c2)
    grad_kernel_two = t2.transpose(4, 3, 0, 1, 2)
    return (level_two, grad_one, grad_kernel_one, grad_kernel_two)


def solution(mesh):
    placed = (P("sa", None, "gz", None, None), P(), P(), P("sa", None, "gz", None, None))
    return jax.shard_map(
        per_device,
        mesh=mesh,
        in_specs=placed,
        out_specs=(P("sa", None, "gz", None, None), P("sa", None, "gz", None, None), P(), P()),
        check_vma=False,
    )
```

```python
import math

import jax
import jax.numpy as jnp
from jax import lax
from jax.experimental import pallas as pl
from jax.experimental.pallas import tpu as pltpu
from jax.sharding import PartitionSpec as P

F32 = jnp.float32
BF16 = jnp.bfloat16


def shifted(block, axis, distance):
    devices = range(lax.axis_size(axis))
    route = [(i - distance, i) for i in devices if i - distance in devices]
    return lax.ppermute(block, axis, route)


def _all_sum(x, axes):
    steps = []
    for axis in axes:
        n = lax.axis_size(axis)
        assert n & (n - 1) == 0
        k = 1
        while k < n:
            steps.append((axis, n, k))
            k *= 2
    axis0, n0, k0 = steps[0]
    rows = x.shape[0]
    half = -(-rows // 16) * 8
    x = jnp.pad(x, ((0, 2 * half - rows), (0, 0)))
    low = (lax.axis_index(axis0) & k0) == 0
    lo, hi = x[:half], x[half:]
    pair = [(i, i ^ k0) for i in range(n0)]
    part = jnp.where(low, lo, hi) + lax.ppermute(jnp.where(low, hi, lo), axis0, pair)
    for axis, n, k in steps[1:]:
        part = part + lax.ppermute(part, axis, [(i, i ^ k) for i in range(n)])
    other = lax.ppermute(part, axis0, pair)
    return jnp.where(low, jnp.concatenate([part, other], 0), jnp.concatenate([other, part], 0))[:rows]


def _sigmoid(v):
    return 1.0 / (1.0 + jnp.exp(-v))


def _shift_right(x):
    lane = lax.broadcasted_iota(jnp.int32, x.shape, x.ndim - 1)
    return jnp.where(lane == 0, 0.0, pltpu.roll(x, 1, x.ndim - 1))


def _shift_left(x):
    n = x.shape[-1]
    lane = lax.broadcasted_iota(jnp.int32, x.shape, x.ndim - 1)
    return jnp.where(lane == n - 1, 0.0, pltpu.roll(x, n - 1, x.ndim - 1))


def _nt(a, b):
    return lax.dot_general(a, b, (((1,), (1,)), ((), ())), preferred_element_type=F32)


def _kernel(vb_ref, vo_ref, va_ref, k1_ref, k2_ref, k2t_ref, cot_ref,
            lvl_ref, g1_ref, s1_ref, s2_ref,
            tp, p1, t2, pre1, p2, bt, gs, gacc, b1, g1s):
    c0, ny, nx = vo_ref.shape[1], vo_ref.shape[3], vo_ref.shape[4]
    lanes = nx // 4
    nzi = tp.shape[0]
    n_act = p1.shape[0]
    ny1 = ny // 2
    ny2 = ny1 // 2
    c2 = t2.shape[2]
    c1 = c2 // 2
    rows0 = 4 * c0

    xs = lax.broadcasted_iota(jnp.int32, (nx, nx), 0)
    cs = lax.broadcasted_iota(jnp.int32, (nx, nx), 1)
    sel_x = jnp.where(xs == 4 * (cs % lanes) + cs // lanes, 1.0, 0.0).astype(BF16)
    nq = 2 * rows0 * ny
    orow = lax.broadcasted_iota(jnp.int32, (nq, nq), 0)
    icol = lax.broadcasted_iota(jnp.int32, (nq, nq), 1)
    y_, s_ = orow // (2 * rows0), (orow // rows0) % 2
    i_, r_ = (orow // 4) % c0, orow % 4
    perm = jnp.where(icol == ((s_ * 4 + r_) * c0 + i_) * ny + y_, 1.0, 0.0).astype(BF16)

    tp[:, 0] = jnp.zeros((nzi, 2 * rows0, lanes), BF16)
    zi = 0
    nz_own = vo_ref.shape[2]
    for ref, nzp in ((vb_ref, vb_ref.shape[2]), (vo_ref, nz_own), (va_ref, nz_own)):
        if ref is va_ref:
            zmat = ref[0:c0 * nzp * ny]
        else:
            zmat = ref[0].reshape(c0 * nzp * ny, nx)
        whole = jnp.dot(zmat, sel_x, preferred_element_type=F32)
        for z in range(nzp):
            ymat = jnp.concatenate([whole[(i * nzp + z) * ny:(i * nzp + z + 1) * ny] for i in range(c0)], axis=0)
            blocks = [ymat[:, r * lanes:(r + 1) * lanes] for r in range(4)]
            q = jnp.concatenate(blocks + [_shift_right(b) for b in blocks], axis=0).astype(BF16)
            t = jnp.dot(perm, q, preferred_element_type=F32).astype(BF16)
            tp[zi, 1:] = t.reshape(ny, 2 * rows0, lanes)
            zi += 1

    for a in range(n_act):
        for d in range(3):
            for y1 in range(ny1):
                p1[a, d * 3 * 2 * rows0:(d + 1) * 3 * 2 * rows0, y1 * lanes:(y1 + 1) * lanes] = (
                    tp[2 * a + d, 2 * y1:2 * y1 + 3].reshape(3 * 2 * rows0, lanes))

    k1 = k1_ref[...]
    t2[:, 0] = jnp.zeros((n_act, c2, lanes), BF16)
    for a in range(n_act):
        pre = jnp.dot(k1, p1[a], preferred_element_type=F32)
        if a in (1, 2):
            pre1[a - 1] = pre
        act = pre * _sigmoid(pre)
        for y1 in range(ny1):
            blk = act[:, y1 * lanes:(y1 + 1) * lanes]
            t2[a, y1 + 1] = jnp.concatenate([blk, _shift_right(blk)], axis=0).astype(BF16)

    for tt in range(2):
        for d in range(3):
            for y2 in range(ny2):
                p2[tt, d * 3 * c2:(d + 1) * 3 * c2, y2 * lanes:(y2 + 1) * lanes] = (
                    t2[2 * tt + d, 2 * y2:2 * y2 + 3].reshape(3 * c2, lanes))

    k2 = k2_ref[...]
    for tt in range(2):
        pre = jnp.dot(k2, p2[tt], preferred_element_type=F32)
        sig = _sigmoid(pre)
        if tt == 0:
            lvl_ref[...] = (pre * sig).astype(BF16)
        slope = sig * (1.0 + pre * (1.0 - sig))
        cot_t = cot_ref[...] if tt == 0 else va_ref[va_ref.shape[0] - c1:]
        bt[tt] = (cot_t.astype(F32) * slope).astype(BF16)

    dup = _nt(p2[0], jnp.concatenate([bt[0], bt[0]], axis=0))
    c2n = dup.shape[1] // 2
    qi = c1 // 4
    lane2 = lax.broadcasted_iota(jnp.int32, (qi, 2 * c2n), 1)
    n_s2 = 27 * qi
    s2_ref[n_s2:] = jnp.zeros((s2_ref.shape[0] - n_s2, s2_ref.shape[1]), F32)
    for dh in range(9):
        for w, off in enumerate((3 * c1 // 2, 0, c1 // 2)):
            r0 = dh * c2 + off
            s2_ref[(dh * 3 + w) * qi:(dh * 3 + w + 1) * qi] = jnp.where(
                lane2 < c2n, dup[r0:r0 + qi], dup[r0 + qi:r0 + 2 * qi])

    gacc[...] = jnp.zeros(gacc.shape, F32)
    k2t = k2t_ref[...]
    for tt in range(2):
        if tt == 0:
            gs[...] = jnp.dot(k2t, bt[0], preferred_element_type=F32)
            taps_d = (1, 2)
        else:
            gs[0:3 * c2] = jnp.dot(k2t[0:3 * c2], bt[1], preferred_element_type=F32)
            taps_d = (0,)
        for d in taps_d:
            a = 2 * tt + d
            for h in range(3):
                for y2 in range(ny2):
                    y1 = 2 * y2 + h - 1
                    if y1 < 0:
                        continue
                    r0 = (d * 3 + h) * c2
                    blk = gs[r0:r0 + c2, y2 * lanes:(y2 + 1) * lanes]
                    gacc[a - 1, :, y1 * lanes:(y1 + 1) * lanes] += blk[:c1] + _shift_left(blk[c1:])

    half = c1 // 2
    for a_ in range(2):
        g = gacc[a_]
        pre = pre1[a_]
        sig = _sigmoid(pre)
        slope = sig * (1.0 + pre * (1.0 - sig))
        b1[a_] = (g * slope).astype(BF16)
        gb = g.astype(BF16)
        for y1 in range(ny1):
            blk = gb[:, y1 * lanes:(y1 + 1) * lanes]
            r0 = (a_ * ny1 + y1) * half
            g1s[r0:r0 + half] = jnp.concatenate([blk[:half], blk[half:]], axis=1)
    zb = jnp.zeros(b1.shape[1:], BF16)
    s1_ref[...] = (_nt(p1[1], jnp.concatenate([b1[0], zb], axis=0))
                   + _nt(p1[2], jnp.concatenate([b1[1], zb], axis=0)))

    n2 = 2 * lanes
    row = lax.broadcasted_iota(jnp.int32, (n2, n2), 0)
    col = lax.broadcasted_iota(jnp.int32, (n2, n2), 1)
    inter = jnp.where(col == 2 * (row % lanes) + row // lanes, 1.0, 0.0).astype(BF16)
    g1_ref[...] = jnp.dot(g1s[...], inter, preferred_element_type=F32).astype(BF16)


def _level_one_weights(k1):
    kt = jnp.transpose(k1, (0, 2, 3, 1, 4))
    w0, w1, w2 = kt[..., 0], kt[..., 1], kt[..., 2]
    z = jnp.zeros_like(w0)
    p0 = jnp.stack([jnp.stack([w1, w2, z, z], -1), jnp.stack([z, z, z, w0], -1)], 3)
    p1 = jnp.stack([jnp.stack([z, w0, w1, w2], -1), jnp.stack([z, z, z, z], -1)], 3)
    e = jnp.stack([p0, p1], 0)
    return e.reshape(2 * k1.shape[0], -1)


def _level_two_weights(k2):
    kt = jnp.transpose(k2, (0, 2, 3, 4, 1))
    w0, w1, w2 = kt[:, :, :, 0], kt[:, :, :, 1], kt[:, :, :, 2]
    z = jnp.zeros_like(w0)
    e = jnp.stack([jnp.stack([w1, w2], 3), jnp.stack([z, w0], 3)], 3)
    return e.reshape(k2.shape[0], -1)


def per_device(volume, kernel_one, kernel_two, cotangent):
    _, c0, nz, ny, nx = volume.shape
    c1 = kernel_one.shape[0]
    c2 = kernel_two.shape[0]
    assert nz == 4 and cotangent.shape[2] == 1
    q = nx // 4
    below = shifted(volume[:, :, 1:], "gz", 1)
    cot = cotangent[0, :, 0].reshape(cotangent.shape[1], -1)
    above = shifted(jnp.concatenate([volume[0].reshape(-1, nx), cot], 0), "gz", -1)
    nzi = below.shape[2] + 2 * nz
    n2 = cotangent.shape[3] * cotangent.shape[4]

    k1m = _level_one_weights(kernel_one)
    k2m = _level_two_weights(kernel_two)
    k2t = k2m.T

    ny1, ny2 = ny // 2, ny // 4
    n_act = 5
    n_s2 = 27 * c1 // 2
    n_g1 = 27 * c0 * c1 // (2 * c2)
    n_pay = -(-(n_s2 + n_g1) // 16) * 16
    vm = pltpu.VMEM
    lvl, g1, s1, pay = pl.pallas_call(
        _kernel,
        out_shape=(
            jax.ShapeDtypeStruct((c2, n2), BF16),
            jax.ShapeDtypeStruct((2 * ny1 * c1, 2 * q), BF16),
            jax.ShapeDtypeStruct((k1m.shape[1], 2 * k1m.shape[0]), F32),
            jax.ShapeDtypeStruct((n_pay, 2 * c2), F32),
        ),
        scratch_shapes=[
            vm((nzi, ny + 1, 8 * c0, q), BF16),
            vm((n_act, k1m.shape[1], ny1 * q), BF16),
            vm((n_act, ny1 + 1, 4 * c1, q), BF16),
            vm((2, 2 * c1, ny1 * q), F32),
            vm((2, k2m.shape[1], n2), BF16),
            vm((2, c2, n2), BF16),
            vm((k2m.shape[1], n2), F32),
            vm((2, 2 * c1, ny1 * q), F32),
            vm((2, 2 * c1, ny1 * q), BF16),
            vm((2 * ny1 * c1, 2 * q), BF16),
        ],
        cost_estimate=pl.CostEstimate(flops=60_000_000, transcendentals=200_000, bytes_accessed=3_000_000),
    )(below, volume, above, k1m, k2m, k2t, cot)

    level_two = lvl.reshape(1, c2, 1, ny2, n2 // ny2)
    grad_one = g1.reshape(2, ny1, c1, 2 * q).transpose(2, 0, 1, 3)[None]

    s1r = s1.reshape(3, 3, 2, c0, 4, 2 * 2 * c1)[..., :2 * c1].reshape(3, 3, 2, c0, 4, 2, c1)
    gk1 = jnp.stack([
        s1r[:, :, 1, :, 3, 0] + s1r[:, :, 0, :, 1, 1],
        s1r[:, :, 0, :, 0, 0] + s1r[:, :, 0, :, 2, 1],
        s1r[:, :, 0, :, 1, 0] + s1r[:, :, 0, :, 3, 1],
    ], 2)
    pay = lax.dynamic_update_slice(pay, gk1.reshape(n_g1, 2 * c2), (n_s2, 0))
    total = _all_sum(pay, ("gz", "sa"))
    samples = volume.shape[0] * lax.axis_size("sa")
    cells_one = samples * (nz // 2) * lax.axis_size("gz") * ny1 * (nx // 2)
    cells_two = samples * cotangent.shape[2] * lax.axis_size("gz") * cotangent.shape[3] * cotangent.shape[4]
    t1 = total[n_s2:n_s2 + n_g1] / math.sqrt(float(cells_one))
    t2 = total[:n_s2] / math.sqrt(float(cells_two))
    grad_kernel_one = t1.reshape(3, 3, 3, c0, c1).transpose(4, 3, 0, 1, 2)
    t2 = t2.reshape(27, c1 // 2, 2, c2).transpose(0, 2, 1, 3).reshape(3, 3, 3, c1, c2)
    grad_kernel_two = t2.transpose(4, 3, 0, 1, 2)
    return (level_two, grad_one, grad_kernel_one, grad_kernel_two)


def solution(mesh):
    placed = (P("sa", None, "gz", None, None), P(), P(), P("sa", None, "gz", None, None))
    return jax.shard_map(
        per_device,
        mesh=mesh,
        in_specs=placed,
        out_specs=(P("sa", None, "gz", None, None), P("sa", None, "gz", None, None), P(), P()),
        check_vma=False,
    )
```

```python
import math

import jax
import jax.numpy as jnp
from jax import lax
from jax.experimental import pallas as pl
from jax.experimental.pallas import tpu as pltpu
from jax.sharding import PartitionSpec as P

F32 = jnp.float32
BF16 = jnp.bfloat16


def shifted(block, axis, distance):
    devices = range(lax.axis_size(axis))
    route = [(i - distance, i) for i in devices if i - distance in devices]
    return lax.ppermute(block, axis, route)


def _all_sum(x, axes):
    steps = []
    for axis in axes:
        n = lax.axis_size(axis)
        assert n & (n - 1) == 0
        k = 1
        while k < n:
            steps.append((axis, n, k))
            k *= 2
    axis0, n0, k0 = steps[0]
    rows = x.shape[0]
    half = -(-rows // 16) * 8
    x = jnp.pad(x, ((0, 2 * half - rows), (0, 0)))
    low = (lax.axis_index(axis0) & k0) == 0
    lo, hi = x[:half], x[half:]
    pair = [(i, i ^ k0) for i in range(n0)]
    part = jnp.where(low, lo, hi) + lax.ppermute(jnp.where(low, hi, lo), axis0, pair)
    for axis, n, k in steps[1:]:
        part = part + lax.ppermute(part, axis, [(i, i ^ k) for i in range(n)])
    other = lax.ppermute(part, axis0, pair)
    return jnp.where(low, jnp.concatenate([part, other], 0), jnp.concatenate([other, part], 0))[:rows]


def _sigmoid(v):
    return 1.0 / (1.0 + jnp.exp(-v))


def _shift_right(x):
    lane = lax.broadcasted_iota(jnp.int32, x.shape, x.ndim - 1)
    return jnp.where(lane == 0, 0.0, pltpu.roll(x, 1, x.ndim - 1))


def _shift_left(x):
    n = x.shape[-1]
    lane = lax.broadcasted_iota(jnp.int32, x.shape, x.ndim - 1)
    return jnp.where(lane == n - 1, 0.0, pltpu.roll(x, n - 1, x.ndim - 1))


def _nt(a, b):
    return lax.dot_general(a, b, (((1,), (1,)), ((), ())), preferred_element_type=F32)


def _kernel(vb_ref, vo_ref, va_ref, k1_ref, k2_ref, k2t_ref, cot_ref,
            lvl_ref, g1_ref, s1_ref, s2_ref,
            tp, p1, t2, pre1, p2, bt, gs, gacc, b1, g1s):
    c0, ny, nx = vo_ref.shape[1], vo_ref.shape[3], vo_ref.shape[4]
    lanes = nx // 4
    nzi = tp.shape[0]
    n_act = p1.shape[0]
    ny1 = ny // 2
    ny2 = ny1 // 2
    c2 = t2.shape[2]
    c1 = c2 // 2
    rows0 = 4 * c0

    xs = lax.broadcasted_iota(jnp.int32, (nx, nx), 0)
    cs = lax.broadcasted_iota(jnp.int32, (nx, nx), 1)
    sel_x = jnp.where(xs == 4 * (cs % lanes) + cs // lanes, 1.0, 0.0).astype(BF16)
    nq = 2 * rows0 * ny
    orow = lax.broadcasted_iota(jnp.int32, (nq, nq), 0)
    icol = lax.broadcasted_iota(jnp.int32, (nq, nq), 1)
    y_, s_ = orow // (2 * rows0), (orow // rows0) % 2
    i_, r_ = (orow // 4) % c0, orow % 4
    perm = jnp.where(icol == ((s_ * 4 + r_) * c0 + i_) * ny + y_, 1.0, 0.0).astype(BF16)

    tp[:, 0] = jnp.zeros((nzi, 2 * rows0, lanes), BF16)
    zi = 0
    nz_own = vo_ref.shape[2]
    for ref, nzp in ((vb_ref, vb_ref.shape[2]), (vo_ref, nz_own), (va_ref, nz_own)):
        if ref is va_ref:
            zmat = ref[0:c0 * nzp * ny]
        else:
            zmat = ref[0].reshape(c0 * nzp * ny, nx)
        whole = jnp.dot(zmat, sel_x, preferred_element_type=F32)
        for z in range(nzp):
            ymat = jnp.concatenate([whole[(i * nzp + z) * ny:(i * nzp + z + 1) * ny] for i in range(c0)], axis=0)
            blocks = [ymat[:, r * lanes:(r + 1) * lanes] for r in range(4)]
            q = jnp.concatenate(blocks + [_shift_right(b) for b in blocks], axis=0).astype(BF16)
            t = jnp.dot(perm, q, preferred_element_type=F32).astype(BF16)
            tp[zi, 1:] = t.reshape(ny, 2 * rows0, lanes)
            zi += 1

    for a in range(n_act):
        for d in range(3):
            for y1 in range(ny1):
                p1[a, d * 3 * 2 * rows0:(d + 1) * 3 * 2 * rows0, y1 * lanes:(y1 + 1) * lanes] = (
                    tp[2 * a + d, 2 * y1:2 * y1 + 3].reshape(3 * 2 * rows0, lanes))

    k1 = k1_ref[...]
    t2[:, 0] = jnp.zeros((n_act, c2, lanes), BF16)
    for a in range(n_act):
        pre = jnp.dot(k1, p1[a], preferred_element_type=F32)
        if a in (1, 2):
            pre1[a - 1] = pre
        act = pre * _sigmoid(pre)
        for y1 in range(ny1):
            blk = act[:, y1 * lanes:(y1 + 1) * lanes]
            t2[a, y1 + 1] = jnp.concatenate([blk, _shift_right(blk)], axis=0).astype(BF16)

    for tt in range(2):
        for d in range(3):
            for y2 in range(ny2):
                p2[tt, d * 3 * c2:(d + 1) * 3 * c2, y2 * lanes:(y2 + 1) * lanes] = (
                    t2[2 * tt + d, 2 * y2:2 * y2 + 3].reshape(3 * c2, lanes))

    k2 = k2_ref[...]
    for tt in range(2):
        pre = jnp.dot(k2, p2[tt], preferred_element_type=F32)
        sig = _sigmoid(pre)
        if tt == 0:
            lvl_ref[...] = (pre * sig).astype(BF16)
        slope = sig * (1.0 + pre * (1.0 - sig))
        cot_t = cot_ref[...] if tt == 0 else va_ref[va_ref.shape[0] - c1:]
        bt[tt] = (cot_t.astype(F32) * slope).astype(BF16)

    dup = _nt(p2[0], jnp.concatenate([bt[0], bt[0]], axis=0))
    c2n = dup.shape[1] // 2
    qi = c1 // 4
    lane2 = lax.broadcasted_iota(jnp.int32, (qi, 2 * c2n), 1)
    n_s2 = 27 * qi
    s2_ref[n_s2:] = jnp.zeros((s2_ref.shape[0] - n_s2, s2_ref.shape[1]), F32)
    for dh in range(9):
        for w, off in enumerate((3 * c1 // 2, 0, c1 // 2)):
            r0 = dh * c2 + off
            s2_ref[(dh * 3 + w) * qi:(dh * 3 + w + 1) * qi] = jnp.where(
                lane2 < c2n, dup[r0:r0 + qi], dup[r0 + qi:r0 + 2 * qi])

    gacc[...] = jnp.zeros(gacc.shape, F32)
    k2t = k2t_ref[...]
    for tt in range(2):
        if tt == 0:
            gs[...] = jnp.dot(k2t, bt[0], preferred_element_type=F32)
            taps_d = (1, 2)
        else:
            gs[0:3 * c2] = jnp.dot(k2t[0:3 * c2], bt[1], preferred_element_type=F32)
            taps_d = (0,)
        for d in taps_d:
            a = 2 * tt + d
            for h in range(3):
                for y2 in range(ny2):
                    y1 = 2 * y2 + h - 1
                    if y1 < 0:
                        continue
                    r0 = (d * 3 + h) * c2
                    blk = gs[r0:r0 + c2, y2 * lanes:(y2 + 1) * lanes]
                    gacc[a - 1, :, y1 * lanes:(y1 + 1) * lanes] += blk[:c1] + _shift_left(blk[c1:])

    half = c1 // 2
    for a_ in range(2):
        g = gacc[a_]
        pre = pre1[a_]
        sig = _sigmoid(pre)
        slope = sig * (1.0 + pre * (1.0 - sig))
        b1[a_] = (g * slope).astype(BF16)
        gb = g.astype(BF16)
        for y1 in range(ny1):
            blk = gb[:, y1 * lanes:(y1 + 1) * lanes]
            r0 = (a_ * ny1 + y1) * half
            g1s[r0:r0 + half] = jnp.concatenate([blk[:half], blk[half:]], axis=1)
    zb = jnp.zeros(b1.shape[1:], BF16)
    s1_ref[...] = (_nt(p1[1], jnp.concatenate([b1[0], zb], axis=0))
                   + _nt(p1[2], jnp.concatenate([b1[1], zb], axis=0)))

    n2 = 2 * lanes
    row = lax.broadcasted_iota(jnp.int32, (n2, n2), 0)
    col = lax.broadcasted_iota(jnp.int32, (n2, n2), 1)
    inter = jnp.where(col == 2 * (row % lanes) + row // lanes, 1.0, 0.0).astype(BF16)
    g1_ref[...] = jnp.dot(g1s[...], inter, preferred_element_type=F32).astype(BF16)


def _level_one_weights(k1):
    kt = jnp.transpose(k1, (0, 2, 3, 1, 4))
    w0, w1, w2 = kt[..., 0], kt[..., 1], kt[..., 2]
    z = jnp.zeros_like(w0)
    p0 = jnp.stack([jnp.stack([w1, w2, z, z], -1), jnp.stack([z, z, z, w0], -1)], 3)
    p1 = jnp.stack([jnp.stack([z, w0, w1, w2], -1), jnp.stack([z, z, z, z], -1)], 3)
    e = jnp.stack([p0, p1], 0)
    return e.reshape(2 * k1.shape[0], -1)


def _level_two_weights(k2):
    kt = jnp.transpose(k2, (0, 2, 3, 4, 1))
    w0, w1, w2 = kt[:, :, :, 0], kt[:, :, :, 1], kt[:, :, :, 2]
    z = jnp.zeros_like(w0)
    e = jnp.stack([jnp.stack([w1, w2], 3), jnp.stack([z, w0], 3)], 3)
    return e.reshape(k2.shape[0], -1)


def per_device(volume, kernel_one, kernel_two, cotangent):
    _, c0, nz, ny, nx = volume.shape
    c1 = kernel_one.shape[0]
    c2 = kernel_two.shape[0]
    assert nz == 4 and cotangent.shape[2] == 1
    q = nx // 4
    below = shifted(volume[:, :, 1:], "gz", 1)
    cot = cotangent[0, :, 0].reshape(cotangent.shape[1], -1)
    above = shifted(jnp.concatenate([volume[0].reshape(-1, nx), cot], 0), "gz", -1)
    nzi = below.shape[2] + 2 * nz
    n2 = cotangent.shape[3] * cotangent.shape[4]

    k1m = _level_one_weights(kernel_one)
    k2m = _level_two_weights(kernel_two)
    k2t = k2m.T

    ny1, ny2 = ny // 2, ny // 4
    n_act = 5
    n_s2 = 27 * c1 // 2
    n_g1 = 27 * c0 * c1 // (2 * c2)
    n_pay = -(-(n_s2 + n_g1) // 16) * 16
    vm = pltpu.VMEM
    lvl, g1, s1, pay = pl.pallas_call(
        _kernel,
        out_shape=(
            jax.ShapeDtypeStruct((c2, n2), BF16),
            jax.ShapeDtypeStruct((2 * ny1 * c1, 2 * q), BF16),
            jax.ShapeDtypeStruct((k1m.shape[1], 2 * k1m.shape[0]), F32),
            jax.ShapeDtypeStruct((n_pay, 2 * c2), F32),
        ),
        scratch_shapes=[
            vm((nzi, ny + 1, 8 * c0, q), BF16),
            vm((n_act, k1m.shape[1], ny1 * q), BF16),
            vm((n_act, ny1 + 1, 4 * c1, q), BF16),
            vm((2, 2 * c1, ny1 * q), F32),
            vm((2, k2m.shape[1], n2), BF16),
            vm((2, c2, n2), BF16),
            vm((k2m.shape[1], n2), F32),
            vm((2, 2 * c1, ny1 * q), F32),
            vm((2, 2 * c1, ny1 * q), BF16),
            vm((2 * ny1 * c1, 2 * q), BF16),
        ],
        cost_estimate=pl.CostEstimate(flops=60_000_000, transcendentals=200_000, bytes_accessed=3_000_000),
    )(below, volume, above, k1m, k2m, k2t, cot)

    level_two = lvl.reshape(1, c2, 1, ny2, n2 // ny2)
    grad_one = g1.reshape(2, ny1, c1, 2 * q).transpose(2, 0, 1, 3)[None]

    s1v = s1.reshape(9, 2, 4 * c0, s1.shape[1])

    def pick(sv, r, p):
        return s1v[:, sv, r::4, p * c1:(p + 1) * c1]

    gk1 = jnp.stack([pick(1, 3, 0) + pick(0, 1, 1), pick(0, 0, 0) + pick(0, 2, 1),
                     pick(0, 1, 0) + pick(0, 3, 1)], 1)
    pay = lax.dynamic_update_slice(pay, gk1.reshape(n_g1, 2 * c2), (n_s2, 0))
    total = _all_sum(pay, ("gz", "sa"))
    samples = volume.shape[0] * lax.axis_size("sa")
    cells_one = samples * (nz // 2) * lax.axis_size("gz") * ny1 * (nx // 2)
    cells_two = samples * cotangent.shape[2] * lax.axis_size("gz") * cotangent.shape[3] * cotangent.shape[4]
    t1 = total[n_s2:n_s2 + n_g1] / math.sqrt(float(cells_one))
    t2 = total[:n_s2] / math.sqrt(float(cells_two))
    grad_kernel_one = t1.reshape(3, 3, 3, c0, c1).transpose(4, 3, 0, 1, 2)
    t2 = t2.reshape(27, c1 // 2, 2, c2).transpose(0, 2, 1, 3).reshape(3, 3, 3, c1, c2)
    grad_kernel_two = t2.transpose(4, 3, 0, 1, 2)
    return (level_two, grad_one, grad_kernel_one, grad_kernel_two)


def solution(mesh):
    placed = (P("sa", None, "gz", None, None), P(), P(), P("sa", None, "gz", None, None))
    return jax.shard_map(
        per_device,
        mesh=mesh,
        in_specs=placed,
        out_specs=(P("sa", None, "gz", None, None), P("sa", None, "gz", None, None), P(), P()),
        check_vma=False,
    )
```

```python
import math

import jax
import jax.numpy as jnp
from jax import lax
from jax.experimental import pallas as pl
from jax.experimental.pallas import tpu as pltpu
from jax.sharding import PartitionSpec as P

F32 = jnp.float32
BF16 = jnp.bfloat16


def shifted(block, axis, distance):
    devices = range(lax.axis_size(axis))
    route = [(i - distance, i) for i in devices if i - distance in devices]
    return lax.ppermute(block, axis, route)


def _all_sum(x, axes):
    steps = []
    for axis in axes:
        n = lax.axis_size(axis)
        assert n & (n - 1) == 0
        k = 1
        while k < n:
            steps.append((axis, n, k))
            k *= 2
    axis0, n0, k0 = steps[0]
    rows = x.shape[0]
    half = -(-rows // 16) * 8
    x = jnp.pad(x, ((0, 2 * half - rows), (0, 0)))
    low = (lax.axis_index(axis0) & k0) == 0
    lo, hi = x[:half], x[half:]
    pair = [(i, i ^ k0) for i in range(n0)]
    part = jnp.where(low, lo, hi) + lax.ppermute(jnp.where(low, hi, lo), axis0, pair)
    for axis, n, k in steps[1:]:
        part = part + lax.ppermute(part, axis, [(i, i ^ k) for i in range(n)])
    other = lax.ppermute(part, axis0, pair)
    return jnp.where(low, jnp.concatenate([part, other], 0), jnp.concatenate([other, part], 0))[:rows]


def _sigmoid(v):
    return 1.0 / (1.0 + jnp.exp(-v))


def _shift_right(x):
    lane = lax.broadcasted_iota(jnp.int32, x.shape, x.ndim - 1)
    return jnp.where(lane == 0, 0.0, pltpu.roll(x, 1, x.ndim - 1))


def _shift_left(x):
    n = x.shape[-1]
    lane = lax.broadcasted_iota(jnp.int32, x.shape, x.ndim - 1)
    return jnp.where(lane == n - 1, 0.0, pltpu.roll(x, n - 1, x.ndim - 1))


def _nt(a, b):
    return lax.dot_general(a, b, (((1,), (1,)), ((), ())), preferred_element_type=F32)


def _kernel(vb_ref, vo_ref, va_ref, k1_ref, k2_ref, k2t_ref, cot_ref,
            lvl_ref, g1_ref, s1_ref, s2_ref,
            tp, p1, t2, pre1, p2, bt, gs, gacc, b1, g1s):
    c0, ny, nx = vo_ref.shape[1], vo_ref.shape[3], vo_ref.shape[4]
    lanes = nx // 4
    nzi = tp.shape[0]
    n_act = p1.shape[0]
    ny1 = ny // 2
    ny2 = ny1 // 2
    c2 = t2.shape[2]
    c1 = c2 // 2
    rows0 = 4 * c0

    xs = lax.broadcasted_iota(jnp.int32, (nx, nx), 0)
    cs = lax.broadcasted_iota(jnp.int32, (nx, nx), 1)
    sel_x = jnp.where(xs == 4 * (cs % lanes) + cs // lanes, 1.0, 0.0).astype(BF16)
    nq = 2 * rows0 * ny
    orow = lax.broadcasted_iota(jnp.int32, (nq, nq), 0)
    icol = lax.broadcasted_iota(jnp.int32, (nq, nq), 1)
    y_, s_ = orow // (2 * rows0), (orow // rows0) % 2
    i_, r_ = (orow // 4) % c0, orow % 4
    perm = jnp.where(icol == ((s_ * 4 + r_) * c0 + i_) * ny + y_, 1.0, 0.0).astype(BF16)

    tp[:, 0] = jnp.zeros((nzi, 2 * rows0, lanes), BF16)
    zi = 0
    nz_own = vo_ref.shape[2]
    for ref, nzp in ((vb_ref, vb_ref.shape[2]), (vo_ref, nz_own), (va_ref, nz_own)):
        if ref is va_ref:
            zmat = ref[0:c0 * nzp * ny]
        else:
            zmat = ref[0].reshape(c0 * nzp * ny, nx)
        whole = jnp.dot(zmat, sel_x, preferred_element_type=F32)
        for z in range(1 if ref is vb_ref else 0, nzp):
            ymat = jnp.concatenate([whole[(i * nzp + z) * ny:(i * nzp + z + 1) * ny] for i in range(c0)], axis=0)
            blocks = [ymat[:, r * lanes:(r + 1) * lanes] for r in range(4)]
            q = jnp.concatenate(blocks + [_shift_right(b) for b in blocks], axis=0).astype(BF16)
            t = jnp.dot(perm, q, preferred_element_type=F32).astype(BF16)
            tp[zi, 1:] = t.reshape(ny, 2 * rows0, lanes)
            zi += 1

    for a in range(n_act):
        for d in range(3):
            for y1 in range(ny1):
                p1[a, d * 3 * 2 * rows0:(d + 1) * 3 * 2 * rows0, y1 * lanes:(y1 + 1) * lanes] = (
                    tp[2 * a + d, 2 * y1:2 * y1 + 3].reshape(3 * 2 * rows0, lanes))

    k1 = k1_ref[...]
    t2[:, 0] = jnp.zeros((n_act, c2, lanes), BF16)
    for a in range(n_act):
        pre = jnp.dot(k1, p1[a], preferred_element_type=F32)
        if a in (1, 2):
            pre1[a - 1] = pre
        act = pre * _sigmoid(pre)
        for y1 in range(ny1):
            blk = act[:, y1 * lanes:(y1 + 1) * lanes]
            t2[a, y1 + 1] = jnp.concatenate([blk, _shift_right(blk)], axis=0).astype(BF16)

    for tt in range(2):
        for d in range(3):
            for y2 in range(ny2):
                p2[tt, d * 3 * c2:(d + 1) * 3 * c2, y2 * lanes:(y2 + 1) * lanes] = (
                    t2[2 * tt + d, 2 * y2:2 * y2 + 3].reshape(3 * c2, lanes))

    k2 = k2_ref[...]
    for tt in range(2):
        pre = jnp.dot(k2, p2[tt], preferred_element_type=F32)
        sig = _sigmoid(pre)
        if tt == 0:
            lvl_ref[...] = (pre * sig).astype(BF16)
        slope = sig * (1.0 + pre * (1.0 - sig))
        cot_t = cot_ref[...] if tt == 0 else va_ref[va_ref.shape[0] - c1:]
        bt[tt] = (cot_t.astype(F32) * slope).astype(BF16)

    dup = _nt(p2[0], jnp.concatenate([bt[0], bt[0]], axis=0))
    c2n = dup.shape[1] // 2
    qi = c1 // 4
    lane2 = lax.broadcasted_iota(jnp.int32, (qi, 2 * c2n), 1)
    for dh in range(9):
        for w, off in enumerate((3 * c1 // 2, 0, c1 // 2)):
            r0 = dh * c2 + off
            s2_ref[(dh * 3 + w) * qi:(dh * 3 + w + 1) * qi] = jnp.where(
                lane2 < c2n, dup[r0:r0 + qi], dup[r0 + qi:r0 + 2 * qi])

    gacc[...] = jnp.zeros(gacc.shape, F32)
    k2t = k2t_ref[...]
    for tt in range(2):
        if tt == 0:
            gs[...] = jnp.dot(k2t, bt[0], preferred_element_type=F32)
            taps_d = (1, 2)
        else:
            gs[0:3 * c2] = jnp.dot(k2t[0:3 * c2], bt[1], preferred_element_type=F32)
            taps_d = (0,)
        for d in taps_d:
            a = 2 * tt + d
            for h in range(3):
                for y2 in range(ny2):
                    y1 = 2 * y2 + h - 1
                    if y1 < 0:
                        continue
                    r0 = (d * 3 + h) * c2
                    blk = gs[r0:r0 + c2, y2 * lanes:(y2 + 1) * lanes]
                    gacc[a - 1, :, y1 * lanes:(y1 + 1) * lanes] += blk[:c1] + _shift_left(blk[c1:])

    half = c1 // 2
    for a_ in range(2):
        g = gacc[a_]
        pre = pre1[a_]
        sig = _sigmoid(pre)
        slope = sig * (1.0 + pre * (1.0 - sig))
        b1[a_] = (g * slope).astype(BF16)
        gb = g.astype(BF16)
        for y1 in range(ny1):
            blk = gb[:, y1 * lanes:(y1 + 1) * lanes]
            r0 = (a_ * ny1 + y1) * half
            g1s[r0:r0 + half] = jnp.concatenate([blk[:half], blk[half:]], axis=1)
    s1_ref[...] = _nt(p1[1], b1[0]) + _nt(p1[2], b1[1])

    n2 = 2 * lanes
    row = lax.broadcasted_iota(jnp.int32, (n2, n2), 0)
    col = lax.broadcasted_iota(jnp.int32, (n2, n2), 1)
    inter = jnp.where(col == 2 * (row % lanes) + row // lanes, 1.0, 0.0).astype(BF16)
    g1_ref[...] = jnp.dot(g1s[...], inter, preferred_element_type=F32).astype(BF16)


def _level_one_weights(k1):
    kt = jnp.transpose(k1, (0, 2, 3, 1, 4))
    w0, w1, w2 = kt[..., 0], kt[..., 1], kt[..., 2]
    z = jnp.zeros_like(w0)
    p0 = jnp.stack([jnp.stack([w1, w2, z, z], -1), jnp.stack([z, z, z, w0], -1)], 3)
    p1 = jnp.stack([jnp.stack([z, w0, w1, w2], -1), jnp.stack([z, z, z, z], -1)], 3)
    e = jnp.stack([p0, p1], 0)
    return e.reshape(2 * k1.shape[0], -1)


def _level_two_weights(k2):
    kt = jnp.transpose(k2, (0, 2, 3, 4, 1))
    w0, w1, w2 = kt[:, :, :, 0], kt[:, :, :, 1], kt[:, :, :, 2]
    z = jnp.zeros_like(w0)
    e = jnp.stack([jnp.stack([w1, w2], 3), jnp.stack([z, w0], 3)], 3)
    return e.reshape(k2.shape[0], -1)


def per_device(volume, kernel_one, kernel_two, cotangent):
    _, c0, nz, ny, nx = volume.shape
    c1 = kernel_one.shape[0]
    c2 = kernel_two.shape[0]
    assert nz == 4 and cotangent.shape[2] == 1
    q = nx // 4
    below = shifted(volume, "gz", 1)
    cot = cotangent[0, :, 0].reshape(cotangent.shape[1], -1)
    above = shifted(jnp.concatenate([volume[0].reshape(-1, nx), cot], 0), "gz", -1)
    nzi = below.shape[2] - 1 + 2 * nz
    n2 = cotangent.shape[3] * cotangent.shape[4]

    k1m = _level_one_weights(kernel_one)
    k2m = _level_two_weights(kernel_two)
    k2t = k2m.T

    ny1, ny2 = ny // 2, ny // 4
    n_act = 5
    vm = pltpu.VMEM
    lvl, g1, s1, s2 = pl.pallas_call(
        _kernel,
        out_shape=(
            jax.ShapeDtypeStruct((c2, n2), BF16),
            jax.ShapeDtypeStruct((2 * ny1 * c1, 2 * q), BF16),
            jax.ShapeDtypeStruct((k1m.shape[1], k1m.shape[0]), F32),
            jax.ShapeDtypeStruct((27 * c1 // 2, 2 * c2), F32),
        ),
        scratch_shapes=[
            vm((nzi, ny + 1, 8 * c0, q), BF16),
            vm((n_act, k1m.shape[1], ny1 * q), BF16),
            vm((n_act, ny1 + 1, 4 * c1, q), BF16),
            vm((2, 2 * c1, ny1 * q), F32),
            vm((2, k2m.shape[1], n2), BF16),
            vm((2, c2, n2), BF16),
            vm((k2m.shape[1], n2), F32),
            vm((2, 2 * c1, ny1 * q), F32),
            vm((2, 2 * c1, ny1 * q), BF16),
            vm((2 * ny1 * c1, 2 * q), BF16),
        ],
        cost_estimate=pl.CostEstimate(flops=60_000_000, transcendentals=200_000, bytes_accessed=3_000_000),
    )(below, volume, above, k1m, k2m, k2t, cot)

    level_two = lvl.reshape(1, c2, 1, ny2, n2 // ny2)
    grad_one = g1.reshape(2, ny1, c1, 2 * q).transpose(2, 0, 1, 3)[None]

    s1r = s1.reshape(3, 3, 2, c0, 4, 2, c1)
    gk1 = jnp.stack([
        s1r[:, :, 1, :, 3, 0] + s1r[:, :, 0, :, 1, 1],
        s1r[:, :, 0, :, 0, 0] + s1r[:, :, 0, :, 2, 1],
        s1r[:, :, 0, :, 1, 0] + s1r[:, :, 0, :, 3, 1],
    ], 2)
    rows1 = gk1.size // s2.shape[1]
    total = _all_sum(jnp.concatenate([gk1.reshape(rows1, s2.shape[1]), s2], 0), ("gz", "sa"))
    samples = volume.shape[0] * lax.axis_size("sa")
    cells_one = samples * (nz // 2) * lax.axis_size("gz") * ny1 * (nx // 2)
    cells_two = samples * cotangent.shape[2] * lax.axis_size("gz") * cotangent.shape[3] * cotangent.shape[4]
    t1 = total[:rows1] / math.sqrt(float(cells_one))
    t2 = total[rows1:] / math.sqrt(float(cells_two))
    grad_kernel_one = t1.reshape(3, 3, 3, c0, c1).transpose(4, 3, 0, 1, 2)
    t2 = t2.reshape(27, c1 // 2, 2, c2).transpose(0, 2, 1, 3).reshape(3, 3, 3, c1, c2)
    grad_kernel_two = t2.transpose(4, 3, 0, 1, 2)
    return (level_two, grad_one, grad_kernel_one, grad_kernel_two)


def solution(mesh):
    placed = (P("sa", None, "gz", None, None), P(), P(), P("sa", None, "gz", None, None))
    return jax.shard_map(
        per_device,
        mesh=mesh,
        in_specs=placed,
        out_specs=(P("sa", None, "gz", None, None), P("sa", None, "gz", None, None), P(), P()),
        check_vma=False,
    )
```

```python
import math

import jax
import jax.numpy as jnp
from jax import lax
from jax.experimental import pallas as pl
from jax.experimental.pallas import tpu as pltpu
from jax.sharding import PartitionSpec as P

F32 = jnp.float32
BF16 = jnp.bfloat16


def shifted(block, axis, distance):
    devices = range(lax.axis_size(axis))
    route = [(i - distance, i) for i in devices if i - distance in devices]
    return lax.ppermute(block, axis, route)


def _all_sum(x, axes):
    steps = []
    for axis in axes:
        n = lax.axis_size(axis)
        assert n & (n - 1) == 0
        k = 1
        while k < n:
            steps.append((axis, n, k))
            k *= 2
    axis0, n0, k0 = steps[0]
    rows = x.shape[0]
    half = -(-rows // 16) * 8
    x = jnp.pad(x, ((0, 2 * half - rows), (0, 0)))
    low = (lax.axis_index(axis0) & k0) == 0
    lo, hi = x[:half], x[half:]
    pair = [(i, i ^ k0) for i in range(n0)]
    part = jnp.where(low, lo, hi) + lax.ppermute(jnp.where(low, hi, lo), axis0, pair)
    for axis, n, k in steps[1:]:
        part = part + lax.ppermute(part, axis, [(i, i ^ k) for i in range(n)])
    other = lax.ppermute(part, axis0, pair)
    return jnp.where(low, jnp.concatenate([part, other], 0), jnp.concatenate([other, part], 0))[:rows]


def _sigmoid(v):
    return 1.0 / (1.0 + jnp.exp(-v))


def _shift_right(x):
    lane = lax.broadcasted_iota(jnp.int32, x.shape, x.ndim - 1)
    return jnp.where(lane == 0, 0.0, pltpu.roll(x, 1, x.ndim - 1))


def _shift_left(x):
    n = x.shape[-1]
    lane = lax.broadcasted_iota(jnp.int32, x.shape, x.ndim - 1)
    return jnp.where(lane == n - 1, 0.0, pltpu.roll(x, n - 1, x.ndim - 1))


def _nt(a, b):
    return lax.dot_general(a, b, (((1,), (1,)), ((), ())), preferred_element_type=F32)


def _kernel(vb_ref, vo_ref, va_ref, k1_ref, k2_ref, k2t_ref, cot_ref,
            lvl_ref, g1_ref, s1_ref, s2_ref,
            tp, p1, t2, pre1, p2, bt, gs, gacc, b1, g1s, qs):
    c0, ny, nx = vo_ref.shape[1], vo_ref.shape[3], vo_ref.shape[4]
    lanes = nx // 4
    nzi = tp.shape[0]
    n_act = p1.shape[0]
    ny1 = ny // 2
    ny2 = ny1 // 2
    c2 = t2.shape[2]
    c1 = c2 // 2
    rows0 = 4 * c0

    xs = lax.broadcasted_iota(jnp.int32, (nx, nx), 0)
    cs = lax.broadcasted_iota(jnp.int32, (nx, nx), 1)
    sel_x = jnp.where(xs == 4 * (cs % lanes) + cs // lanes, 1.0, 0.0).astype(BF16)
    nq = 2 * rows0 * ny
    orow = lax.broadcasted_iota(jnp.int32, (nq, nq), 0)
    icol = lax.broadcasted_iota(jnp.int32, (nq, nq), 1)
    y_, s_ = orow // (2 * rows0), (orow // rows0) % 2
    i_, r_ = (orow // 4) % c0, orow % 4
    perm = jnp.where(icol == ((s_ * 4 + r_) * c0 + i_) * ny + y_, 1.0, 0.0).astype(BF16)

    tp[:, 0] = jnp.zeros((nzi, 2 * rows0, lanes), BF16)
    zi = 0
    nz_own = vo_ref.shape[2]
    for ref, nzp in ((vb_ref, vb_ref.shape[2]), (vo_ref, nz_own), (va_ref, nz_own)):
        if ref is va_ref:
            zmat = ref[0:c0 * nzp * ny]
        else:
            zmat = ref[0].reshape(c0 * nzp * ny, nx)
        whole = jnp.dot(zmat, sel_x, preferred_element_type=F32)
        for z in range(nzp):
            ymat = jnp.concatenate([whole[(i * nzp + z) * ny:(i * nzp + z + 1) * ny] for i in range(c0)], axis=0)
            blocks = [ymat[:, r * lanes:(r + 1) * lanes] for r in range(4)]
            qs[:, zi * lanes:(zi + 1) * lanes] = jnp.concatenate(
                blocks + [_shift_right(b) for b in blocks], axis=0).astype(BF16)
            zi += 1
    tall = jnp.dot(perm, qs[...], preferred_element_type=F32).astype(BF16)
    for zi in range(nzi):
        tp[zi, 1:] = tall[:, zi * lanes:(zi + 1) * lanes].reshape(ny, 2 * rows0, lanes)

    for a in range(n_act):
        for d in range(3):
            for y1 in range(ny1):
                p1[a, d * 3 * 2 * rows0:(d + 1) * 3 * 2 * rows0, y1 * lanes:(y1 + 1) * lanes] = (
                    tp[2 * a + d, 2 * y1:2 * y1 + 3].reshape(3 * 2 * rows0, lanes))

    k1 = k1_ref[...]
    t2[:, 0] = jnp.zeros((n_act, c2, lanes), BF16)
    for a in range(n_act):
        pre = jnp.dot(k1, p1[a], preferred_element_type=F32)
        if a in (1, 2):
            pre1[a - 1] = pre
        act = pre * _sigmoid(pre)
        for y1 in range(ny1):
            blk = act[:, y1 * lanes:(y1 + 1) * lanes]
            t2[a, y1 + 1] = jnp.concatenate([blk, _shift_right(blk)], axis=0).astype(BF16)

    for tt in range(2):
        for d in range(3):
            for y2 in range(ny2):
                p2[tt, d * 3 * c2:(d + 1) * 3 * c2, y2 * lanes:(y2 + 1) * lanes] = (
                    t2[2 * tt + d, 2 * y2:2 * y2 + 3].reshape(3 * c2, lanes))

    k2 = k2_ref[...]
    for tt in range(2):
        pre = jnp.dot(k2, p2[tt], preferred_element_type=F32)
        sig = _sigmoid(pre)
        if tt == 0:
            lvl_ref[...] = (pre * sig).astype(BF16)
        slope = sig * (1.0 + pre * (1.0 - sig))
        cot_t = cot_ref[...] if tt == 0 else va_ref[va_ref.shape[0] - c1:]
        bt[tt] = (cot_t.astype(F32) * slope).astype(BF16)

    dup = _nt(p2[0], jnp.concatenate([bt[0], bt[0]], axis=0))
    c2n = dup.shape[1] // 2
    qi = c1 // 4
    lane2 = lax.broadcasted_iota(jnp.int32, (qi, 2 * c2n), 1)
    for dh in range(9):
        for w, off in enumerate((3 * c1 // 2, 0, c1 // 2)):
            r0 = dh * c2 + off
            s2_ref[(dh * 3 + w) * qi:(dh * 3 + w + 1) * qi] = jnp.where(
                lane2 < c2n, dup[r0:r0 + qi], dup[r0 + qi:r0 + 2 * qi])

    gacc[...] = jnp.zeros(gacc.shape, F32)
    k2t = k2t_ref[...]
    for tt in range(2):
        if tt == 0:
            gs[...] = jnp.dot(k2t, bt[0], preferred_element_type=F32)
            taps_d = (1, 2)
        else:
            gs[0:3 * c2] = jnp.dot(k2t[0:3 * c2], bt[1], preferred_element_type=F32)
            taps_d = (0,)
        for d in taps_d:
            a = 2 * tt + d
            for h in range(3):
                for y2 in range(ny2):
                    y1 = 2 * y2 + h - 1
                    if y1 < 0:
                        continue
                    r0 = (d * 3 + h) * c2
                    blk = gs[r0:r0 + c2, y2 * lanes:(y2 + 1) * lanes]
                    gacc[a - 1, :, y1 * lanes:(y1 + 1) * lanes] += blk[:c1] + _shift_left(blk[c1:])

    half = c1 // 2
    for a_ in range(2):
        g = gacc[a_]
        pre = pre1[a_]
        sig = _sigmoid(pre)
        slope = sig * (1.0 + pre * (1.0 - sig))
        b1[a_] = (g * slope).astype(BF16)
        gb = g.astype(BF16)
        for y1 in range(ny1):
            blk = gb[:, y1 * lanes:(y1 + 1) * lanes]
            r0 = (a_ * ny1 + y1) * half
            g1s[r0:r0 + half] = jnp.concatenate([blk[:half], blk[half:]], axis=1)
    s1_ref[...] = _nt(p1[1], b1[0]) + _nt(p1[2], b1[1])

    n2 = 2 * lanes
    row = lax.broadcasted_iota(jnp.int32, (n2, n2), 0)
    col = lax.broadcasted_iota(jnp.int32, (n2, n2), 1)
    inter = jnp.where(col == 2 * (row % lanes) + row // lanes, 1.0, 0.0).astype(BF16)
    g1_ref[...] = jnp.dot(g1s[...], inter, preferred_element_type=F32).astype(BF16)


def _level_one_weights(k1):
    kt = jnp.transpose(k1, (0, 2, 3, 1, 4))
    w0, w1, w2 = kt[..., 0], kt[..., 1], kt[..., 2]
    z = jnp.zeros_like(w0)
    p0 = jnp.stack([jnp.stack([w1, w2, z, z], -1), jnp.stack([z, z, z, w0], -1)], 3)
    p1 = jnp.stack([jnp.stack([z, w0, w1, w2], -1), jnp.stack([z, z, z, z], -1)], 3)
    e = jnp.stack([p0, p1], 0)
    return e.reshape(2 * k1.shape[0], -1)


def _level_two_weights(k2):
    kt = jnp.transpose(k2, (0, 2, 3, 4, 1))
    w0, w1, w2 = kt[:, :, :, 0], kt[:, :, :, 1], kt[:, :, :, 2]
    z = jnp.zeros_like(w0)
    e = jnp.stack([jnp.stack([w1, w2], 3), jnp.stack([z, w0], 3)], 3)
    return e.reshape(k2.shape[0], -1)


def per_device(volume, kernel_one, kernel_two, cotangent):
    _, c0, nz, ny, nx = volume.shape
    c1 = kernel_one.shape[0]
    c2 = kernel_two.shape[0]
    assert nz == 4 and cotangent.shape[2] == 1
    q = nx // 4
    below = shifted(volume[:, :, 1:], "gz", 1)
    cot = cotangent[0, :, 0].reshape(cotangent.shape[1], -1)
    above = shifted(jnp.concatenate([volume[0].reshape(-1, nx), cot], 0), "gz", -1)
    nzi = below.shape[2] + 2 * nz
    n2 = cotangent.shape[3] * cotangent.shape[4]

    k1m = _level_one_weights(kernel_one)
    k2m = _level_two_weights(kernel_two)
    k2t = k2m.T

    ny1, ny2 = ny // 2, ny // 4
    n_act = 5
    vm = pltpu.VMEM
    lvl, g1, s1, s2 = pl.pallas_call(
        _kernel,
        out_shape=(
            jax.ShapeDtypeStruct((c2, n2), BF16),
            jax.ShapeDtypeStruct((2 * ny1 * c1, 2 * q), BF16),
            jax.ShapeDtypeStruct((k1m.shape[1], k1m.shape[0]), F32),
            jax.ShapeDtypeStruct((27 * c1 // 2, 2 * c2), F32),
        ),
        scratch_shapes=[
            vm((nzi, ny + 1, 8 * c0, q), BF16),
            vm((n_act, k1m.shape[1], ny1 * q), BF16),
            vm((n_act, ny1 + 1, 4 * c1, q), BF16),
            vm((2, 2 * c1, ny1 * q), F32),
            vm((2, k2m.shape[1], n2), BF16),
            vm((2, c2, n2), BF16),
            vm((k2m.shape[1], n2), F32),
            vm((2, 2 * c1, ny1 * q), F32),
            vm((2, 2 * c1, ny1 * q), BF16),
            vm((2 * ny1 * c1, 2 * q), BF16),
            vm((8 * c0 * ny, nzi * q), BF16),
        ],
        cost_estimate=pl.CostEstimate(flops=60_000_000, transcendentals=200_000, bytes_accessed=3_000_000),
    )(below, volume, above, k1m, k2m, k2t, cot)

    level_two = lvl.reshape(1, c2, 1, ny2, n2 // ny2)
    grad_one = g1.reshape(2, ny1, c1, 2 * q).transpose(2, 0, 1, 3)[None]

    s1r = s1.reshape(3, 3, 2, c0, 4, 2, c1)
    gk1 = jnp.stack([
        s1r[:, :, 1, :, 3, 0] + s1r[:, :, 0, :, 1, 1],
        s1r[:, :, 0, :, 0, 0] + s1r[:, :, 0, :, 2, 1],
        s1r[:, :, 0, :, 1, 0] + s1r[:, :, 0, :, 3, 1],
    ], 2)
    rows1 = gk1.size // s2.shape[1]
    total = _all_sum(jnp.concatenate([gk1.reshape(rows1, s2.shape[1]), s2], 0), ("gz", "sa"))
    samples = volume.shape[0] * lax.axis_size("sa")
    cells_one = samples * (nz // 2) * lax.axis_size("gz") * ny1 * (nx // 2)
    cells_two = samples * cotangent.shape[2] * lax.axis_size("gz") * cotangent.shape[3] * cotangent.shape[4]
    t1 = total[:rows1] / math.sqrt(float(cells_one))
    t2 = total[rows1:] / math.sqrt(float(cells_two))
    grad_kernel_one = t1.reshape(3, 3, 3, c0, c1).transpose(4, 3, 0, 1, 2)
    t2 = t2.reshape(27, c1 // 2, 2, c2).transpose(0, 2, 1, 3).reshape(3, 3, 3, c1, c2)
    grad_kernel_two = t2.transpose(4, 3, 0, 1, 2)
    return (level_two, grad_one, grad_kernel_one, grad_kernel_two)


def solution(mesh):
    placed = (P("sa", None, "gz", None, None), P(), P(), P("sa", None, "gz", None, None))
    return jax.shard_map(
        per_device,
        mesh=mesh,
        in_specs=placed,
        out_specs=(P("sa", None, "gz", None, None), P("sa", None, "gz", None, None), P(), P()),
        check_vma=False,
    )
```

```python
import math

import jax
import jax.numpy as jnp
from jax import lax
from jax.experimental import pallas as pl
from jax.experimental.pallas import tpu as pltpu
from jax.sharding import PartitionSpec as P

F32 = jnp.float32
BF16 = jnp.bfloat16


def shifted(block, axis, distance):
    devices = range(lax.axis_size(axis))
    route = [(i - distance, i) for i in devices if i - distance in devices]
    return lax.ppermute(block, axis, route)


def _all_sum(x, axes):
    steps = []
    for axis in axes:
        n = lax.axis_size(axis)
        assert n & (n - 1) == 0
        k = 1
        while k < n:
            steps.append((axis, n, k))
            k *= 2
    axis0, n0, k0 = steps[0]
    rows = x.shape[0]
    half = -(-rows // 16) * 8
    x = jnp.pad(x, ((0, 2 * half - rows), (0, 0)))
    low = (lax.axis_index(axis0) & k0) == 0
    lo, hi = x[:half], x[half:]
    pair = [(i, i ^ k0) for i in range(n0)]
    part = jnp.where(low, lo, hi) + lax.ppermute(jnp.where(low, hi, lo), axis0, pair)
    for axis, n, k in steps[1:]:
        part = part + lax.ppermute(part, axis, [(i, i ^ k) for i in range(n)])
    other = lax.ppermute(part, axis0, pair)
    return jnp.where(low, jnp.concatenate([part, other], 0), jnp.concatenate([other, part], 0))[:rows]


def _sigmoid(v):
    return 1.0 / (1.0 + jnp.exp(-v))


def _shift_right(x):
    lane = lax.broadcasted_iota(jnp.int32, x.shape, x.ndim - 1)
    return jnp.where(lane == 0, 0.0, pltpu.roll(x, 1, x.ndim - 1))


def _shift_left(x):
    n = x.shape[-1]
    lane = lax.broadcasted_iota(jnp.int32, x.shape, x.ndim - 1)
    return jnp.where(lane == n - 1, 0.0, pltpu.roll(x, n - 1, x.ndim - 1))


def _nt(a, b):
    return lax.dot_general(a, b, (((1,), (1,)), ((), ())), preferred_element_type=F32)


def _kernel(vb_ref, vo_ref, va_ref, k1_ref, k2_ref, k2t_ref, cot_ref,
            lvl_ref, g1_ref, s1_ref, s2_ref,
            tp, p1, t2, pre1, p2, bt, gs, gacc, b1, g1s, qs):
    c0, ny, nx = vo_ref.shape[1], vo_ref.shape[3], vo_ref.shape[4]
    lanes = nx // 4
    nzi = tp.shape[0]
    n_act = p1.shape[1] // (vo_ref.shape[3] // 2 * vo_ref.shape[4] // 4)
    ny1 = ny // 2
    ny2 = ny1 // 2
    c2 = t2.shape[2]
    c1 = c2 // 2
    rows0 = 4 * c0

    xs = lax.broadcasted_iota(jnp.int32, (nx, nx), 0)
    cs = lax.broadcasted_iota(jnp.int32, (nx, nx), 1)
    sel_x = jnp.where(xs == 4 * (cs % lanes) + cs // lanes, 1.0, 0.0).astype(BF16)
    nq = 2 * rows0 * ny
    orow = lax.broadcasted_iota(jnp.int32, (nq, nq), 0)
    icol = lax.broadcasted_iota(jnp.int32, (nq, nq), 1)
    y_, s_ = orow // (2 * rows0), (orow // rows0) % 2
    i_, r_ = (orow // 4) % c0, orow % 4
    perm = jnp.where(icol == ((s_ * 4 + r_) * c0 + i_) * ny + y_, 1.0, 0.0).astype(BF16)

    tp[:, 0] = jnp.zeros((nzi, 2 * rows0, lanes), BF16)
    zi = 0
    nz_own = vo_ref.shape[2]
    for ref, nzp in ((vb_ref, vb_ref.shape[2]), (vo_ref, nz_own), (va_ref, nz_own)):
        if ref is va_ref:
            zmat = ref[0:c0 * nzp * ny]
        else:
            zmat = ref[0].reshape(c0 * nzp * ny, nx)
        whole = jnp.dot(zmat, sel_x, preferred_element_type=F32)
        for z in range(nzp):
            ymat = jnp.concatenate([whole[(i * nzp + z) * ny:(i * nzp + z + 1) * ny] for i in range(c0)], axis=0)
            blocks = [ymat[:, r * lanes:(r + 1) * lanes] for r in range(4)]
            qs[:, zi * lanes:(zi + 1) * lanes] = jnp.concatenate(
                blocks + [_shift_right(b) for b in blocks], axis=0).astype(BF16)
            zi += 1
    tall = jnp.dot(perm, qs[...], preferred_element_type=F32).astype(BF16)
    for zi in range(nzi):
        tp[zi, 1:] = tall[:, zi * lanes:(zi + 1) * lanes].reshape(ny, 2 * rows0, lanes)

    for a in range(n_act):
        for d in range(3):
            for y1 in range(ny1):
                p1[d * 3 * 2 * rows0:(d + 1) * 3 * 2 * rows0, (a * ny1 + y1) * lanes:(a * ny1 + y1 + 1) * lanes] = (
                    tp[2 * a + d, 2 * y1:2 * y1 + 3].reshape(3 * 2 * rows0, lanes))

    k1 = k1_ref[...]
    t2[:, 0] = jnp.zeros((n_act, c2, lanes), BF16)
    pre_all = jnp.dot(k1, p1[...], preferred_element_type=F32)
    for a in range(n_act):
        pre = pre_all[:, a * ny1 * lanes:(a + 1) * ny1 * lanes]
        if a in (1, 2):
            pre1[a - 1] = pre
        act = pre * _sigmoid(pre)
        for y1 in range(ny1):
            blk = act[:, y1 * lanes:(y1 + 1) * lanes]
            t2[a, y1 + 1] = jnp.concatenate([blk, _shift_right(blk)], axis=0).astype(BF16)

    for tt in range(2):
        for d in range(3):
            for y2 in range(ny2):
                p2[d * 3 * c2:(d + 1) * 3 * c2, (tt * ny2 + y2) * lanes:(tt * ny2 + y2 + 1) * lanes] = (
                    t2[2 * tt + d, 2 * y2:2 * y2 + 3].reshape(3 * c2, lanes))

    pre2 = jnp.dot(k2_ref[...], p2[...], preferred_element_type=F32)
    n2 = ny2 * lanes
    for tt in range(2):
        pre = pre2[:, tt * n2:(tt + 1) * n2]
        sig = _sigmoid(pre)
        if tt == 0:
            lvl_ref[...] = (pre * sig).astype(BF16)
        slope = sig * (1.0 + pre * (1.0 - sig))
        cot_t = cot_ref[...] if tt == 0 else va_ref[va_ref.shape[0] - c1:]
        bt[:, tt * n2:(tt + 1) * n2] = (cot_t.astype(F32) * slope).astype(BF16)

    bt0 = bt[:, :n2]
    dup = _nt(p2[:, :n2], jnp.concatenate([bt0, bt0], axis=0))
    c2n = dup.shape[1] // 2
    qi = c1 // 4
    lane2 = lax.broadcasted_iota(jnp.int32, (qi, 2 * c2n), 1)
    for dh in range(9):
        for w, off in enumerate((3 * c1 // 2, 0, c1 // 2)):
            r0 = dh * c2 + off
            s2_ref[(dh * 3 + w) * qi:(dh * 3 + w + 1) * qi] = jnp.where(
                lane2 < c2n, dup[r0:r0 + qi], dup[r0 + qi:r0 + 2 * qi])

    gacc[...] = jnp.zeros(gacc.shape, F32)
    gs[...] = jnp.dot(k2t_ref[...], bt[...], preferred_element_type=F32)
    for tt in range(2):
        taps_d = (1, 2) if tt == 0 else (0,)
        for d in taps_d:
            a = 2 * tt + d
            for h in range(3):
                for y2 in range(ny2):
                    y1 = 2 * y2 + h - 1
                    if y1 < 0:
                        continue
                    r0 = (d * 3 + h) * c2
                    blk = gs[r0:r0 + c2, (tt * ny2 + y2) * lanes:(tt * ny2 + y2 + 1) * lanes]
                    gacc[a - 1, :, y1 * lanes:(y1 + 1) * lanes] += blk[:c1] + _shift_left(blk[c1:])

    half = c1 // 2
    for a_ in range(2):
        g = gacc[a_]
        pre = pre1[a_]
        sig = _sigmoid(pre)
        slope = sig * (1.0 + pre * (1.0 - sig))
        b1[a_] = (g * slope).astype(BF16)
        gb = g.astype(BF16)
        for y1 in range(ny1):
            blk = gb[:, y1 * lanes:(y1 + 1) * lanes]
            r0 = (a_ * ny1 + y1) * half
            g1s[r0:r0 + half] = jnp.concatenate([blk[:half], blk[half:]], axis=1)
    s1_ref[...] = _nt(p1[:, ny1 * lanes:3 * ny1 * lanes], jnp.concatenate([b1[0], b1[1]], axis=1))

    n2 = 2 * lanes
    row = lax.broadcasted_iota(jnp.int32, (n2, n2), 0)
    col = lax.broadcasted_iota(jnp.int32, (n2, n2), 1)
    inter = jnp.where(col == 2 * (row % lanes) + row // lanes, 1.0, 0.0).astype(BF16)
    g1_ref[...] = jnp.dot(g1s[...], inter, preferred_element_type=F32).astype(BF16)


def _level_one_weights(k1):
    kt = jnp.transpose(k1, (0, 2, 3, 1, 4))
    w0, w1, w2 = kt[..., 0], kt[..., 1], kt[..., 2]
    z = jnp.zeros_like(w0)
    p0 = jnp.stack([jnp.stack([w1, w2, z, z], -1), jnp.stack([z, z, z, w0], -1)], 3)
    p1 = jnp.stack([jnp.stack([z, w0, w1, w2], -1), jnp.stack([z, z, z, z], -1)], 3)
    e = jnp.stack([p0, p1], 0)
    return e.reshape(2 * k1.shape[0], -1)


def _level_two_weights(k2):
    kt = jnp.transpose(k2, (0, 2, 3, 4, 1))
    w0, w1, w2 = kt[:, :, :, 0], kt[:, :, :, 1], kt[:, :, :, 2]
    z = jnp.zeros_like(w0)
    e = jnp.stack([jnp.stack([w1, w2], 3), jnp.stack([z, w0], 3)], 3)
    return e.reshape(k2.shape[0], -1)


def per_device(volume, kernel_one, kernel_two, cotangent):
    _, c0, nz, ny, nx = volume.shape
    c1 = kernel_one.shape[0]
    c2 = kernel_two.shape[0]
    assert nz == 4 and cotangent.shape[2] == 1
    q = nx // 4
    below = shifted(volume[:, :, 1:], "gz", 1)
    cot = cotangent[0, :, 0].reshape(cotangent.shape[1], -1)
    above = shifted(jnp.concatenate([volume[0].reshape(-1, nx), cot], 0), "gz", -1)
    nzi = below.shape[2] + 2 * nz
    n2 = cotangent.shape[3] * cotangent.shape[4]

    k1m = _level_one_weights(kernel_one)
    k2m = _level_two_weights(kernel_two)
    k2t = k2m.T

    ny1, ny2 = ny // 2, ny // 4
    n_act = 5
    vm = pltpu.VMEM
    lvl, g1, s1, s2 = pl.pallas_call(
        _kernel,
        out_shape=(
            jax.ShapeDtypeStruct((c2, n2), BF16),
            jax.ShapeDtypeStruct((2 * ny1 * c1, 2 * q), BF16),
            jax.ShapeDtypeStruct((k1m.shape[1], k1m.shape[0]), F32),
            jax.ShapeDtypeStruct((27 * c1 // 2, 2 * c2), F32),
        ),
        scratch_shapes=[
            vm((nzi, ny + 1, 8 * c0, q), BF16),
            vm((k1m.shape[1], n_act * ny1 * q), BF16),
            vm((n_act, ny1 + 1, 4 * c1, q), BF16),
            vm((2, 2 * c1, ny1 * q), F32),
            vm((k2m.shape[1], 2 * n2), BF16),
            vm((c2, 2 * n2), BF16),
            vm((k2m.shape[1], 2 * n2), F32),
            vm((2, 2 * c1, ny1 * q), F32),
            vm((2, 2 * c1, ny1 * q), BF16),
            vm((2 * ny1 * c1, 2 * q), BF16),
            vm((8 * c0 * ny, nzi * q), BF16),
        ],
        cost_estimate=pl.CostEstimate(flops=60_000_000, transcendentals=200_000, bytes_accessed=3_000_000),
    )(below, volume, above, k1m, k2m, k2t, cot)

    level_two = lvl.reshape(1, c2, 1, ny2, n2 // ny2)
    grad_one = g1.reshape(2, ny1, c1, 2 * q).transpose(2, 0, 1, 3)[None]

    s1r = s1.reshape(3, 3, 2, c0, 4, 2, c1)
    gk1 = jnp.stack([
        s1r[:, :, 1, :, 3, 0] + s1r[:, :, 0, :, 1, 1],
        s1r[:, :, 0, :, 0, 0] + s1r[:, :, 0, :, 2, 1],
        s1r[:, :, 0, :, 1, 0] + s1r[:, :, 0, :, 3, 1],
    ], 2)
    rows1 = gk1.size // s2.shape[1]
    total = _all_sum(jnp.concatenate([gk1.reshape(rows1, s2.shape[1]), s2], 0), ("gz", "sa"))
    samples = volume.shape[0] * lax.axis_size("sa")
    cells_one = samples * (nz // 2) * lax.axis_size("gz") * ny1 * (nx // 2)
    cells_two = samples * cotangent.shape[2] * lax.axis_size("gz") * cotangent.shape[3] * cotangent.shape[4]
    t1 = total[:rows1] / math.sqrt(float(cells_one))
    t2 = total[rows1:] / math.sqrt(float(cells_two))
    grad_kernel_one = t1.reshape(3, 3, 3, c0, c1).transpose(4, 3, 0, 1, 2)
    t2 = t2.reshape(27, c1 // 2, 2, c2).transpose(0, 2, 1, 3).reshape(3, 3, 3, c1, c2)
    grad_kernel_two = t2.transpose(4, 3, 0, 1, 2)
    return (level_two, grad_one, grad_kernel_one, grad_kernel_two)


def solution(mesh):
    placed = (P("sa", None, "gz", None, None), P(), P(), P("sa", None, "gz", None, None))
    return jax.shard_map(
        per_device,
        mesh=mesh,
        in_specs=placed,
        out_specs=(P("sa", None, "gz", None, None), P("sa", None, "gz", None, None), P(), P()),
        check_vma=False,
    )
```

```python
import math

import jax
import jax.numpy as jnp
from jax import lax
from jax.experimental import pallas as pl
from jax.experimental.pallas import tpu as pltpu
from jax.sharding import PartitionSpec as P

F32 = jnp.float32
BF16 = jnp.bfloat16


def shifted(block, axis, distance):
    devices = range(lax.axis_size(axis))
    route = [(i - distance, i) for i in devices if i - distance in devices]
    return lax.ppermute(block, axis, route)


def _all_sum(x, axes):
    steps = []
    for axis in axes:
        n = lax.axis_size(axis)
        assert n & (n - 1) == 0
        k = 1
        while k < n:
            steps.append((axis, n, k))
            k *= 2
    axis0, n0, k0 = steps[0]
    rows = x.shape[0]
    half = -(-rows // 16) * 8
    x = jnp.pad(x, ((0, 2 * half - rows), (0, 0)))
    low = (lax.axis_index(axis0) & k0) == 0
    lo, hi = x[:half], x[half:]
    pair = [(i, i ^ k0) for i in range(n0)]
    part = jnp.where(low, lo, hi) + lax.ppermute(jnp.where(low, hi, lo), axis0, pair)
    for axis, n, k in steps[1:]:
        part = part + lax.ppermute(part, axis, [(i, i ^ k) for i in range(n)])
    other = lax.ppermute(part, axis0, pair)
    return jnp.where(low, jnp.concatenate([part, other], 0), jnp.concatenate([other, part], 0))[:rows]


def _sigmoid(v):
    return 1.0 / (1.0 + jnp.exp(-v))


def _shift_right(x):
    lane = lax.broadcasted_iota(jnp.int32, x.shape, x.ndim - 1)
    return jnp.where(lane == 0, 0.0, pltpu.roll(x, 1, x.ndim - 1))


def _shift_left(x):
    n = x.shape[-1]
    lane = lax.broadcasted_iota(jnp.int32, x.shape, x.ndim - 1)
    return jnp.where(lane == n - 1, 0.0, pltpu.roll(x, n - 1, x.ndim - 1))


def _nt(a, b):
    return lax.dot_general(a, b, (((1,), (1,)), ((), ())), preferred_element_type=F32)


def _kernel(vb_ref, vo_ref, va_ref, k1_ref, k2_ref, k2t_ref, cot_ref,
            lvl_ref, g1_ref, s1_ref, s2_ref,
            tp, p1, t2, pre1, p2, bt, gs, gacc, b1, g1s, qs, vbuf, vsem):
    c0, ny, nx = vo_ref.shape[1], vo_ref.shape[3], vo_ref.shape[4]
    lanes = nx // 4
    nzi = tp.shape[0]
    n_act = p1.shape[1] // (vo_ref.shape[3] // 2 * vo_ref.shape[4] // 4)
    ny1 = ny // 2
    ny2 = ny1 // 2
    c2 = t2.shape[2]
    c1 = c2 // 2
    rows0 = 4 * c0

    xs = lax.broadcasted_iota(jnp.int32, (nx, nx), 0)
    cs = lax.broadcasted_iota(jnp.int32, (nx, nx), 1)
    sel_x = jnp.where(xs == 4 * (cs % lanes) + cs // lanes, 1.0, 0.0).astype(BF16)
    nq = 2 * rows0 * ny
    orow = lax.broadcasted_iota(jnp.int32, (nq, nq), 0)
    icol = lax.broadcasted_iota(jnp.int32, (nq, nq), 1)
    y_, s_ = orow // (2 * rows0), (orow // rows0) % 2
    i_, r_ = (orow // 4) % c0, orow % 4
    perm = jnp.where(icol == ((s_ * 4 + r_) * c0 + i_) * ny + y_, 1.0, 0.0).astype(BF16)

    tp[:, 0] = jnp.zeros((nzi, 2 * rows0, lanes), BF16)
    vb_copy = pltpu.make_async_copy(vb_ref, vbuf, vsem)
    vb_copy.start()
    nz_own = vo_ref.shape[2]
    nzb = vbuf.shape[2]
    for ref, nzp, zi0 in ((vo_ref, nz_own, nzb), (va_ref, nz_own, nzb + nz_own), (vbuf, nzb, 0)):
        if ref is va_ref:
            zmat = ref[0:c0 * nzp * ny]
        else:
            if ref is vbuf:
                vb_copy.wait()
            zmat = ref[0].reshape(c0 * nzp * ny, nx)
        whole = jnp.dot(zmat, sel_x, preferred_element_type=F32)
        for z in range(nzp):
            zi = zi0 + z
            ymat = jnp.concatenate([whole[(i * nzp + z) * ny:(i * nzp + z + 1) * ny] for i in range(c0)], axis=0)
            blocks = [ymat[:, r * lanes:(r + 1) * lanes] for r in range(4)]
            qs[:, zi * lanes:(zi + 1) * lanes] = jnp.concatenate(
                blocks + [_shift_right(b) for b in blocks], axis=0).astype(BF16)
    tall = jnp.dot(perm, qs[...], preferred_element_type=F32).astype(BF16)
    for zi in range(nzi):
        tp[zi, 1:] = tall[:, zi * lanes:(zi + 1) * lanes].reshape(ny, 2 * rows0, lanes)

    for a in range(n_act):
        for d in range(3):
            for y1 in range(ny1):
                p1[d * 3 * 2 * rows0:(d + 1) * 3 * 2 * rows0, (a * ny1 + y1) * lanes:(a * ny1 + y1 + 1) * lanes] = (
                    tp[2 * a + d, 2 * y1:2 * y1 + 3].reshape(3 * 2 * rows0, lanes))

    k1 = k1_ref[...]
    t2[:, 0] = jnp.zeros((n_act, c2, lanes), BF16)
    pre_all = jnp.dot(k1, p1[...], preferred_element_type=F32)
    for a in range(n_act):
        pre = pre_all[:, a * ny1 * lanes:(a + 1) * ny1 * lanes]
        if a in (1, 2):
            pre1[a - 1] = pre
        act = pre * _sigmoid(pre)
        for y1 in range(ny1):
            blk = act[:, y1 * lanes:(y1 + 1) * lanes]
            t2[a, y1 + 1] = jnp.concatenate([blk, _shift_right(blk)], axis=0).astype(BF16)

    for tt in range(2):
        for d in range(3):
            for y2 in range(ny2):
                p2[d * 3 * c2:(d + 1) * 3 * c2, (tt * ny2 + y2) * lanes:(tt * ny2 + y2 + 1) * lanes] = (
                    t2[2 * tt + d, 2 * y2:2 * y2 + 3].reshape(3 * c2, lanes))

    pre2 = jnp.dot(k2_ref[...], p2[...], preferred_element_type=F32)
    n2 = ny2 * lanes
    for tt in range(2):
        pre = pre2[:, tt * n2:(tt + 1) * n2]
        sig = _sigmoid(pre)
        if tt == 0:
            lvl_ref[...] = (pre * sig).astype(BF16)
        slope = sig * (1.0 + pre * (1.0 - sig))
        cot_t = cot_ref[...] if tt == 0 else va_ref[va_ref.shape[0] - c1:]
        bt[:, tt * n2:(tt + 1) * n2] = (cot_t.astype(F32) * slope).astype(BF16)

    bt0 = bt[:, :n2]
    dup = _nt(p2[:, :n2], jnp.concatenate([bt0, bt0], axis=0))
    c2n = dup.shape[1] // 2
    qi = c1 // 4
    lane2 = lax.broadcasted_iota(jnp.int32, (qi, 2 * c2n), 1)
    for dh in range(9):
        for w, off in enumerate((3 * c1 // 2, 0, c1 // 2)):
            r0 = dh * c2 + off
            s2_ref[(dh * 3 + w) * qi:(dh * 3 + w + 1) * qi] = jnp.where(
                lane2 < c2n, dup[r0:r0 + qi], dup[r0 + qi:r0 + 2 * qi])

    gacc[...] = jnp.zeros(gacc.shape, F32)
    gs[...] = jnp.dot(k2t_ref[...], bt[...], preferred_element_type=F32)
    for tt in range(2):
        taps_d = (1, 2) if tt == 0 else (0,)
        for d in taps_d:
            a = 2 * tt + d
            for h in range(3):
                for y2 in range(ny2):
                    y1 = 2 * y2 + h - 1
                    if y1 < 0:
                        continue
                    r0 = (d * 3 + h) * c2
                    blk = gs[r0:r0 + c2, (tt * ny2 + y2) * lanes:(tt * ny2 + y2 + 1) * lanes]
                    gacc[a - 1, :, y1 * lanes:(y1 + 1) * lanes] += blk[:c1] + _shift_left(blk[c1:])

    half = c1 // 2
    for a_ in range(2):
        g = gacc[a_]
        pre = pre1[a_]
        sig = _sigmoid(pre)
        slope = sig * (1.0 + pre * (1.0 - sig))
        b1[a_] = (g * slope).astype(BF16)
        gb = g.astype(BF16)
        for y1 in range(ny1):
            blk = gb[:, y1 * lanes:(y1 + 1) * lanes]
            r0 = (a_ * ny1 + y1) * half
            g1s[r0:r0 + half] = jnp.concatenate([blk[:half], blk[half:]], axis=1)
    s1_ref[...] = _nt(p1[:, ny1 * lanes:3 * ny1 * lanes], jnp.concatenate([b1[0], b1[1]], axis=1))

    n2 = 2 * lanes
    row = lax.broadcasted_iota(jnp.int32, (n2, n2), 0)
    col = lax.broadcasted_iota(jnp.int32, (n2, n2), 1)
    inter = jnp.where(col == 2 * (row % lanes) + row // lanes, 1.0, 0.0).astype(BF16)
    g1_ref[...] = jnp.dot(g1s[...], inter, preferred_element_type=F32).astype(BF16)


def _level_one_weights(k1):
    kt = jnp.transpose(k1, (0, 2, 3, 1, 4))
    w0, w1, w2 = kt[..., 0], kt[..., 1], kt[..., 2]
    z = jnp.zeros_like(w0)
    p0 = jnp.stack([jnp.stack([w1, w2, z, z], -1), jnp.stack([z, z, z, w0], -1)], 3)
    p1 = jnp.stack([jnp.stack([z, w0, w1, w2], -1), jnp.stack([z, z, z, z], -1)], 3)
    e = jnp.stack([p0, p1], 0)
    return e.reshape(2 * k1.shape[0], -1)


def _level_two_weights(k2):
    kt = jnp.transpose(k2, (0, 2, 3, 4, 1))
    w0, w1, w2 = kt[:, :, :, 0], kt[:, :, :, 1], kt[:, :, :, 2]
    z = jnp.zeros_like(w0)
    e = jnp.stack([jnp.stack([w1, w2], 3), jnp.stack([z, w0], 3)], 3)
    return e.reshape(k2.shape[0], -1)


def per_device(volume, kernel_one, kernel_two, cotangent):
    _, c0, nz, ny, nx = volume.shape
    c1 = kernel_one.shape[0]
    c2 = kernel_two.shape[0]
    assert nz == 4 and cotangent.shape[2] == 1
    q = nx // 4
    below = shifted(volume[:, :, 1:], "gz", 1)
    cot = cotangent[0, :, 0].reshape(cotangent.shape[1], -1)
    above = shifted(jnp.concatenate([volume[0].reshape(-1, nx), cot], 0), "gz", -1)
    nzi = below.shape[2] + 2 * nz
    n2 = cotangent.shape[3] * cotangent.shape[4]

    k1m = _level_one_weights(kernel_one)
    k2m = _level_two_weights(kernel_two)
    k2t = k2m.T

    ny1, ny2 = ny // 2, ny // 4
    n_act = 5
    vm = pltpu.VMEM
    lvl, g1, s1, s2 = pl.pallas_call(
        _kernel,
        in_specs=[pl.BlockSpec(memory_space=pl.ANY)] + [pl.BlockSpec(memory_space=vm)] * 6,
        out_shape=(
            jax.ShapeDtypeStruct((c2, n2), BF16),
            jax.ShapeDtypeStruct((2 * ny1 * c1, 2 * q), BF16),
            jax.ShapeDtypeStruct((k1m.shape[1], k1m.shape[0]), F32),
            jax.ShapeDtypeStruct((27 * c1 // 2, 2 * c2), F32),
        ),
        scratch_shapes=[
            vm((nzi, ny + 1, 8 * c0, q), BF16),
            vm((k1m.shape[1], n_act * ny1 * q), BF16),
            vm((n_act, ny1 + 1, 4 * c1, q), BF16),
            vm((2, 2 * c1, ny1 * q), F32),
            vm((k2m.shape[1], 2 * n2), BF16),
            vm((c2, 2 * n2), BF16),
            vm((k2m.shape[1], 2 * n2), F32),
            vm((2, 2 * c1, ny1 * q), F32),
            vm((2, 2 * c1, ny1 * q), BF16),
            vm((2 * ny1 * c1, 2 * q), BF16),
            vm((8 * c0 * ny, nzi * q), BF16),
            vm(below.shape, BF16),
            pltpu.SemaphoreType.DMA(()),
        ],
        cost_estimate=pl.CostEstimate(flops=60_000_000, transcendentals=200_000, bytes_accessed=3_000_000),
    )(below, volume, above, k1m, k2m, k2t, cot)

    level_two = lvl.reshape(1, c2, 1, ny2, n2 // ny2)
    grad_one = g1.reshape(2, ny1, c1, 2 * q).transpose(2, 0, 1, 3)[None]

    s1r = s1.reshape(3, 3, 2, c0, 4, 2, c1)
    gk1 = jnp.stack([
        s1r[:, :, 1, :, 3, 0] + s1r[:, :, 0, :, 1, 1],
        s1r[:, :, 0, :, 0, 0] + s1r[:, :, 0, :, 2, 1],
        s1r[:, :, 0, :, 1, 0] + s1r[:, :, 0, :, 3, 1],
    ], 2)
    rows1 = gk1.size // s2.shape[1]
    total = _all_sum(jnp.concatenate([gk1.reshape(rows1, s2.shape[1]), s2], 0), ("gz", "sa"))
    samples = volume.shape[0] * lax.axis_size("sa")
    cells_one = samples * (nz // 2) * lax.axis_size("gz") * ny1 * (nx // 2)
    cells_two = samples * cotangent.shape[2] * lax.axis_size("gz") * cotangent.shape[3] * cotangent.shape[4]
    t1 = total[:rows1] / math.sqrt(float(cells_one))
    t2 = total[rows1:] / math.sqrt(float(cells_two))
    grad_kernel_one = t1.reshape(3, 3, 3, c0, c1).transpose(4, 3, 0, 1, 2)
    t2 = t2.reshape(27, c1 // 2, 2, c2).transpose(0, 2, 1, 3).reshape(3, 3, 3, c1, c2)
    grad_kernel_two = t2.transpose(4, 3, 0, 1, 2)
    return (level_two, grad_one, grad_kernel_one, grad_kernel_two)


def solution(mesh):
    placed = (P("sa", None, "gz", None, None), P(), P(), P("sa", None, "gz", None, None))
    return jax.shard_map(
        per_device,
        mesh=mesh,
        in_specs=placed,
        out_specs=(P("sa", None, "gz", None, None), P("sa", None, "gz", None, None), P(), P()),
        check_vma=False,
    )
```

```python
import math

import jax
import jax.numpy as jnp
from jax import lax
from jax.experimental import pallas as pl
from jax.experimental.pallas import tpu as pltpu
from jax.sharding import PartitionSpec as P

F32 = jnp.float32
BF16 = jnp.bfloat16


def shifted(block, axis, distance):
    devices = range(lax.axis_size(axis))
    route = [(i - distance, i) for i in devices if i - distance in devices]
    return lax.ppermute(block, axis, route)


def _all_sum(x, axes):
    steps = []
    for axis in axes:
        n = lax.axis_size(axis)
        assert n & (n - 1) == 0
        k = 1
        while k < n:
            steps.append((axis, n, k))
            k *= 2
    axis0, n0, k0 = steps[0]
    rows = x.shape[0]
    half = -(-rows // 16) * 8
    x = jnp.pad(x, ((0, 2 * half - rows), (0, 0)))
    low = (lax.axis_index(axis0) & k0) == 0
    lo, hi = x[:half], x[half:]
    pair = [(i, i ^ k0) for i in range(n0)]
    part = jnp.where(low, lo, hi) + lax.ppermute(jnp.where(low, hi, lo), axis0, pair)
    for axis, n, k in steps[1:]:
        part = part + lax.ppermute(part, axis, [(i, i ^ k) for i in range(n)])
    other = lax.ppermute(part, axis0, pair)
    return jnp.where(low, jnp.concatenate([part, other], 0), jnp.concatenate([other, part], 0))[:rows]


def _sigmoid(v):
    return 1.0 / (1.0 + jnp.exp(-v))


def _shift_right(x):
    lane = lax.broadcasted_iota(jnp.int32, x.shape, x.ndim - 1)
    return jnp.where(lane == 0, 0.0, pltpu.roll(x, 1, x.ndim - 1))


def _shift_left(x):
    n = x.shape[-1]
    lane = lax.broadcasted_iota(jnp.int32, x.shape, x.ndim - 1)
    return jnp.where(lane == n - 1, 0.0, pltpu.roll(x, n - 1, x.ndim - 1))


def _nt(a, b):
    return lax.dot_general(a, b, (((1,), (1,)), ((), ())), preferred_element_type=F32)


def _kernel(vb_ref, vo_ref, va_ref, k1_ref, k2_ref, k2t_ref, cot_ref,
            lvl_ref, g1_ref, s2_ref,
            tp, p1, t2, pre1, p2, bt, gs, gacc, b1, g1s, qs, s1s):
    c0, ny, nx = vo_ref.shape[1], vo_ref.shape[3], vo_ref.shape[4]
    lanes = nx // 4
    nzi = tp.shape[0]
    n_act = p1.shape[1] // (vo_ref.shape[3] // 2 * vo_ref.shape[4] // 4)
    ny1 = ny // 2
    ny2 = ny1 // 2
    c2 = t2.shape[2]
    c1 = c2 // 2
    rows0 = 4 * c0

    xs = lax.broadcasted_iota(jnp.int32, (nx, nx), 0)
    cs = lax.broadcasted_iota(jnp.int32, (nx, nx), 1)
    sel_x = jnp.where(xs == 4 * (cs % lanes) + cs // lanes, 1.0, 0.0).astype(BF16)
    nq = 2 * rows0 * ny
    orow = lax.broadcasted_iota(jnp.int32, (nq, nq), 0)
    icol = lax.broadcasted_iota(jnp.int32, (nq, nq), 1)
    y_, s_ = orow // (2 * rows0), (orow // rows0) % 2
    i_, r_ = (orow // 4) % c0, orow % 4
    perm = jnp.where(icol == ((s_ * 4 + r_) * c0 + i_) * ny + y_, 1.0, 0.0).astype(BF16)

    tp[:, 0] = jnp.zeros((nzi, 2 * rows0, lanes), BF16)
    zi = 0
    nz_own = vo_ref.shape[2]
    for ref, nzp in ((vb_ref, vb_ref.shape[2]), (vo_ref, nz_own), (va_ref, nz_own)):
        if ref is va_ref:
            zmat = ref[0:c0 * nzp * ny]
        else:
            zmat = ref[0].reshape(c0 * nzp * ny, nx)
        whole = jnp.dot(zmat, sel_x, preferred_element_type=F32)
        for z in range(nzp):
            ymat = jnp.concatenate([whole[(i * nzp + z) * ny:(i * nzp + z + 1) * ny] for i in range(c0)], axis=0)
            blocks = [ymat[:, r * lanes:(r + 1) * lanes] for r in range(4)]
            qs[:, zi * lanes:(zi + 1) * lanes] = jnp.concatenate(
                blocks + [_shift_right(b) for b in blocks], axis=0).astype(BF16)
            zi += 1
    tall = jnp.dot(perm, qs[...], preferred_element_type=F32).astype(BF16)
    for zi in range(nzi):
        tp[zi, 1:] = tall[:, zi * lanes:(zi + 1) * lanes].reshape(ny, 2 * rows0, lanes)

    for a in range(n_act):
        for d in range(3):
            for y1 in range(ny1):
                p1[d * 3 * 2 * rows0:(d + 1) * 3 * 2 * rows0, (a * ny1 + y1) * lanes:(a * ny1 + y1 + 1) * lanes] = (
                    tp[2 * a + d, 2 * y1:2 * y1 + 3].reshape(3 * 2 * rows0, lanes))

    k1 = k1_ref[...]
    t2[:, 0] = jnp.zeros((n_act, c2, lanes), BF16)
    pre_all = jnp.dot(k1, p1[...], preferred_element_type=F32)
    for a in range(n_act):
        pre = pre_all[:, a * ny1 * lanes:(a + 1) * ny1 * lanes]
        if a in (1, 2):
            pre1[a - 1] = pre
        act = pre * _sigmoid(pre)
        for y1 in range(ny1):
            blk = act[:, y1 * lanes:(y1 + 1) * lanes]
            t2[a, y1 + 1] = jnp.concatenate([blk, _shift_right(blk)], axis=0).astype(BF16)

    for tt in range(2):
        for d in range(3):
            for y2 in range(ny2):
                p2[d * 3 * c2:(d + 1) * 3 * c2, (tt * ny2 + y2) * lanes:(tt * ny2 + y2 + 1) * lanes] = (
                    t2[2 * tt + d, 2 * y2:2 * y2 + 3].reshape(3 * c2, lanes))

    pre2 = jnp.dot(k2_ref[...], p2[...], preferred_element_type=F32)
    n2 = ny2 * lanes
    for tt in range(2):
        pre = pre2[:, tt * n2:(tt + 1) * n2]
        sig = _sigmoid(pre)
        if tt == 0:
            lvl_ref[...] = (pre * sig).astype(BF16)
        slope = sig * (1.0 + pre * (1.0 - sig))
        cot_t = cot_ref[...] if tt == 0 else va_ref[va_ref.shape[0] - c1:]
        bt[:, tt * n2:(tt + 1) * n2] = (cot_t.astype(F32) * slope).astype(BF16)

    bt0 = bt[:, :n2]
    dup = _nt(p2[:, :n2], jnp.concatenate([bt0, bt0], axis=0))
    c2n = dup.shape[1] // 2
    qi = c1 // 4
    lane2 = lax.broadcasted_iota(jnp.int32, (qi, 2 * c2n), 1)
    n_s2 = 27 * qi
    s2_ref[n_s2:] = jnp.zeros((s2_ref.shape[0] - n_s2, s2_ref.shape[1]), F32)
    for dh in range(9):
        for w, off in enumerate((3 * c1 // 2, 0, c1 // 2)):
            r0 = dh * c2 + off
            s2_ref[(dh * 3 + w) * qi:(dh * 3 + w + 1) * qi] = jnp.where(
                lane2 < c2n, dup[r0:r0 + qi], dup[r0 + qi:r0 + 2 * qi])

    gacc[...] = jnp.zeros(gacc.shape, F32)
    gs[...] = jnp.dot(k2t_ref[...], bt[...], preferred_element_type=F32)
    for tt in range(2):
        taps_d = (1, 2) if tt == 0 else (0,)
        for d in taps_d:
            a = 2 * tt + d
            for h in range(3):
                for y2 in range(ny2):
                    y1 = 2 * y2 + h - 1
                    if y1 < 0:
                        continue
                    r0 = (d * 3 + h) * c2
                    blk = gs[r0:r0 + c2, (tt * ny2 + y2) * lanes:(tt * ny2 + y2 + 1) * lanes]
                    gacc[a - 1, :, y1 * lanes:(y1 + 1) * lanes] += blk[:c1] + _shift_left(blk[c1:])

    half = c1 // 2
    for a_ in range(2):
        g = gacc[a_]
        pre = pre1[a_]
        sig = _sigmoid(pre)
        slope = sig * (1.0 + pre * (1.0 - sig))
        b1[a_] = (g * slope).astype(BF16)
        gb = g.astype(BF16)
        for y1 in range(ny1):
            blk = gb[:, y1 * lanes:(y1 + 1) * lanes]
            r0 = (a_ * ny1 + y1) * half
            g1s[r0:r0 + half] = jnp.concatenate([blk[:half], blk[half:]], axis=1)
    bcat = jnp.concatenate([b1[0], b1[1]], axis=1)
    s1s[...] = _nt(p1[:, ny1 * lanes:3 * ny1 * lanes],
                   jnp.concatenate([bcat, jnp.zeros(bcat.shape, BF16)], axis=0))
    qo = c1 // 2
    lane1 = lax.broadcasted_iota(jnp.int32, (1, 4 * qo), 1)
    taps = (((1, 3), (0, 1)), ((0, 0), (0, 2)), ((0, 1), (0, 3)))
    out_rows = []
    for dh in range(9):
        for (sa, ra), (sb, rb) in taps:
            acc = jnp.zeros((1, 4 * qo), F32)
            for i in range(c0):
                xa = s1s[pl.ds(dh * 2 * rows0 + sa * rows0 + i * 4 + ra, 1), :]
                xb = s1s[pl.ds(dh * 2 * rows0 + sb * rows0 + i * 4 + rb, 1), :]
                if i:
                    xa = pltpu.roll(xa, i * qo, 1)
                xb = pltpu.roll(xb, (i * qo - qo) % (4 * qo), 1)
                m = (lane1 >= i * qo) & (lane1 < (i + 1) * qo)
                acc = acc + jnp.where(m, xa + xb, 0.0)
            out_rows.append(acc)
    n_s2 = 27 * qi
    s2_ref[n_s2:n_s2 + 27] = jnp.concatenate(out_rows, axis=0)

    n2 = 2 * lanes
    row = lax.broadcasted_iota(jnp.int32, (n2, n2), 0)
    col = lax.broadcasted_iota(jnp.int32, (n2, n2), 1)
    inter = jnp.where(col == 2 * (row % lanes) + row // lanes, 1.0, 0.0).astype(BF16)
    g1_ref[...] = jnp.dot(g1s[...], inter, preferred_element_type=F32).astype(BF16)


def _level_one_weights(k1):
    kt = jnp.transpose(k1, (0, 2, 3, 1, 4))
    w0, w1, w2 = kt[..., 0], kt[..., 1], kt[..., 2]
    z = jnp.zeros_like(w0)
    p0 = jnp.stack([jnp.stack([w1, w2, z, z], -1), jnp.stack([z, z, z, w0], -1)], 3)
    p1 = jnp.stack([jnp.stack([z, w0, w1, w2], -1), jnp.stack([z, z, z, z], -1)], 3)
    e = jnp.stack([p0, p1], 0)
    return e.reshape(2 * k1.shape[0], -1)


def _level_two_weights(k2):
    kt = jnp.transpose(k2, (0, 2, 3, 4, 1))
    w0, w1, w2 = kt[:, :, :, 0], kt[:, :, :, 1], kt[:, :, :, 2]
    z = jnp.zeros_like(w0)
    e = jnp.stack([jnp.stack([w1, w2], 3), jnp.stack([z, w0], 3)], 3)
    return e.reshape(k2.shape[0], -1)


def per_device(volume, kernel_one, kernel_two, cotangent):
    _, c0, nz, ny, nx = volume.shape
    c1 = kernel_one.shape[0]
    c2 = kernel_two.shape[0]
    assert nz == 4 and cotangent.shape[2] == 1
    q = nx // 4
    below = shifted(volume[:, :, 1:], "gz", 1)
    cot = cotangent[0, :, 0].reshape(cotangent.shape[1], -1)
    above = shifted(jnp.concatenate([volume[0].reshape(-1, nx), cot], 0), "gz", -1)
    nzi = below.shape[2] + 2 * nz
    n2 = cotangent.shape[3] * cotangent.shape[4]

    k1m = _level_one_weights(kernel_one)
    k2m = _level_two_weights(kernel_two)
    k2t = k2m.T

    ny1, ny2 = ny // 2, ny // 4
    n_act = 5
    n_s2 = 27 * c1 // 2
    n_g1 = 27 * c0 * c1 // (2 * c2)
    n_pay = -(-(n_s2 + n_g1) // 16) * 16
    vm = pltpu.VMEM
    lvl, g1, pay = pl.pallas_call(
        _kernel,
        out_shape=(
            jax.ShapeDtypeStruct((c2, n2), BF16),
            jax.ShapeDtypeStruct((2 * ny1 * c1, 2 * q), BF16),
            jax.ShapeDtypeStruct((n_pay, 2 * c2), F32),
        ),
        scratch_shapes=[
            vm((nzi, ny + 1, 8 * c0, q), BF16),
            vm((k1m.shape[1], n_act * ny1 * q), BF16),
            vm((n_act, ny1 + 1, 4 * c1, q), BF16),
            vm((2, 2 * c1, ny1 * q), F32),
            vm((k2m.shape[1], 2 * n2), BF16),
            vm((c2, 2 * n2), BF16),
            vm((k2m.shape[1], 2 * n2), F32),
            vm((2, 2 * c1, ny1 * q), F32),
            vm((2, 2 * c1, ny1 * q), BF16),
            vm((2 * ny1 * c1, 2 * q), BF16),
            vm((8 * c0 * ny, nzi * q), BF16),
            vm((k1m.shape[1], 2 * k1m.shape[0]), F32),
        ],
        cost_estimate=pl.CostEstimate(flops=60_000_000, transcendentals=200_000, bytes_accessed=3_000_000),
    )(below, volume, above, k1m, k2m, k2t, cot)

    level_two = lvl.reshape(1, c2, 1, ny2, n2 // ny2)
    grad_one = g1.reshape(2, ny1, c1, 2 * q).transpose(2, 0, 1, 3)[None]

    total = _all_sum(pay, ("gz", "sa"))
    samples = volume.shape[0] * lax.axis_size("sa")
    cells_one = samples * (nz // 2) * lax.axis_size("gz") * ny1 * (nx // 2)
    cells_two = samples * cotangent.shape[2] * lax.axis_size("gz") * cotangent.shape[3] * cotangent.shape[4]
    t1 = total[n_s2:n_s2 + n_g1] / math.sqrt(float(cells_one))
    t2 = total[:n_s2] / math.sqrt(float(cells_two))
    grad_kernel_one = t1.reshape(3, 3, 3, c0, c1).transpose(4, 3, 0, 1, 2)
    t2 = t2.reshape(27, c1 // 2, 2, c2).transpose(0, 2, 1, 3).reshape(3, 3, 3, c1, c2)
    grad_kernel_two = t2.transpose(4, 3, 0, 1, 2)
    return (level_two, grad_one, grad_kernel_one, grad_kernel_two)


def solution(mesh):
    placed = (P("sa", None, "gz", None, None), P(), P(), P("sa", None, "gz", None, None))
    return jax.shard_map(
        per_device,
        mesh=mesh,
        in_specs=placed,
        out_specs=(P("sa", None, "gz", None, None), P("sa", None, "gz", None, None), P(), P()),
        check_vma=False,
    )
```

```python
import math

import jax
import jax.numpy as jnp
from jax import lax
from jax.experimental import pallas as pl
from jax.experimental.pallas import tpu as pltpu
from jax.sharding import PartitionSpec as P

F32 = jnp.float32
BF16 = jnp.bfloat16


def shifted(block, axis, distance):
    devices = range(lax.axis_size(axis))
    route = [(i - distance, i) for i in devices if i - distance in devices]
    return lax.ppermute(block, axis, route)


def _all_sum(keep, send, axes):
    steps = []
    for axis in axes:
        n = lax.axis_size(axis)
        assert n & (n - 1) == 0
        k = 1
        while k < n:
            steps.append((axis, n, k))
            k *= 2
    axis0, n0, k0 = steps[0]
    assert axis0 == "gz" and k0 == 1
    low = (lax.axis_index(axis0) & k0) == 0
    pair = [(i, i ^ k0) for i in range(n0)]
    part = keep + lax.ppermute(send, axis0, pair)
    for axis, n, k in steps[1:]:
        part = part + lax.ppermute(part, axis, [(i, i ^ k) for i in range(n)])
    other = lax.ppermute(part, axis0, pair)
    return jnp.where(low, jnp.concatenate([part, other], 0), jnp.concatenate([other, part], 0))


def _sigmoid(v):
    return 1.0 / (1.0 + jnp.exp(-v))


def _shift_right(x):
    lane = lax.broadcasted_iota(jnp.int32, x.shape, x.ndim - 1)
    return jnp.where(lane == 0, 0.0, pltpu.roll(x, 1, x.ndim - 1))


def _shift_left(x):
    n = x.shape[-1]
    lane = lax.broadcasted_iota(jnp.int32, x.shape, x.ndim - 1)
    return jnp.where(lane == n - 1, 0.0, pltpu.roll(x, n - 1, x.ndim - 1))


def _nt(a, b):
    return lax.dot_general(a, b, (((1,), (1,)), ((), ())), preferred_element_type=F32)


def _kernel(vb_ref, vo_ref, va_ref, k1_ref, k2_ref, k2t_ref, cot_ref,
            lvl_ref, g1_ref, keep_ref, send_ref,
            tp, p1, t2, pre1, p2, bt, gs, gacc, b1, g1s, qs, s1s, s2_ref):
    c0, ny, nx = vo_ref.shape[1], vo_ref.shape[3], vo_ref.shape[4]
    lanes = nx // 4
    nzi = tp.shape[0]
    n_act = p1.shape[1] // (vo_ref.shape[3] // 2 * vo_ref.shape[4] // 4)
    ny1 = ny // 2
    ny2 = ny1 // 2
    c2 = t2.shape[2]
    c1 = c2 // 2
    rows0 = 4 * c0

    xs = lax.broadcasted_iota(jnp.int32, (nx, nx), 0)
    cs = lax.broadcasted_iota(jnp.int32, (nx, nx), 1)
    sel_x = jnp.where(xs == 4 * (cs % lanes) + cs // lanes, 1.0, 0.0).astype(BF16)
    nq = 2 * rows0 * ny
    orow = lax.broadcasted_iota(jnp.int32, (nq, nq), 0)
    icol = lax.broadcasted_iota(jnp.int32, (nq, nq), 1)
    y_, s_ = orow // (2 * rows0), (orow // rows0) % 2
    i_, r_ = (orow // 4) % c0, orow % 4
    perm = jnp.where(icol == ((s_ * 4 + r_) * c0 + i_) * ny + y_, 1.0, 0.0).astype(BF16)

    tp[:, 0] = jnp.zeros((nzi, 2 * rows0, lanes), BF16)
    zi = 0
    nz_own = vo_ref.shape[2]
    for ref, nzp in ((vb_ref, vb_ref.shape[2]), (vo_ref, nz_own), (va_ref, nz_own)):
        if ref is va_ref:
            zmat = ref[0:c0 * nzp * ny]
        else:
            zmat = ref[0].reshape(c0 * nzp * ny, nx)
        whole = jnp.dot(zmat, sel_x, preferred_element_type=F32)
        for z in range(nzp):
            ymat = jnp.concatenate([whole[(i * nzp + z) * ny:(i * nzp + z + 1) * ny] for i in range(c0)], axis=0)
            blocks = [ymat[:, r * lanes:(r + 1) * lanes] for r in range(4)]
            qs[:, zi * lanes:(zi + 1) * lanes] = jnp.concatenate(
                blocks + [_shift_right(b) for b in blocks], axis=0).astype(BF16)
            zi += 1
    tall = jnp.dot(perm, qs[...], preferred_element_type=F32).astype(BF16)
    for zi in range(nzi):
        tp[zi, 1:] = tall[:, zi * lanes:(zi + 1) * lanes].reshape(ny, 2 * rows0, lanes)

    for a in range(n_act):
        for d in range(3):
            for y1 in range(ny1):
                p1[d * 3 * 2 * rows0:(d + 1) * 3 * 2 * rows0, (a * ny1 + y1) * lanes:(a * ny1 + y1 + 1) * lanes] = (
                    tp[2 * a + d, 2 * y1:2 * y1 + 3].reshape(3 * 2 * rows0, lanes))

    k1 = k1_ref[...]
    t2[:, 0] = jnp.zeros((n_act, c2, lanes), BF16)
    pre_all = jnp.dot(k1, p1[...], preferred_element_type=F32)
    for a in range(n_act):
        pre = pre_all[:, a * ny1 * lanes:(a + 1) * ny1 * lanes]
        if a in (1, 2):
            pre1[a - 1] = pre
        act = pre * _sigmoid(pre)
        for y1 in range(ny1):
            blk = act[:, y1 * lanes:(y1 + 1) * lanes]
            t2[a, y1 + 1] = jnp.concatenate([blk, _shift_right(blk)], axis=0).astype(BF16)

    for tt in range(2):
        for d in range(3):
            for y2 in range(ny2):
                p2[d * 3 * c2:(d + 1) * 3 * c2, (tt * ny2 + y2) * lanes:(tt * ny2 + y2 + 1) * lanes] = (
                    t2[2 * tt + d, 2 * y2:2 * y2 + 3].reshape(3 * c2, lanes))

    pre2 = jnp.dot(k2_ref[...], p2[...], preferred_element_type=F32)
    n2 = ny2 * lanes
    for tt in range(2):
        pre = pre2[:, tt * n2:(tt + 1) * n2]
        sig = _sigmoid(pre)
        if tt == 0:
            lvl_ref[...] = (pre * sig).astype(BF16)
        slope = sig * (1.0 + pre * (1.0 - sig))
        cot_t = cot_ref[...] if tt == 0 else va_ref[va_ref.shape[0] - c1:]
        bt[:, tt * n2:(tt + 1) * n2] = (cot_t.astype(F32) * slope).astype(BF16)

    bt0 = bt[:, :n2]
    dup = _nt(p2[:, :n2], jnp.concatenate([bt0, bt0], axis=0))
    c2n = dup.shape[1] // 2
    qi = c1 // 4
    lane2 = lax.broadcasted_iota(jnp.int32, (qi, 2 * c2n), 1)
    n_s2 = 27 * qi
    s2_ref[n_s2:] = jnp.zeros((s2_ref.shape[0] - n_s2, s2_ref.shape[1]), F32)
    for dh in range(9):
        for w, off in enumerate((3 * c1 // 2, 0, c1 // 2)):
            r0 = dh * c2 + off
            s2_ref[(dh * 3 + w) * qi:(dh * 3 + w + 1) * qi] = jnp.where(
                lane2 < c2n, dup[r0:r0 + qi], dup[r0 + qi:r0 + 2 * qi])

    gacc[...] = jnp.zeros(gacc.shape, F32)
    gs[...] = jnp.dot(k2t_ref[...], bt[...], preferred_element_type=F32)
    for tt in range(2):
        taps_d = (1, 2) if tt == 0 else (0,)
        for d in taps_d:
            a = 2 * tt + d
            for h in range(3):
                for y2 in range(ny2):
                    y1 = 2 * y2 + h - 1
                    if y1 < 0:
                        continue
                    r0 = (d * 3 + h) * c2
                    blk = gs[r0:r0 + c2, (tt * ny2 + y2) * lanes:(tt * ny2 + y2 + 1) * lanes]
                    gacc[a - 1, :, y1 * lanes:(y1 + 1) * lanes] += blk[:c1] + _shift_left(blk[c1:])

    half = c1 // 2
    for a_ in range(2):
        g = gacc[a_]
        pre = pre1[a_]
        sig = _sigmoid(pre)
        slope = sig * (1.0 + pre * (1.0 - sig))
        b1[a_] = (g * slope).astype(BF16)
        gb = g.astype(BF16)
        for y1 in range(ny1):
            blk = gb[:, y1 * lanes:(y1 + 1) * lanes]
            r0 = (a_ * ny1 + y1) * half
            g1s[r0:r0 + half] = jnp.concatenate([blk[:half], blk[half:]], axis=1)
    bcat = jnp.concatenate([b1[0], b1[1]], axis=1)
    s1s[...] = _nt(p1[:, ny1 * lanes:3 * ny1 * lanes],
                   jnp.concatenate([bcat, jnp.zeros(bcat.shape, BF16)], axis=0))
    qo = c1 // 2
    lane1 = lax.broadcasted_iota(jnp.int32, (1, 4 * qo), 1)
    taps = (((1, 3), (0, 1)), ((0, 0), (0, 2)), ((0, 1), (0, 3)))
    out_rows = []
    for dh in range(9):
        for (sa, ra), (sb, rb) in taps:
            acc = jnp.zeros((1, 4 * qo), F32)
            for i in range(c0):
                xa = s1s[pl.ds(dh * 2 * rows0 + sa * rows0 + i * 4 + ra, 1), :]
                xb = s1s[pl.ds(dh * 2 * rows0 + sb * rows0 + i * 4 + rb, 1), :]
                if i:
                    xa = pltpu.roll(xa, i * qo, 1)
                xb = pltpu.roll(xb, (i * qo - qo) % (4 * qo), 1)
                m = (lane1 >= i * qo) & (lane1 < (i + 1) * qo)
                acc = acc + jnp.where(m, xa + xb, 0.0)
            out_rows.append(acc)
    n_s2 = 27 * qi
    s2_ref[n_s2:n_s2 + 27] = jnp.concatenate(out_rows, axis=0)
    half_rows = keep_ref.shape[0]
    low = jnp.full((half_rows, s2_ref.shape[1]), lax.axis_index("gz") % 2) == 0
    lo_h, hi_h = s2_ref[:half_rows], s2_ref[half_rows:]
    keep_ref[...] = jnp.where(low, lo_h, hi_h)
    send_ref[...] = jnp.where(low, hi_h, lo_h)

    n2 = 2 * lanes
    row = lax.broadcasted_iota(jnp.int32, (n2, n2), 0)
    col = lax.broadcasted_iota(jnp.int32, (n2, n2), 1)
    inter = jnp.where(col == 2 * (row % lanes) + row // lanes, 1.0, 0.0).astype(BF16)
    g1_ref[...] = jnp.dot(g1s[...], inter, preferred_element_type=F32).astype(BF16)


def _level_one_weights(k1):
    kt = jnp.transpose(k1, (0, 2, 3, 1, 4))
    w0, w1, w2 = kt[..., 0], kt[..., 1], kt[..., 2]
    z = jnp.zeros_like(w0)
    p0 = jnp.stack([jnp.stack([w1, w2, z, z], -1), jnp.stack([z, z, z, w0], -1)], 3)
    p1 = jnp.stack([jnp.stack([z, w0, w1, w2], -1), jnp.stack([z, z, z, z], -1)], 3)
    e = jnp.stack([p0, p1], 0)
    return e.reshape(2 * k1.shape[0], -1)


def _level_two_weights(k2):
    kt = jnp.transpose(k2, (0, 2, 3, 4, 1))
    w0, w1, w2 = kt[:, :, :, 0], kt[:, :, :, 1], kt[:, :, :, 2]
    z = jnp.zeros_like(w0)
    e = jnp.stack([jnp.stack([w1, w2], 3), jnp.stack([z, w0], 3)], 3)
    return e.reshape(k2.shape[0], -1)


def per_device(volume, kernel_one, kernel_two, cotangent):
    _, c0, nz, ny, nx = volume.shape
    c1 = kernel_one.shape[0]
    c2 = kernel_two.shape[0]
    assert nz == 4 and cotangent.shape[2] == 1
    q = nx // 4
    below = shifted(volume[:, :, 1:], "gz", 1)
    cot = cotangent[0, :, 0].reshape(cotangent.shape[1], -1)
    above = shifted(jnp.concatenate([volume[0].reshape(-1, nx), cot], 0), "gz", -1)
    nzi = below.shape[2] + 2 * nz
    n2 = cotangent.shape[3] * cotangent.shape[4]

    k1m = _level_one_weights(kernel_one)
    k2m = _level_two_weights(kernel_two)
    k2t = k2m.T

    ny1, ny2 = ny // 2, ny // 4
    n_act = 5
    n_s2 = 27 * c1 // 2
    n_g1 = 27 * c0 * c1 // (2 * c2)
    n_pay = -(-(n_s2 + n_g1) // 16) * 16
    vm = pltpu.VMEM
    lvl, g1, keep, send = pl.pallas_call(
        _kernel,
        out_shape=(
            jax.ShapeDtypeStruct((c2, n2), BF16),
            jax.ShapeDtypeStruct((2 * ny1 * c1, 2 * q), BF16),
            jax.ShapeDtypeStruct((n_pay // 2, 2 * c2), F32),
            jax.ShapeDtypeStruct((n_pay // 2, 2 * c2), F32),
        ),
        scratch_shapes=[
            vm((nzi, ny + 1, 8 * c0, q), BF16),
            vm((k1m.shape[1], n_act * ny1 * q), BF16),
            vm((n_act, ny1 + 1, 4 * c1, q), BF16),
            vm((2, 2 * c1, ny1 * q), F32),
            vm((k2m.shape[1], 2 * n2), BF16),
            vm((c2, 2 * n2), BF16),
            vm((k2m.shape[1], 2 * n2), F32),
            vm((2, 2 * c1, ny1 * q), F32),
            vm((2, 2 * c1, ny1 * q), BF16),
            vm((2 * ny1 * c1, 2 * q), BF16),
            vm((8 * c0 * ny, nzi * q), BF16),
            vm((k1m.shape[1], 2 * k1m.shape[0]), F32),
            vm((n_pay, 2 * c2), F32),
        ],
        cost_estimate=pl.CostEstimate(flops=60_000_000, transcendentals=200_000, bytes_accessed=3_000_000),
    )(below, volume, above, k1m, k2m, k2t, cot)

    level_two = lvl.reshape(1, c2, 1, ny2, n2 // ny2)
    grad_one = g1.reshape(2, ny1, c1, 2 * q).transpose(2, 0, 1, 3)[None]

    total = _all_sum(keep, send, ("gz", "sa"))
    samples = volume.shape[0] * lax.axis_size("sa")
    cells_one = samples * (nz // 2) * lax.axis_size("gz") * ny1 * (nx // 2)
    cells_two = samples * cotangent.shape[2] * lax.axis_size("gz") * cotangent.shape[3] * cotangent.shape[4]
    t1 = total[n_s2:n_s2 + n_g1] / math.sqrt(float(cells_one))
    t2 = total[:n_s2] / math.sqrt(float(cells_two))
    grad_kernel_one = t1.reshape(3, 3, 3, c0, c1).transpose(4, 3, 0, 1, 2)
    t2 = t2.reshape(27, c1 // 2, 2, c2).transpose(0, 2, 1, 3).reshape(3, 3, 3, c1, c2)
    grad_kernel_two = t2.transpose(4, 3, 0, 1, 2)
    return (level_two, grad_one, grad_kernel_one, grad_kernel_two)


def solution(mesh):
    placed = (P("sa", None, "gz", None, None), P(), P(), P("sa", None, "gz", None, None))
    return jax.shard_map(
        per_device,
        mesh=mesh,
        in_specs=placed,
        out_specs=(P("sa", None, "gz", None, None), P("sa", None, "gz", None, None), P(), P()),
        check_vma=False,
    )
```

```python
import math

import jax
import jax.numpy as jnp
from jax import lax
from jax.experimental import pallas as pl
from jax.experimental.pallas import tpu as pltpu
from jax.sharding import PartitionSpec as P

F32 = jnp.float32
BF16 = jnp.bfloat16


def shifted(block, axis, distance):
    devices = range(lax.axis_size(axis))
    route = [(i - distance, i) for i in devices if i - distance in devices]
    return lax.ppermute(block, axis, route)


def _all_sum(x, axes, early=()):
    steps = []
    for axis in axes:
        n = lax.axis_size(axis)
        assert n & (n - 1) == 0
        k = 1
        while k < n:
            steps.append((axis, n, k))
            k *= 2
    axis0, n0, k0 = steps[0]
    rows = x.shape[0]
    half = -(-rows // 16) * 8
    x = jnp.pad(x, ((0, 2 * half - rows), (0, 0)))
    low = (lax.axis_index(axis0) & k0) == 0
    lo, hi = x[:half], x[half:]
    pair = [(i, i ^ k0) for i in range(n0)]
    part = jnp.where(low, lo, hi) + lax.ppermute(jnp.where(low, hi, lo), axis0, pair)
    part, early = lax.optimization_barrier((part, early))
    for axis, n, k in steps[1:]:
        part = part + lax.ppermute(part, axis, [(i, i ^ k) for i in range(n)])
    other = lax.ppermute(part, axis0, pair)
    return jnp.where(low, jnp.concatenate([part, other], 0), jnp.concatenate([other, part], 0))[:rows], early


def _sigmoid(v):
    return 1.0 / (1.0 + jnp.exp(-v))


def _shift_right(x):
    lane = lax.broadcasted_iota(jnp.int32, x.shape, x.ndim - 1)
    return jnp.where(lane == 0, 0.0, pltpu.roll(x, 1, x.ndim - 1))


def _shift_left(x):
    n = x.shape[-1]
    lane = lax.broadcasted_iota(jnp.int32, x.shape, x.ndim - 1)
    return jnp.where(lane == n - 1, 0.0, pltpu.roll(x, n - 1, x.ndim - 1))


def _nt(a, b):
    return lax.dot_general(a, b, (((1,), (1,)), ((), ())), preferred_element_type=F32)


def _kernel(vb_ref, vo_ref, va_ref, k1_ref, k2_ref, k2t_ref, cot_ref,
            lvl_ref, g1_ref, s2_ref,
            tp, p1, t2, pre1, p2, bt, gs, gacc, b1, g1s, qs, s1s):
    c0, ny, nx = vo_ref.shape[1], vo_ref.shape[3], vo_ref.shape[4]
    lanes = nx // 4
    nzi = tp.shape[0]
    n_act = p1.shape[1] // (vo_ref.shape[3] // 2 * vo_ref.shape[4] // 4)
    ny1 = ny // 2
    ny2 = ny1 // 2
    c2 = t2.shape[2]
    c1 = c2 // 2
    rows0 = 4 * c0

    xs = lax.broadcasted_iota(jnp.int32, (nx, nx), 0)
    cs = lax.broadcasted_iota(jnp.int32, (nx, nx), 1)
    sel_x = jnp.where(xs == 4 * (cs % lanes) + cs // lanes, 1.0, 0.0).astype(BF16)
    nq = 2 * rows0 * ny
    orow = lax.broadcasted_iota(jnp.int32, (nq, nq), 0)
    icol = lax.broadcasted_iota(jnp.int32, (nq, nq), 1)
    y_, s_ = orow // (2 * rows0), (orow // rows0) % 2
    i_, r_ = (orow // 4) % c0, orow % 4
    perm = jnp.where(icol == ((s_ * 4 + r_) * c0 + i_) * ny + y_, 1.0, 0.0).astype(BF16)

    tp[:, 0] = jnp.zeros((nzi, 2 * rows0, lanes), BF16)
    zi = 0
    nz_own = vo_ref.shape[2]
    for ref, nzp in ((vb_ref, vb_ref.shape[2]), (vo_ref, nz_own), (va_ref, nz_own)):
        if ref is va_ref:
            zmat = ref[0:c0 * nzp * ny]
        else:
            zmat = ref[0].reshape(c0 * nzp * ny, nx)
        whole = jnp.dot(zmat, sel_x, preferred_element_type=F32)
        for z in range(nzp):
            ymat = jnp.concatenate([whole[(i * nzp + z) * ny:(i * nzp + z + 1) * ny] for i in range(c0)], axis=0)
            blocks = [ymat[:, r * lanes:(r + 1) * lanes] for r in range(4)]
            qs[:, zi * lanes:(zi + 1) * lanes] = jnp.concatenate(
                blocks + [_shift_right(b) for b in blocks], axis=0).astype(BF16)
            zi += 1
    tall = jnp.dot(perm, qs[...], preferred_element_type=F32).astype(BF16)
    for zi in range(nzi):
        tp[zi, 1:] = tall[:, zi * lanes:(zi + 1) * lanes].reshape(ny, 2 * rows0, lanes)

    for a in range(n_act):
        for d in range(3):
            for y1 in range(ny1):
                p1[d * 3 * 2 * rows0:(d + 1) * 3 * 2 * rows0, (a * ny1 + y1) * lanes:(a * ny1 + y1 + 1) * lanes] = (
                    tp[2 * a + d, 2 * y1:2 * y1 + 3].reshape(3 * 2 * rows0, lanes))

    k1 = k1_ref[...]
    t2[:, 0] = jnp.zeros((n_act, c2, lanes), BF16)
    pre_all = jnp.dot(k1, p1[...], preferred_element_type=F32)
    for a in range(n_act):
        pre = pre_all[:, a * ny1 * lanes:(a + 1) * ny1 * lanes]
        if a in (1, 2):
            pre1[a - 1] = pre
        act = pre * _sigmoid(pre)
        for y1 in range(ny1):
            blk = act[:, y1 * lanes:(y1 + 1) * lanes]
            t2[a, y1 + 1] = jnp.concatenate([blk, _shift_right(blk)], axis=0).astype(BF16)

    for tt in range(2):
        for d in range(3):
            for y2 in range(ny2):
                p2[d * 3 * c2:(d + 1) * 3 * c2, (tt * ny2 + y2) * lanes:(tt * ny2 + y2 + 1) * lanes] = (
                    t2[2 * tt + d, 2 * y2:2 * y2 + 3].reshape(3 * c2, lanes))

    pre2 = jnp.dot(k2_ref[...], p2[...], preferred_element_type=F32)
    n2 = ny2 * lanes
    for tt in range(2):
        pre = pre2[:, tt * n2:(tt + 1) * n2]
        sig = _sigmoid(pre)
        if tt == 0:
            lvl_ref[...] = (pre * sig).astype(BF16)
        slope = sig * (1.0 + pre * (1.0 - sig))
        cot_t = cot_ref[...] if tt == 0 else va_ref[va_ref.shape[0] - c1:]
        bt[:, tt * n2:(tt + 1) * n2] = (cot_t.astype(F32) * slope).astype(BF16)

    bt0 = bt[:, :n2]
    dup = _nt(p2[:, :n2], jnp.concatenate([bt0, bt0], axis=0))
    c2n = dup.shape[1] // 2
    qi = c1 // 4
    lane2 = lax.broadcasted_iota(jnp.int32, (qi, 2 * c2n), 1)
    n_s2 = 27 * qi
    s2_ref[n_s2:] = jnp.zeros((s2_ref.shape[0] - n_s2, s2_ref.shape[1]), F32)
    for dh in range(9):
        for w, off in enumerate((3 * c1 // 2, 0, c1 // 2)):
            r0 = dh * c2 + off
            s2_ref[(dh * 3 + w) * qi:(dh * 3 + w + 1) * qi] = jnp.where(
                lane2 < c2n, dup[r0:r0 + qi], dup[r0 + qi:r0 + 2 * qi])

    gacc[...] = jnp.zeros(gacc.shape, F32)
    gs[...] = jnp.dot(k2t_ref[...], bt[...], preferred_element_type=F32)
    for tt in range(2):
        taps_d = (1, 2) if tt == 0 else (0,)
        for d in taps_d:
            a = 2 * tt + d
            for h in range(3):
                for y2 in range(ny2):
                    y1 = 2 * y2 + h - 1
                    if y1 < 0:
                        continue
                    r0 = (d * 3 + h) * c2
                    blk = gs[r0:r0 + c2, (tt * ny2 + y2) * lanes:(tt * ny2 + y2 + 1) * lanes]
                    gacc[a - 1, :, y1 * lanes:(y1 + 1) * lanes] += blk[:c1] + _shift_left(blk[c1:])

    half = c1 // 2
    for a_ in range(2):
        g = gacc[a_]
        pre = pre1[a_]
        sig = _sigmoid(pre)
        slope = sig * (1.0 + pre * (1.0 - sig))
        b1[a_] = (g * slope).astype(BF16)
        gb = g.astype(BF16)
        for y1 in range(ny1):
            blk = gb[:, y1 * lanes:(y1 + 1) * lanes]
            r0 = (a_ * ny1 + y1) * half
            g1s[r0:r0 + half] = jnp.concatenate([blk[:half], blk[half:]], axis=1)
    bcat = jnp.concatenate([b1[0], b1[1]], axis=1)
    s1s[...] = _nt(p1[:, ny1 * lanes:3 * ny1 * lanes],
                   jnp.concatenate([bcat, jnp.zeros(bcat.shape, BF16)], axis=0))
    qo = c1 // 2
    lane1 = lax.broadcasted_iota(jnp.int32, (1, 4 * qo), 1)
    taps = (((1, 3), (0, 1)), ((0, 0), (0, 2)), ((0, 1), (0, 3)))
    out_rows = []
    for dh in range(9):
        for (sa, ra), (sb, rb) in taps:
            acc = jnp.zeros((1, 4 * qo), F32)
            for i in range(c0):
                xa = s1s[pl.ds(dh * 2 * rows0 + sa * rows0 + i * 4 + ra, 1), :]
                xb = s1s[pl.ds(dh * 2 * rows0 + sb * rows0 + i * 4 + rb, 1), :]
                if i:
                    xa = pltpu.roll(xa, i * qo, 1)
                xb = pltpu.roll(xb, (i * qo - qo) % (4 * qo), 1)
                m = (lane1 >= i * qo) & (lane1 < (i + 1) * qo)
                acc = acc + jnp.where(m, xa + xb, 0.0)
            out_rows.append(acc)
    n_s2 = 27 * qi
    s2_ref[n_s2:n_s2 + 27] = jnp.concatenate(out_rows, axis=0)

    n2 = 2 * lanes
    row = lax.broadcasted_iota(jnp.int32, (n2, n2), 0)
    col = lax.broadcasted_iota(jnp.int32, (n2, n2), 1)
    inter = jnp.where(col == 2 * (row % lanes) + row // lanes, 1.0, 0.0).astype(BF16)
    g1_ref[...] = jnp.dot(g1s[...], inter, preferred_element_type=F32).astype(BF16)


def _level_one_weights(k1):
    kt = jnp.transpose(k1, (0, 2, 3, 1, 4))
    w0, w1, w2 = kt[..., 0], kt[..., 1], kt[..., 2]
    z = jnp.zeros_like(w0)
    p0 = jnp.stack([jnp.stack([w1, w2, z, z], -1), jnp.stack([z, z, z, w0], -1)], 3)
    p1 = jnp.stack([jnp.stack([z, w0, w1, w2], -1), jnp.stack([z, z, z, z], -1)], 3)
    e = jnp.stack([p0, p1], 0)
    return e.reshape(2 * k1.shape[0], -1)


def _level_two_weights(k2):
    kt = jnp.transpose(k2, (0, 2, 3, 4, 1))
    w0, w1, w2 = kt[:, :, :, 0], kt[:, :, :, 1], kt[:, :, :, 2]
    z = jnp.zeros_like(w0)
    e = jnp.stack([jnp.stack([w1, w2], 3), jnp.stack([z, w0], 3)], 3)
    return e.reshape(k2.shape[0], -1)


def per_device(volume, kernel_one, kernel_two, cotangent):
    _, c0, nz, ny, nx = volume.shape
    c1 = kernel_one.shape[0]
    c2 = kernel_two.shape[0]
    assert nz == 4 and cotangent.shape[2] == 1
    q = nx // 4
    below = shifted(volume[:, :, 1:], "gz", 1)
    cot = cotangent[0, :, 0].reshape(cotangent.shape[1], -1)
    above = shifted(jnp.concatenate([volume[0].reshape(-1, nx), cot], 0), "gz", -1)
    nzi = below.shape[2] + 2 * nz
    n2 = cotangent.shape[3] * cotangent.shape[4]

    k1m = _level_one_weights(kernel_one)
    k2m = _level_two_weights(kernel_two)
    k2t = k2m.T

    ny1, ny2 = ny // 2, ny // 4
    n_act = 5
    n_s2 = 27 * c1 // 2
    n_g1 = 27 * c0 * c1 // (2 * c2)
    n_pay = -(-(n_s2 + n_g1) // 16) * 16
    vm = pltpu.VMEM
    lvl, g1, pay = pl.pallas_call(
        _kernel,
        out_shape=(
            jax.ShapeDtypeStruct((c2, n2), BF16),
            jax.ShapeDtypeStruct((2 * ny1 * c1, 2 * q), BF16),
            jax.ShapeDtypeStruct((n_pay, 2 * c2), F32),
        ),
        scratch_shapes=[
            vm((nzi, ny + 1, 8 * c0, q), BF16),
            vm((k1m.shape[1], n_act * ny1 * q), BF16),
            vm((n_act, ny1 + 1, 4 * c1, q), BF16),
            vm((2, 2 * c1, ny1 * q), F32),
            vm((k2m.shape[1], 2 * n2), BF16),
            vm((c2, 2 * n2), BF16),
            vm((k2m.shape[1], 2 * n2), F32),
            vm((2, 2 * c1, ny1 * q), F32),
            vm((2, 2 * c1, ny1 * q), BF16),
            vm((2 * ny1 * c1, 2 * q), BF16),
            vm((8 * c0 * ny, nzi * q), BF16),
            vm((k1m.shape[1], 2 * k1m.shape[0]), F32),
        ],
        cost_estimate=pl.CostEstimate(flops=60_000_000, transcendentals=200_000, bytes_accessed=3_000_000),
    )(below, volume, above, k1m, k2m, k2t, cot)

    level_two = lvl.reshape(1, c2, 1, ny2, n2 // ny2)
    grad_one = g1.reshape(2, ny1, c1, 2 * q).transpose(2, 0, 1, 3)[None]


    total, (level_two, grad_one) = _all_sum(pay, ("gz", "sa"), (level_two, grad_one))
    samples = volume.shape[0] * lax.axis_size("sa")
    cells_one = samples * (nz // 2) * lax.axis_size("gz") * ny1 * (nx // 2)
    cells_two = samples * cotangent.shape[2] * lax.axis_size("gz") * cotangent.shape[3] * cotangent.shape[4]
    t1 = total[n_s2:n_s2 + n_g1] / math.sqrt(float(cells_one))
    t2 = total[:n_s2] / math.sqrt(float(cells_two))
    grad_kernel_one = t1.reshape(3, 3, 3, c0, c1).transpose(4, 3, 0, 1, 2)
    t2 = t2.reshape(27, c1 // 2, 2, c2).transpose(0, 2, 1, 3).reshape(3, 3, 3, c1, c2)
    grad_kernel_two = t2.transpose(4, 3, 0, 1, 2)
    return (level_two, grad_one, grad_kernel_one, grad_kernel_two)


def solution(mesh):
    placed = (P("sa", None, "gz", None, None), P(), P(), P("sa", None, "gz", None, None))
    return jax.shard_map(
        per_device,
        mesh=mesh,
        in_specs=placed,
        out_specs=(P("sa", None, "gz", None, None), P("sa", None, "gz", None, None), P(), P()),
        check_vma=False,
    )
```

```python
import math

import jax
import jax.numpy as jnp
from jax import lax
from jax.experimental import pallas as pl
from jax.experimental.pallas import tpu as pltpu
from jax.sharding import PartitionSpec as P

F32 = jnp.float32
BF16 = jnp.bfloat16


def shifted(block, axis, distance):
    devices = range(lax.axis_size(axis))
    route = [(i - distance, i) for i in devices if i - distance in devices]
    return lax.ppermute(block, axis, route)


def _all_sum(x, axes):
    steps = []
    for axis in axes:
        n = lax.axis_size(axis)
        assert n & (n - 1) == 0
        k = 1
        while k < n:
            steps.append((axis, n, k))
            k *= 2
    axis0, n0, k0 = steps[0]
    rows = x.shape[0]
    half = -(-rows // 16) * 8
    x = jnp.pad(x, ((0, 2 * half - rows), (0, 0)))
    low = (lax.axis_index(axis0) & k0) == 0
    lo, hi = x[:half], x[half:]
    pair = [(i, i ^ k0) for i in range(n0)]
    part = jnp.where(low, lo, hi) + lax.ppermute(jnp.where(low, hi, lo), axis0, pair)
    for axis, n, k in steps[1:]:
        part = part + lax.ppermute(part, axis, [(i, i ^ k) for i in range(n)])
    other = lax.ppermute(part, axis0, pair)
    return jnp.where(low, jnp.concatenate([part, other], 0), jnp.concatenate([other, part], 0))[:rows]


def _sigmoid(v):
    return 0.5 * (jnp.tanh(0.5 * v) + 1.0)


def _shift_right(x):
    lane = lax.broadcasted_iota(jnp.int32, x.shape, x.ndim - 1)
    return jnp.where(lane == 0, 0.0, pltpu.roll(x, 1, x.ndim - 1))


def _shift_left(x):
    n = x.shape[-1]
    lane = lax.broadcasted_iota(jnp.int32, x.shape, x.ndim - 1)
    return jnp.where(lane == n - 1, 0.0, pltpu.roll(x, n - 1, x.ndim - 1))


def _nt(a, b):
    return lax.dot_general(a, b, (((1,), (1,)), ((), ())), preferred_element_type=F32)


def _kernel(vb_ref, vo_ref, va_ref, k1_ref, k2_ref, k2t_ref, cot_ref,
            lvl_ref, g1_ref, s2_ref,
            tp, p1, t2, pre1, p2, bt, gs, gacc, b1, g1s, qs, s1s):
    c0, ny, nx = vo_ref.shape[1], vo_ref.shape[3], vo_ref.shape[4]
    lanes = nx // 4
    nzi = tp.shape[0]
    n_act = p1.shape[1] // (vo_ref.shape[3] // 2 * vo_ref.shape[4] // 4)
    ny1 = ny // 2
    ny2 = ny1 // 2
    c2 = t2.shape[2]
    c1 = c2 // 2
    rows0 = 4 * c0

    xs = lax.broadcasted_iota(jnp.int32, (nx, nx), 0)
    cs = lax.broadcasted_iota(jnp.int32, (nx, nx), 1)
    sel_x = jnp.where(xs == 4 * (cs % lanes) + cs // lanes, 1.0, 0.0).astype(BF16)
    nq = 2 * rows0 * ny
    orow = lax.broadcasted_iota(jnp.int32, (nq, nq), 0)
    icol = lax.broadcasted_iota(jnp.int32, (nq, nq), 1)
    y_, s_ = orow // (2 * rows0), (orow // rows0) % 2
    i_, r_ = (orow // 4) % c0, orow % 4
    perm = jnp.where(icol == ((s_ * 4 + r_) * c0 + i_) * ny + y_, 1.0, 0.0).astype(BF16)

    tp[:, 0] = jnp.zeros((nzi, 2 * rows0, lanes), BF16)
    zi = 0
    nz_own = vo_ref.shape[2]
    for ref, nzp in ((vb_ref, vb_ref.shape[2]), (vo_ref, nz_own), (va_ref, nz_own)):
        if ref is va_ref:
            zmat = ref[0:c0 * nzp * ny]
        else:
            zmat = ref[0].reshape(c0 * nzp * ny, nx)
        whole = jnp.dot(zmat, sel_x, preferred_element_type=F32)
        for z in range(nzp):
            ymat = jnp.concatenate([whole[(i * nzp + z) * ny:(i * nzp + z + 1) * ny] for i in range(c0)], axis=0)
            blocks = [ymat[:, r * lanes:(r + 1) * lanes] for r in range(4)]
            qs[:, zi * lanes:(zi + 1) * lanes] = jnp.concatenate(
                blocks + [_shift_right(b) for b in blocks], axis=0).astype(BF16)
            zi += 1
    tall = jnp.dot(perm, qs[...], preferred_element_type=F32).astype(BF16)
    for zi in range(nzi):
        tp[zi, 1:] = tall[:, zi * lanes:(zi + 1) * lanes].reshape(ny, 2 * rows0, lanes)

    for a in range(n_act):
        for d in range(3):
            for y1 in range(ny1):
                p1[d * 3 * 2 * rows0:(d + 1) * 3 * 2 * rows0, (a * ny1 + y1) * lanes:(a * ny1 + y1 + 1) * lanes] = (
                    tp[2 * a + d, 2 * y1:2 * y1 + 3].reshape(3 * 2 * rows0, lanes))

    k1 = k1_ref[...]
    t2[:, 0] = jnp.zeros((n_act, c2, lanes), BF16)
    pre_all = jnp.dot(k1, p1[...], preferred_element_type=F32)
    for a in range(n_act):
        pre = pre_all[:, a * ny1 * lanes:(a + 1) * ny1 * lanes]
        if a in (1, 2):
            pre1[a - 1] = pre
        act = pre * _sigmoid(pre)
        for y1 in range(ny1):
            blk = act[:, y1 * lanes:(y1 + 1) * lanes]
            t2[a, y1 + 1] = jnp.concatenate([blk, _shift_right(blk)], axis=0).astype(BF16)

    for tt in range(2):
        for d in range(3):
            for y2 in range(ny2):
                p2[d * 3 * c2:(d + 1) * 3 * c2, (tt * ny2 + y2) * lanes:(tt * ny2 + y2 + 1) * lanes] = (
                    t2[2 * tt + d, 2 * y2:2 * y2 + 3].reshape(3 * c2, lanes))

    pre2 = jnp.dot(k2_ref[...], p2[...], preferred_element_type=F32)
    n2 = ny2 * lanes
    for tt in range(2):
        pre = pre2[:, tt * n2:(tt + 1) * n2]
        sig = _sigmoid(pre)
        if tt == 0:
            lvl_ref[...] = (pre * sig).astype(BF16)
        slope = sig * (1.0 + pre * (1.0 - sig))
        cot_t = cot_ref[...] if tt == 0 else va_ref[va_ref.shape[0] - c1:]
        bt[:, tt * n2:(tt + 1) * n2] = (cot_t.astype(F32) * slope).astype(BF16)

    bt0 = bt[:, :n2]
    dup = _nt(p2[:, :n2], jnp.concatenate([bt0, bt0], axis=0))
    c2n = dup.shape[1] // 2
    qi = c1 // 4
    lane2 = lax.broadcasted_iota(jnp.int32, (qi, 2 * c2n), 1)
    n_s2 = 27 * qi
    s2_ref[n_s2:] = jnp.zeros((s2_ref.shape[0] - n_s2, s2_ref.shape[1]), F32)
    for dh in range(9):
        for w, off in enumerate((3 * c1 // 2, 0, c1 // 2)):
            r0 = dh * c2 + off
            s2_ref[(dh * 3 + w) * qi:(dh * 3 + w + 1) * qi] = jnp.where(
                lane2 < c2n, dup[r0:r0 + qi], dup[r0 + qi:r0 + 2 * qi])

    gacc[...] = jnp.zeros(gacc.shape, F32)
    gs[...] = jnp.dot(k2t_ref[...], bt[...], preferred_element_type=F32)
    for tt in range(2):
        taps_d = (1, 2) if tt == 0 else (0,)
        for d in taps_d:
            a = 2 * tt + d
            for h in range(3):
                for y2 in range(ny2):
                    y1 = 2 * y2 + h - 1
                    if y1 < 0:
                        continue
                    r0 = (d * 3 + h) * c2
                    blk = gs[r0:r0 + c2, (tt * ny2 + y2) * lanes:(tt * ny2 + y2 + 1) * lanes]
                    gacc[a - 1, :, y1 * lanes:(y1 + 1) * lanes] += blk[:c1] + _shift_left(blk[c1:])

    half = c1 // 2
    for a_ in range(2):
        g = gacc[a_]
        pre = pre1[a_]
        sig = _sigmoid(pre)
        slope = sig * (1.0 + pre * (1.0 - sig))
        b1[a_] = (g * slope).astype(BF16)
        gb = g.astype(BF16)
        for y1 in range(ny1):
            blk = gb[:, y1 * lanes:(y1 + 1) * lanes]
            r0 = (a_ * ny1 + y1) * half
            g1s[r0:r0 + half] = jnp.concatenate([blk[:half], blk[half:]], axis=1)
    bcat = jnp.concatenate([b1[0], b1[1]], axis=1)
    s1s[...] = _nt(p1[:, ny1 * lanes:3 * ny1 * lanes],
                   jnp.concatenate([bcat, jnp.zeros(bcat.shape, BF16)], axis=0))
    qo = c1 // 2
    lane1 = lax.broadcasted_iota(jnp.int32, (1, 4 * qo), 1)
    taps = (((1, 3), (0, 1)), ((0, 0), (0, 2)), ((0, 1), (0, 3)))
    out_rows = []
    for dh in range(9):
        for (sa, ra), (sb, rb) in taps:
            acc = jnp.zeros((1, 4 * qo), F32)
            for i in range(c0):
                xa = s1s[pl.ds(dh * 2 * rows0 + sa * rows0 + i * 4 + ra, 1), :]
                xb = s1s[pl.ds(dh * 2 * rows0 + sb * rows0 + i * 4 + rb, 1), :]
                if i:
                    xa = pltpu.roll(xa, i * qo, 1)
                xb = pltpu.roll(xb, (i * qo - qo) % (4 * qo), 1)
                m = (lane1 >= i * qo) & (lane1 < (i + 1) * qo)
                acc = acc + jnp.where(m, xa + xb, 0.0)
            out_rows.append(acc)
    n_s2 = 27 * qi
    s2_ref[n_s2:n_s2 + 27] = jnp.concatenate(out_rows, axis=0)

    n2 = 2 * lanes
    row = lax.broadcasted_iota(jnp.int32, (n2, n2), 0)
    col = lax.broadcasted_iota(jnp.int32, (n2, n2), 1)
    inter = jnp.where(col == 2 * (row % lanes) + row // lanes, 1.0, 0.0).astype(BF16)
    g1_ref[...] = jnp.dot(g1s[...], inter, preferred_element_type=F32).astype(BF16)


def _level_one_weights(k1):
    kt = jnp.transpose(k1, (0, 2, 3, 1, 4))
    w0, w1, w2 = kt[..., 0], kt[..., 1], kt[..., 2]
    z = jnp.zeros_like(w0)
    p0 = jnp.stack([jnp.stack([w1, w2, z, z], -1), jnp.stack([z, z, z, w0], -1)], 3)
    p1 = jnp.stack([jnp.stack([z, w0, w1, w2], -1), jnp.stack([z, z, z, z], -1)], 3)
    e = jnp.stack([p0, p1], 0)
    return e.reshape(2 * k1.shape[0], -1)


def _level_two_weights(k2):
    kt = jnp.transpose(k2, (0, 2, 3, 4, 1))
    w0, w1, w2 = kt[:, :, :, 0], kt[:, :, :, 1], kt[:, :, :, 2]
    z = jnp.zeros_like(w0)
    e = jnp.stack([jnp.stack([w1, w2], 3), jnp.stack([z, w0], 3)], 3)
    return e.reshape(k2.shape[0], -1)


def per_device(volume, kernel_one, kernel_two, cotangent):
    _, c0, nz, ny, nx = volume.shape
    c1 = kernel_one.shape[0]
    c2 = kernel_two.shape[0]
    assert nz == 4 and cotangent.shape[2] == 1
    q = nx // 4
    below = shifted(volume[:, :, 1:], "gz", 1)
    cot = cotangent[0, :, 0].reshape(cotangent.shape[1], -1)
    above = shifted(jnp.concatenate([volume[0].reshape(-1, nx), cot], 0), "gz", -1)
    nzi = below.shape[2] + 2 * nz
    n2 = cotangent.shape[3] * cotangent.shape[4]

    k1m = _level_one_weights(kernel_one)
    k2m = _level_two_weights(kernel_two)
    k2t = k2m.T

    ny1, ny2 = ny // 2, ny // 4
    n_act = 5
    n_s2 = 27 * c1 // 2
    n_g1 = 27 * c0 * c1 // (2 * c2)
    n_pay = -(-(n_s2 + n_g1) // 16) * 16
    vm = pltpu.VMEM
    lvl, g1, pay = pl.pallas_call(
        _kernel,
        out_shape=(
            jax.ShapeDtypeStruct((c2, n2), BF16),
            jax.ShapeDtypeStruct((2 * ny1 * c1, 2 * q), BF16),
            jax.ShapeDtypeStruct((n_pay, 2 * c2), F32),
        ),
        scratch_shapes=[
            vm((nzi, ny + 1, 8 * c0, q), BF16),
            vm((k1m.shape[1], n_act * ny1 * q), BF16),
            vm((n_act, ny1 + 1, 4 * c1, q), BF16),
            vm((2, 2 * c1, ny1 * q), F32),
            vm((k2m.shape[1], 2 * n2), BF16),
            vm((c2, 2 * n2), BF16),
            vm((k2m.shape[1], 2 * n2), F32),
            vm((2, 2 * c1, ny1 * q), F32),
            vm((2, 2 * c1, ny1 * q), BF16),
            vm((2 * ny1 * c1, 2 * q), BF16),
            vm((8 * c0 * ny, nzi * q), BF16),
            vm((k1m.shape[1], 2 * k1m.shape[0]), F32),
        ],
        cost_estimate=pl.CostEstimate(flops=60_000_000, transcendentals=200_000, bytes_accessed=3_000_000),
    )(below, volume, above, k1m, k2m, k2t, cot)

    level_two = lvl.reshape(1, c2, 1, ny2, n2 // ny2)
    grad_one = g1.reshape(2, ny1, c1, 2 * q).transpose(2, 0, 1, 3)[None]

    total = _all_sum(pay, ("gz", "sa"))
    samples = volume.shape[0] * lax.axis_size("sa")
    cells_one = samples * (nz // 2) * lax.axis_size("gz") * ny1 * (nx // 2)
    cells_two = samples * cotangent.shape[2] * lax.axis_size("gz") * cotangent.shape[3] * cotangent.shape[4]
    t1 = total[n_s2:n_s2 + n_g1] / math.sqrt(float(cells_one))
    t2 = total[:n_s2] / math.sqrt(float(cells_two))
    grad_kernel_one = t1.reshape(3, 3, 3, c0, c1).transpose(4, 3, 0, 1, 2)
    t2 = t2.reshape(27, c1 // 2, 2, c2).transpose(0, 2, 1, 3).reshape(3, 3, 3, c1, c2)
    grad_kernel_two = t2.transpose(4, 3, 0, 1, 2)
    return (level_two, grad_one, grad_kernel_one, grad_kernel_two)


def solution(mesh):
    placed = (P("sa", None, "gz", None, None), P(), P(), P("sa", None, "gz", None, None))
    return jax.shard_map(
        per_device,
        mesh=mesh,
        in_specs=placed,
        out_specs=(P("sa", None, "gz", None, None), P("sa", None, "gz", None, None), P(), P()),
        check_vma=False,
    )
```

```python
import math

import jax
import jax.numpy as jnp
from jax import lax
from jax.experimental import pallas as pl
from jax.experimental.pallas import tpu as pltpu
from jax.sharding import PartitionSpec as P

F32 = jnp.float32
BF16 = jnp.bfloat16


def shifted(block, axis, distance):
    devices = range(lax.axis_size(axis))
    route = [(i - distance, i) for i in devices if i - distance in devices]
    return lax.ppermute(block, axis, route)


def _all_sum(x, axes):
    steps = []
    for axis in axes:
        n = lax.axis_size(axis)
        assert n & (n - 1) == 0
        k = 1
        while k < n:
            steps.append((axis, n, k))
            k *= 2
    axis0, n0, k0 = steps[0]
    steps = steps[:1] + [st for st in steps[1:] if st[0] != axis0] + [st for st in steps[1:] if st[0] == axis0]
    rows = x.shape[0]
    half = -(-rows // 16) * 8
    x = jnp.pad(x, ((0, 2 * half - rows), (0, 0)))
    low = (lax.axis_index(axis0) & k0) == 0
    lo, hi = x[:half], x[half:]
    pair = [(i, i ^ k0) for i in range(n0)]
    part = jnp.where(low, lo, hi) + lax.ppermute(jnp.where(low, hi, lo), axis0, pair)
    for axis, n, k in steps[1:]:
        part = part + lax.ppermute(part, axis, [(i, i ^ k) for i in range(n)])
    other = lax.ppermute(part, axis0, pair)
    return jnp.where(low, jnp.concatenate([part, other], 0), jnp.concatenate([other, part], 0))[:rows]


def _sigmoid(v):
    return 1.0 / (1.0 + jnp.exp(-v))


def _shift_right(x):
    lane = lax.broadcasted_iota(jnp.int32, x.shape, x.ndim - 1)
    return jnp.where(lane == 0, 0.0, pltpu.roll(x, 1, x.ndim - 1))


def _shift_left(x):
    n = x.shape[-1]
    lane = lax.broadcasted_iota(jnp.int32, x.shape, x.ndim - 1)
    return jnp.where(lane == n - 1, 0.0, pltpu.roll(x, n - 1, x.ndim - 1))


def _nt(a, b):
    return lax.dot_general(a, b, (((1,), (1,)), ((), ())), preferred_element_type=F32)


def _kernel(vb_ref, vo_ref, va_ref, k1_ref, k2_ref, k2t_ref, cot_ref,
            lvl_ref, g1_ref, s2_ref,
            tp, p1, t2, pre1, p2, bt, gs, gacc, b1, g1s, qs, s1s):
    c0, ny, nx = vo_ref.shape[1], vo_ref.shape[3], vo_ref.shape[4]
    lanes = nx // 4
    nzi = tp.shape[0]
    n_act = p1.shape[1] // (vo_ref.shape[3] // 2 * vo_ref.shape[4] // 4)
    ny1 = ny // 2
    ny2 = ny1 // 2
    c2 = t2.shape[2]
    c1 = c2 // 2
    rows0 = 4 * c0

    xs = lax.broadcasted_iota(jnp.int32, (nx, nx), 0)
    cs = lax.broadcasted_iota(jnp.int32, (nx, nx), 1)
    sel_x = jnp.where(xs == 4 * (cs % lanes) + cs // lanes, 1.0, 0.0).astype(BF16)
    nq = 2 * rows0 * ny
    orow = lax.broadcasted_iota(jnp.int32, (nq, nq), 0)
    icol = lax.broadcasted_iota(jnp.int32, (nq, nq), 1)
    y_, s_ = orow // (2 * rows0), (orow // rows0) % 2
    i_, r_ = (orow // 4) % c0, orow % 4
    perm = jnp.where(icol == ((s_ * 4 + r_) * c0 + i_) * ny + y_, 1.0, 0.0).astype(BF16)

    tp[:, 0] = jnp.zeros((nzi, 2 * rows0, lanes), BF16)
    zi = 0
    nz_own = vo_ref.shape[2]
    for ref, nzp in ((vb_ref, vb_ref.shape[2]), (vo_ref, nz_own), (va_ref, nz_own)):
        if ref is va_ref:
            zmat = ref[0:c0 * nzp * ny]
        else:
            zmat = ref[0].reshape(c0 * nzp * ny, nx)
        whole = jnp.dot(zmat, sel_x, preferred_element_type=F32)
        for z in range(nzp):
            ymat = jnp.concatenate([whole[(i * nzp + z) * ny:(i * nzp + z + 1) * ny] for i in range(c0)], axis=0)
            blocks = [ymat[:, r * lanes:(r + 1) * lanes] for r in range(4)]
            qs[:, zi * lanes:(zi + 1) * lanes] = jnp.concatenate(
                blocks + [_shift_right(b) for b in blocks], axis=0).astype(BF16)
            zi += 1
    tall = jnp.dot(perm, qs[...], preferred_element_type=F32).astype(BF16)
    for zi in range(nzi):
        tp[zi, 1:] = tall[:, zi * lanes:(zi + 1) * lanes].reshape(ny, 2 * rows0, lanes)

    for a in range(n_act):
        for d in range(3):
            for y1 in range(ny1):
                p1[d * 3 * 2 * rows0:(d + 1) * 3 * 2 * rows0, (a * ny1 + y1) * lanes:(a * ny1 + y1 + 1) * lanes] = (
                    tp[2 * a + d, 2 * y1:2 * y1 + 3].reshape(3 * 2 * rows0, lanes))

    k1 = k1_ref[...]
    t2[:, 0] = jnp.zeros((n_act, c2, lanes), BF16)
    pre_all = jnp.dot(k1, p1[...], preferred_element_type=F32)
    for a in range(n_act):
        pre = pre_all[:, a * ny1 * lanes:(a + 1) * ny1 * lanes]
        if a in (1, 2):
            pre1[a - 1] = pre
        act = pre * _sigmoid(pre)
        for y1 in range(ny1):
            blk = act[:, y1 * lanes:(y1 + 1) * lanes]
            t2[a, y1 + 1] = jnp.concatenate([blk, _shift_right(blk)], axis=0).astype(BF16)

    for tt in range(2):
        for d in range(3):
            for y2 in range(ny2):
                p2[d * 3 * c2:(d + 1) * 3 * c2, (tt * ny2 + y2) * lanes:(tt * ny2 + y2 + 1) * lanes] = (
                    t2[2 * tt + d, 2 * y2:2 * y2 + 3].reshape(3 * c2, lanes))

    pre2 = jnp.dot(k2_ref[...], p2[...], preferred_element_type=F32)
    n2 = ny2 * lanes
    for tt in range(2):
        pre = pre2[:, tt * n2:(tt + 1) * n2]
        sig = _sigmoid(pre)
        if tt == 0:
            lvl_ref[...] = (pre * sig).astype(BF16)
        slope = sig * (1.0 + pre * (1.0 - sig))
        cot_t = cot_ref[...] if tt == 0 else va_ref[va_ref.shape[0] - c1:]
        bt[:, tt * n2:(tt + 1) * n2] = (cot_t.astype(F32) * slope).astype(BF16)

    bt0 = bt[:, :n2]
    dup = _nt(p2[:, :n2], jnp.concatenate([bt0, bt0], axis=0))
    c2n = dup.shape[1] // 2
    qi = c1 // 4
    lane2 = lax.broadcasted_iota(jnp.int32, (qi, 2 * c2n), 1)
    n_s2 = 27 * qi
    s2_ref[n_s2:] = jnp.zeros((s2_ref.shape[0] - n_s2, s2_ref.shape[1]), F32)
    for dh in range(9):
        for w, off in enumerate((3 * c1 // 2, 0, c1 // 2)):
            r0 = dh * c2 + off
            s2_ref[(dh * 3 + w) * qi:(dh * 3 + w + 1) * qi] = jnp.where(
                lane2 < c2n, dup[r0:r0 + qi], dup[r0 + qi:r0 + 2 * qi])

    gacc[...] = jnp.zeros(gacc.shape, F32)
    gs[...] = jnp.dot(k2t_ref[...], bt[...], preferred_element_type=F32)
    for tt in range(2):
        taps_d = (1, 2) if tt == 0 else (0,)
        for d in taps_d:
            a = 2 * tt + d
            for h in range(3):
                for y2 in range(ny2):
                    y1 = 2 * y2 + h - 1
                    if y1 < 0:
                        continue
                    r0 = (d * 3 + h) * c2
                    blk = gs[r0:r0 + c2, (tt * ny2 + y2) * lanes:(tt * ny2 + y2 + 1) * lanes]
                    gacc[a - 1, :, y1 * lanes:(y1 + 1) * lanes] += blk[:c1] + _shift_left(blk[c1:])

    half = c1 // 2
    for a_ in range(2):
        g = gacc[a_]
        pre = pre1[a_]
        sig = _sigmoid(pre)
        slope = sig * (1.0 + pre * (1.0 - sig))
        b1[a_] = (g * slope).astype(BF16)
        gb = g.astype(BF16)
        for y1 in range(ny1):
            blk = gb[:, y1 * lanes:(y1 + 1) * lanes]
            r0 = (a_ * ny1 + y1) * half
            g1s[r0:r0 + half] = jnp.concatenate([blk[:half], blk[half:]], axis=1)
    bcat = jnp.concatenate([b1[0], b1[1]], axis=1)
    s1s[...] = _nt(p1[:, ny1 * lanes:3 * ny1 * lanes],
                   jnp.concatenate([bcat, jnp.zeros(bcat.shape, BF16)], axis=0))
    qo = c1 // 2
    lane1 = lax.broadcasted_iota(jnp.int32, (1, 4 * qo), 1)
    taps = (((1, 3), (0, 1)), ((0, 0), (0, 2)), ((0, 1), (0, 3)))
    out_rows = []
    for dh in range(9):
        for (sa, ra), (sb, rb) in taps:
            acc = jnp.zeros((1, 4 * qo), F32)
            for i in range(c0):
                xa = s1s[pl.ds(dh * 2 * rows0 + sa * rows0 + i * 4 + ra, 1), :]
                xb = s1s[pl.ds(dh * 2 * rows0 + sb * rows0 + i * 4 + rb, 1), :]
                if i:
                    xa = pltpu.roll(xa, i * qo, 1)
                xb = pltpu.roll(xb, (i * qo - qo) % (4 * qo), 1)
                m = (lane1 >= i * qo) & (lane1 < (i + 1) * qo)
                acc = acc + jnp.where(m, xa + xb, 0.0)
            out_rows.append(acc)
    n_s2 = 27 * qi
    s2_ref[n_s2:n_s2 + 27] = jnp.concatenate(out_rows, axis=0)

    n2 = 2 * lanes
    row = lax.broadcasted_iota(jnp.int32, (n2, n2), 0)
    col = lax.broadcasted_iota(jnp.int32, (n2, n2), 1)
    inter = jnp.where(col == 2 * (row % lanes) + row // lanes, 1.0, 0.0).astype(BF16)
    g1_ref[...] = jnp.dot(g1s[...], inter, preferred_element_type=F32).astype(BF16)


def _level_one_weights(k1):
    kt = jnp.transpose(k1, (0, 2, 3, 1, 4))
    w0, w1, w2 = kt[..., 0], kt[..., 1], kt[..., 2]
    z = jnp.zeros_like(w0)
    p0 = jnp.stack([jnp.stack([w1, w2, z, z], -1), jnp.stack([z, z, z, w0], -1)], 3)
    p1 = jnp.stack([jnp.stack([z, w0, w1, w2], -1), jnp.stack([z, z, z, z], -1)], 3)
    e = jnp.stack([p0, p1], 0)
    return e.reshape(2 * k1.shape[0], -1)


def _level_two_weights(k2):
    kt = jnp.transpose(k2, (0, 2, 3, 4, 1))
    w0, w1, w2 = kt[:, :, :, 0], kt[:, :, :, 1], kt[:, :, :, 2]
    z = jnp.zeros_like(w0)
    e = jnp.stack([jnp.stack([w1, w2], 3), jnp.stack([z, w0], 3)], 3)
    return e.reshape(k2.shape[0], -1)


def per_device(volume, kernel_one, kernel_two, cotangent):
    _, c0, nz, ny, nx = volume.shape
    c1 = kernel_one.shape[0]
    c2 = kernel_two.shape[0]
    assert nz == 4 and cotangent.shape[2] == 1
    q = nx // 4
    below = shifted(volume[:, :, 1:], "gz", 1)
    cot = cotangent[0, :, 0].reshape(cotangent.shape[1], -1)
    above = shifted(jnp.concatenate([volume[0].reshape(-1, nx), cot], 0), "gz", -1)
    nzi = below.shape[2] + 2 * nz
    n2 = cotangent.shape[3] * cotangent.shape[4]

    k1m = _level_one_weights(kernel_one)
    k2m = _level_two_weights(kernel_two)
    k2t = k2m.T

    ny1, ny2 = ny // 2, ny // 4
    n_act = 5
    n_s2 = 27 * c1 // 2
    n_g1 = 27 * c0 * c1 // (2 * c2)
    n_pay = -(-(n_s2 + n_g1) // 16) * 16
    vm = pltpu.VMEM
    lvl, g1, pay = pl.pallas_call(
        _kernel,
        out_shape=(
            jax.ShapeDtypeStruct((c2, n2), BF16),
            jax.ShapeDtypeStruct((2 * ny1 * c1, 2 * q), BF16),
            jax.ShapeDtypeStruct((n_pay, 2 * c2), F32),
        ),
        scratch_shapes=[
            vm((nzi, ny + 1, 8 * c0, q), BF16),
            vm((k1m.shape[1], n_act * ny1 * q), BF16),
            vm((n_act, ny1 + 1, 4 * c1, q), BF16),
            vm((2, 2 * c1, ny1 * q), F32),
            vm((k2m.shape[1], 2 * n2), BF16),
            vm((c2, 2 * n2), BF16),
            vm((k2m.shape[1], 2 * n2), F32),
            vm((2, 2 * c1, ny1 * q), F32),
            vm((2, 2 * c1, ny1 * q), BF16),
            vm((2 * ny1 * c1, 2 * q), BF16),
            vm((8 * c0 * ny, nzi * q), BF16),
            vm((k1m.shape[1], 2 * k1m.shape[0]), F32),
        ],
        cost_estimate=pl.CostEstimate(flops=60_000_000, transcendentals=200_000, bytes_accessed=3_000_000),
    )(below, volume, above, k1m, k2m, k2t, cot)

    level_two = lvl.reshape(1, c2, 1, ny2, n2 // ny2)
    grad_one = g1.reshape(2, ny1, c1, 2 * q).transpose(2, 0, 1, 3)[None]

    total = _all_sum(pay, ("gz", "sa"))
    samples = volume.shape[0] * lax.axis_size("sa")
    cells_one = samples * (nz // 2) * lax.axis_size("gz") * ny1 * (nx // 2)
    cells_two = samples * cotangent.shape[2] * lax.axis_size("gz") * cotangent.shape[3] * cotangent.shape[4]
    t1 = total[n_s2:n_s2 + n_g1] / math.sqrt(float(cells_one))
    t2 = total[:n_s2] / math.sqrt(float(cells_two))
    grad_kernel_one = t1.reshape(3, 3, 3, c0, c1).transpose(4, 3, 0, 1, 2)
    t2 = t2.reshape(27, c1 // 2, 2, c2).transpose(0, 2, 1, 3).reshape(3, 3, 3, c1, c2)
    grad_kernel_two = t2.transpose(4, 3, 0, 1, 2)
    return (level_two, grad_one, grad_kernel_one, grad_kernel_two)


def solution(mesh):
    placed = (P("sa", None, "gz", None, None), P(), P(), P("sa", None, "gz", None, None))
    return jax.shard_map(
        per_device,
        mesh=mesh,
        in_specs=placed,
        out_specs=(P("sa", None, "gz", None, None), P("sa", None, "gz", None, None), P(), P()),
        check_vma=False,
    )
```
